128 devices in a mesh: seq: 16 (over x, y), tensor: 8 (over z, core).
Axes of the slice: x: 4, y: 4, z: 4, core: 2. Of those that a mesh axis runs over, the one named last changes fastest.
Arguments:
- tokens: bfloat16 [12288, 2048], P('seq'), may hold values from -6 to 6
- norm_gain: float32 [2048], replicated, may hold values from 0.1 to 1.9
- query_weight: bfloat16 [2048, 2048], P(None, 'tensor'), may hold values from -0.125 to 0.125
- key_value_matrix: bfloat16 [2048, 4, 128], replicated, may hold values from -0.125 to 0.125
- out_weight: bfloat16 [2048, 2048], replicated, may hold values from -0.125 to 0.125
- cache_pages: bfloat16 [1024, 4, 128, 128], P('seq'), may hold values from -180 to 180, as said below
- page_table: int32 [16, 64], replicated, may hold values from 0 to 1023, as said below
- request_lengths: int32 [80], replicated, may hold values from 1 to 764, as said below
- request_groups: int32 [80], replicated, may hold values from 0 to 15
Outputs:
- projected: bfloat16 [12288, 2048], P('seq', 'tensor')
The draws below stay inside these ranges and needn't reach their ends.
Inputs may be any that keep to these rules, and one draw needn't show every extreme that they name: `page_table`: every page id appears once. Of the last 16 entries of each row, exactly 1 lie in each block of 64 consecutive ids, the pages held by one seq device. `request_lengths`: the lengths of the 5 requests of one seq device sum to at most 768, and to exactly 768 on at least one device. `cache_pages`: keys in the first 64 entries of the last dimension, values in the rest.
All inputs are finite; a program needn't handle non-finite values.
Results may differ from the reference program's by a relative error of at most 0.012.
The reference program's roundings to bfloat16 on the way count: a program that leaves them out, or rounds other values in their place, can miss the bound.
Values may be sent and summed in bfloat16 or wider, within the bound.
No kernel may reach another device: no remote copies, remote signals or barrier semaphores. Data moves between devices by JAX's collectives and lax.ppermute only.
A program may use at most 128 MiB of HBM per device.

```python
import math
import jax
import jax.numpy as jnp
import numpy as np
from jax import lax

MODEL_WIDTH = 2048
QUERY_HEADS = 32
KEY_VALUE_HEADS = 4
HEAD_SIZE = 64
WINDOW_LENGTH = 2048
PAGE_LENGTH = 128
TOKEN_CAPACITY = 768
DEVICE_REQUESTS = 5
PPG = 64
WP = 16
GROUPS = 16
PAGES_DEV = 64
PAGE_TOTAL = 1024
TPO = 1
REQS = 80
ROWS = 12288
N_SEQ = 16


def draw_cache_pages(key, part):
    base_key = jax.random.fold_in(key, 101)
    page_dimensions = (PAGE_TOTAL, KEY_VALUE_HEADS, PAGE_LENGTH, 2 * HEAD_SIZE)
    entries = jnp.clip(jax.random.normal(base_key, page_dimensions, jnp.float32), -5.0, 5.0)
    return entries.astype(jnp.bfloat16)


def draw_page_table(key, part):
    owner_key = jax.random.fold_in(key, 201)
    slot_key = jax.random.fold_in(key, 202)
    tail_scores = jax.random.randint(owner_key, (GROUPS, WP), 0, 1 << 20, dtype=jnp.int32) * WP + lax.broadcasted_iota(jnp.int32, (GROUPS, WP), 1)
    tail_order = jnp.argsort(tail_scores, axis=1).astype(jnp.int32)
    slot_scores = jax.random.randint(slot_key, (N_SEQ, PAGES_DEV), 0, 1 << 20, dtype=jnp.int32) * PAGES_DEV + lax.broadcasted_iota(jnp.int32, (N_SEQ, PAGES_DEV), 1)
    slot_order = jnp.argsort(slot_scores, axis=1).astype(jnp.int32)
    group_ids = lax.broadcasted_iota(jnp.int32, (GROUPS, WP), 0)
    tail_owner = tail_order // TPO
    tail_slot = group_ids * TPO + tail_order % TPO
    tail_ids = tail_owner * PAGES_DEV + slot_order[tail_owner, tail_slot]
    rest_count = PPG - WP
    spare_slots = PAGES_DEV - WP
    flat_index = lax.broadcasted_iota(jnp.int32, (GROUPS, rest_count), 0) * rest_count + lax.broadcasted_iota(jnp.int32, (GROUPS, rest_count), 1)
    rest_owner = flat_index // spare_slots
    rest_slot = WP + flat_index % spare_slots
    rest_ids = rest_owner * PAGES_DEV + slot_order[rest_owner, rest_slot]
    return jnp.concatenate([rest_ids, tail_ids], axis=1).astype(jnp.int32)


def draw_request_lengths(key, part):
    full_key = jax.random.fold_in(key, 301)
    load_key = jax.random.fold_in(key, 302)
    share_key = jax.random.fold_in(key, 303)
    full_device = jax.random.randint(full_key, (), 0, N_SEQ, dtype=jnp.int32)
    device_loads = jax.random.randint(load_key, (N_SEQ,), 2 * TOKEN_CAPACITY // 5, TOKEN_CAPACITY + 1, dtype=jnp.int32)
    device_loads = jnp.where(lax.iota(jnp.int32, N_SEQ) == full_device, TOKEN_CAPACITY, device_loads)
    shares = jax.random.randint(share_key, (N_SEQ, DEVICE_REQUESTS), 1, 17, dtype=jnp.int32)
    share_total = jnp.sum(shares, axis=1, keepdims=True).astype(jnp.int32)
    spare_rows = (device_loads - DEVICE_REQUESTS)[:, None]
    lengths = 1 + spare_rows * shares // share_total
    leftover = device_loads - jnp.sum(lengths, axis=1).astype(jnp.int32)
    last_slot = lax.broadcasted_iota(jnp.int32, (N_SEQ, DEVICE_REQUESTS), 1) == DEVICE_REQUESTS - 1
    lengths = jnp.where(last_slot, lengths + leftover[:, None], lengths)
    full_row = lax.broadcasted_iota(jnp.int32, (N_SEQ, DEVICE_REQUESTS), 0) == full_device
    single = jnp.where(last_slot, TOKEN_CAPACITY - DEVICE_REQUESTS + 1, 1).astype(jnp.int32)
    lengths = jnp.where(full_row, single, lengths)
    return lengths.reshape(N_SEQ * DEVICE_REQUESTS).astype(jnp.int32)


def touch_ends(result, own_key, least, high):
    longest = result.shape.index(max(result.shape))
    spots = []
    for shift in (0, 1):
        where = [jax.random.randint(jax.random.fold_in(own_key, axis), (), 0, length) for axis, length in enumerate(result.shape)]
        where[longest] = (where[longest] + shift) % result.shape[longest]
        spots.append(tuple(where))
    return result.at[spots[0]].set(least).at[spots[1]].set(high)


def steps_of(key, dims, shards, least, top_value):
    loudness = 1.0
    for dim, blocks in shards:
        steps = jax.random.uniform(jax.random.fold_in(jax.random.fold_in(key, 6), dim), (blocks,), jnp.float32, least / len(shards), top_value / len(shards))
        loudness = loudness * jnp.repeat(jnp.exp(steps), dims[dim] // blocks).reshape((-1,) + (1,) * (len(dims) - 1 - dim))
    return loudness


def rank_bounds(count, slope):
    weights = [(1 << 20) // math.isqrt(standing ** slope) + 1 for standing in range(1, count + 1)]
    width = 1 + sum(weights) // (1 << 30)
    return np.cumsum(np.array([max(1, weight // width) for weight in weights]))


def ranked_ids(key, extent, amount, skew):
    grid = rank_bounds(amount, skew)
    ticket = jax.random.randint(jax.random.fold_in(key, 1), extent, 0, int(grid[amount - 1]))
    grade = jnp.searchsorted(jnp.asarray(grid, jnp.int32), ticket, side="right")
    return jax.random.permutation(jax.random.fold_in(key, 2), amount)[grade].astype(jnp.int32)


def normal_values(own_key, shape, width, bound, cuts=(), kind=jnp.bfloat16):
    values = jax.random.normal(own_key, shape, jnp.float32) * width
    if len(cuts) > 0:
        values = steps_of(own_key, shape, cuts, -0.22, 0.18) * values
    return jnp.clip(values, min=-bound, max=bound).astype(kind)


def setup_inputs(seed: int = 0) -> dict:
    key_list = jax.random.split(jax.random.key(seed), 10)
    tokens = normal_values(key_list[0], (ROWS, MODEL_WIDTH), 1.0, 6.0, ((0, 16),))
    norm_gain = jnp.clip(1.0 + 0.18 * jax.random.normal(key_list[1], (MODEL_WIDTH,), jnp.float32), 0.1, 1.9)
    query_weight = normal_values(key_list[2], (MODEL_WIDTH, QUERY_HEADS * HEAD_SIZE), MODEL_WIDTH ** -0.5, 0.125, ((1, 8),))
    key_value_matrix = normal_values(key_list[3], (MODEL_WIDTH, KEY_VALUE_HEADS, 2 * HEAD_SIZE), MODEL_WIDTH ** -0.5, 0.125)
    out_weight = normal_values(key_list[4], (QUERY_HEADS * HEAD_SIZE, MODEL_WIDTH), (QUERY_HEADS * HEAD_SIZE) ** -0.5, 0.125)
    cache_pages = draw_cache_pages(jax.random.fold_in(key_list[9], 71), 0)
    page_table = draw_page_table(jax.random.fold_in(key_list[9], 71), 0)
    request_lengths = draw_request_lengths(jax.random.fold_in(key_list[9], 71), 0)
    request_groups = touch_ends(ranked_ids(key_list[8], (REQS,), GROUPS, 2), jax.random.fold_in(key_list[8], 3), 0, GROUPS - 1).astype(jnp.int32)
    return dict(tokens=tokens, norm_gain=norm_gain, query_weight=query_weight, key_value_matrix=key_value_matrix, out_weight=out_weight, cache_pages=cache_pages, page_table=page_table, request_lengths=request_lengths, request_groups=request_groups)


MASKED_SCORE = -1e+30

def normalize(tokens, norm_gain):
    widened = tokens.astype(jnp.float32)
    factor = lax.rsqrt(lax.optimization_barrier(jnp.mean(widened * widened, axis=-1, keepdims=True)) + 1e-05)
    return (widened * factor * norm_gain).astype(jnp.bfloat16)

def row_layout(lengths, row_total_count):
    lengths = lengths.astype(jnp.int32)
    request_ends = jnp.cumsum(lengths).astype(jnp.int32)
    starts = request_ends - lengths
    slot_ids = lax.iota(jnp.int32, row_total_count)
    row_request = lax.optimization_barrier(jnp.sum((slot_ids[:, None] >= request_ends[None, :]).astype(jnp.int32), axis=1)).astype(jnp.int32)
    row_live = slot_ids < request_ends[-1]
    choose = row_request[:, None] == lax.iota(jnp.int32, lengths.shape[0])[None, :]
    begins = lax.optimization_barrier(jnp.sum(jnp.where(choose, starts[None, :], 0), axis=1)).astype(jnp.int32)
    return (row_request, row_live, slot_ids - begins)

def reference(tokens, norm_gain, query_weight, key_value_matrix, out_weight, cache_pages, page_table, request_lengths, request_groups):
    score_scale = HEAD_SIZE ** (-0.5)
    query_group_width = QUERY_HEADS // KEY_VALUE_HEADS
    tail_ids = page_table[:, PPG - WP:]
    flattened_weight = key_value_matrix.reshape(MODEL_WIDTH, KEY_VALUE_HEADS * 2 * HEAD_SIZE)

    def one_device(inputs):
        device_tokens, lengths, groups_here = inputs
        normed = normalize(device_tokens, norm_gain)
        query_rows = jnp.dot(normed, query_weight, preferred_element_type=jnp.float32).astype(jnp.bfloat16)
        new_token_rows = jnp.dot(normed, flattened_weight, preferred_element_type=jnp.float32).astype(jnp.bfloat16)
        new_rows_widened = new_token_rows.astype(jnp.float32).reshape(TOKEN_CAPACITY, KEY_VALUE_HEADS, 2 * HEAD_SIZE)
        row_request, row_live, row_position = row_layout(lengths, TOKEN_CAPACITY)
        visible_pages = cache_pages[tail_ids[groups_here]]
        window_widened = jnp.transpose(visible_pages, (0, 2, 1, 3, 4)).reshape(DEVICE_REQUESTS, KEY_VALUE_HEADS, WINDOW_LENGTH, 2 * HEAD_SIZE).astype(jnp.float32)
        query_widened = query_rows.astype(jnp.float32).reshape(TOKEN_CAPACITY // 16, 16, KEY_VALUE_HEADS, query_group_width, HEAD_SIZE)
        column = lax.iota(jnp.int32, TOKEN_CAPACITY)
        offsets = lax.iota(jnp.int32, WINDOW_LENGTH)

        def one_block(block_inputs):
            block_query, block_request, block_live, block_position, block_rows = block_inputs
            picked = window_widened[jnp.minimum(block_request, DEVICE_REQUESTS - 1)]
            prefix_scores = jnp.einsum('rkgd,rkmd->rkgm', block_query, picked[..., :HEAD_SIZE]) * score_scale
            suffix_scores = jnp.einsum('rkgd,ckd->rkgc', block_query, new_rows_widened[..., :HEAD_SIZE]) * score_scale
            prefix_mask = (block_live[:, None] & (offsets[None, :] >= block_position[:, None] + 1))[:, None, None, :]
            suffix_mask = ((row_request[None, :] == block_request[:, None]) & block_live[:, None] & (column[None, :] <= block_rows[:, None]) & (block_rows[:, None] - column[None, :] < WINDOW_LENGTH))[:, None, None, :]
            row_top = jnp.maximum(lax.optimization_barrier(jnp.max(jnp.where(prefix_mask, prefix_scores, MASKED_SCORE), axis=-1)), lax.optimization_barrier(jnp.max(jnp.where(suffix_mask, suffix_scores, MASKED_SCORE), axis=-1)))
            prefix_raw = jnp.where(prefix_mask, jnp.exp(prefix_scores - row_top[..., None]), 0.0)
            suffix_raw = jnp.where(suffix_mask, jnp.exp(suffix_scores - row_top[..., None]), 0.0)
            row_total = lax.optimization_barrier(jnp.sum(prefix_raw, axis=-1)) + lax.optimization_barrier(jnp.sum(suffix_raw, axis=-1))
            prefix_weights = lax.optimization_barrier(prefix_raw.astype(jnp.bfloat16)).astype(jnp.float32)
            suffix_weights = lax.optimization_barrier(suffix_raw.astype(jnp.bfloat16)).astype(jnp.float32)
            weighted = jnp.einsum('rkgm,rkmd->rkgd', prefix_weights, picked[..., HEAD_SIZE:])
            weighted = weighted + jnp.einsum('rkgc,ckd->rkgd', suffix_weights, new_rows_widened[..., HEAD_SIZE:])
            safe_total = jnp.where(block_live[:, None, None], row_total, 1.0)
            attended = jnp.where(block_live[:, None, None, None], weighted / safe_total[..., None], 0.0)
            return attended.astype(jnp.bfloat16).reshape(16, QUERY_HEADS * HEAD_SIZE)
        blocks = (query_widened, row_request.reshape(-1, 16), row_live.reshape(-1, 16), row_position.reshape(-1, 16), column.reshape(-1, 16))
        attended = lax.map(one_block, blocks).reshape(TOKEN_CAPACITY, QUERY_HEADS * HEAD_SIZE)
        return jnp.dot(attended, out_weight, preferred_element_type=jnp.float32).astype(jnp.bfloat16)
    outputs = lax.map(one_device, (tokens.reshape(N_SEQ, TOKEN_CAPACITY, MODEL_WIDTH), request_lengths.reshape(N_SEQ, DEVICE_REQUESTS), request_groups.reshape(N_SEQ, DEVICE_REQUESTS)))
    return outputs.reshape(N_SEQ * TOKEN_CAPACITY, MODEL_WIDTH)
```

```python
import math

import jax
import jax.numpy as jnp
from jax import lax
from jax.sharding import PartitionSpec as P
from jax.experimental import pallas as pl
from jax.experimental.pallas import tpu as pltpu

QUERY_HEADS = 32
KEY_VALUE_HEADS = 4
HEAD_SIZE = 64
WINDOW_LENGTH = 2048
DEVICE_REQUESTS = 5
PPG = 64
WP = 16


MASKED_SCORE = -1e30


def normalize(tokens, norm_gain):
    widened = tokens.astype(jnp.float32)
    factor = lax.rsqrt(jnp.mean(widened * widened, axis=-1, keepdims=True) + 1e-05)
    return (widened * factor * norm_gain).astype(jnp.bfloat16)


def row_layout(lengths, row_total_count):
    request_ends = jnp.cumsum(lengths)
    starts = request_ends - lengths
    slot_ids = lax.iota(jnp.int32, row_total_count)
    row_request = jnp.sum((slot_ids[:, None] >= request_ends[None, :]).astype(jnp.int32), axis=1)
    row_live = slot_ids < request_ends[-1]
    choose = row_request[:, None] == lax.iota(jnp.int32, lengths.shape[0])[None, :]
    begins = jnp.sum(jnp.where(choose, starts[None, :], 0), axis=1)
    return (row_request, row_live, slot_ids - begins)


def lookup_rows(table, wanted):
    table_rows = table.shape[0]
    matches = wanted[:, None] == lax.iota(jnp.int32, table_rows)[None, :]
    return jnp.sum(jnp.where(matches[:, :, None], table[None, :, :], 0), axis=1)


def body(
    tokens,
    norm_gain,
    query_weight,
    key_value_matrix,
    out_weight,
    cache_pages,
    page_table,
    request_lengths,
    request_groups,
):
    seq_count = lax.axis_size("seq")
    seq_index = lax.axis_index("seq")
    tensor_rank_index = lax.axis_index("tensor")
    row_count = tokens.shape[0]
    resident_heads = query_weight.shape[1] // HEAD_SIZE
    key_value_head = tensor_rank_index * resident_heads // (QUERY_HEADS // KEY_VALUE_HEADS)
    group_count = page_table.shape[0]
    per_owner = WP // seq_count
    pages_here = cache_pages.shape[0]
    score_scale = HEAD_SIZE ** (-0.5)
    normed = normalize(tokens, norm_gain)
    query_rows = jnp.dot(normed, query_weight, preferred_element_type=jnp.float32).astype(
        jnp.bfloat16
    )
    query_rows = query_rows.reshape(row_count, resident_heads, HEAD_SIZE)
    head_weight = lax.dynamic_index_in_dim(key_value_matrix, key_value_head, 1, keepdims=False)
    new_token_rows = jnp.dot(normed, head_weight, preferred_element_type=jnp.float32).astype(
        jnp.bfloat16
    )
    lengths = lax.dynamic_slice_in_dim(
        request_lengths, seq_index * DEVICE_REQUESTS, DEVICE_REQUESTS
    )
    my_groups = lax.dynamic_slice_in_dim(
        request_groups, seq_index * DEVICE_REQUESTS, DEVICE_REQUESTS
    )
    tail_ids = page_table[:, PPG - WP :]
    holder = tail_ids // pages_here
    local_slot = tail_ids % pages_here
    earlier = lax.iota(jnp.int32, WP)[:, None] > lax.iota(jnp.int32, WP)[None, :]
    same_owner = holder[:, :, None] == holder[:, None, :]
    tail_rank = jnp.sum((same_owner & earlier[None, :, :]).astype(jnp.int32), axis=2)
    tail_hit = (holder == seq_index)[:, :, None] & (
        tail_rank[:, :, None] == lax.iota(jnp.int32, per_owner)[None, None, :]
    )
    tail_pick = jnp.sum(jnp.where(tail_hit, local_slot[:, :, None], 0), axis=1)
    head_pages = lax.dynamic_index_in_dim(cache_pages, key_value_head, 1, keepdims=False)
    my_holder = lookup_rows(holder, my_groups)
    my_rank = lookup_rows(tail_rank, my_groups)
    outgoing = head_pages[tail_pick.reshape(-1)]
    gathered = lax.all_gather(outgoing, "seq", axis=0, tiled=True)
    where_from = my_holder * (group_count * per_owner) + my_groups[:, None] * per_owner + my_rank
    window_rows = gathered[where_from.reshape(-1)]
    window_rows = window_rows.reshape(DEVICE_REQUESTS, WINDOW_LENGTH, 2 * HEAD_SIZE)
    starts = jnp.cumsum(lengths) - lengths
    bounds = jnp.concatenate([starts, starts + lengths]).astype(jnp.int32)
    fresh_pad = new_token_rows
    query_pad = jnp.concatenate(
        [query_rows, jnp.zeros_like(query_rows)], axis=-1
    ).transpose(1, 0, 2)
    attended = attend(bounds, query_pad, window_rows, fresh_pad)
    gathered_heads = lax.all_gather(attended, "tensor", axis=0, tiled=True)
    columns = out_weight.shape[1] // lax.axis_size("tensor")
    my_columns = lax.dynamic_slice_in_dim(out_weight, tensor_rank_index * columns, columns, 1)
    my_columns = my_columns.reshape(gathered_heads.shape[0], HEAD_SIZE, columns)
    projected = jnp.einsum(
        "hrd,hdc->rc", gathered_heads, my_columns, preferred_element_type=jnp.float32
    )
    return projected.astype(jnp.bfloat16)


BLOCK_ROWS = 64


def attend_kernel(bounds_ref, q_ref, win_ref, fresh_ref, o_ref):
    heads, block_rows, _ = q_ref.shape
    stacked = heads * block_rows
    request_count = win_ref.shape[0]
    window = win_ref.shape[1]
    row_count = fresh_ref.shape[0]
    first_row = pl.program_id(0) * block_rows
    score_scale = HEAD_SIZE ** (-0.5)
    q = q_ref[...].reshape(stacked, 2 * HEAD_SIZE)
    rows = first_row + lax.broadcasted_iota(jnp.int32, (heads, block_rows, 1), 1).reshape(stacked, 1)
    r_first = jnp.int32(0)
    r_last = jnp.int32(-1)
    for k in range(request_count):
        r_first = r_first + (bounds_ref[request_count + k] <= first_row).astype(jnp.int32)
        r_last = r_last + (bounds_ref[k] < first_row + block_rows).astype(jnp.int32)
    r_last = jnp.minimum(r_last, request_count - 1)
    offsets = lax.broadcasted_iota(jnp.int32, (stacked, window), 1)
    column = lax.broadcasted_iota(jnp.int32, (stacked, row_count), 1)
    fresh = fresh_ref[...]

    def one_request(r, out_acc):
        begin = bounds_ref[r]
        finish = bounds_ref[request_count + r]
        in_request = (rows >= begin) & (rows < finish)
        threshold = jnp.where(in_request, rows - begin + 1, window)
        newest = jnp.where(in_request, rows, -1)
        keys = win_ref[r]
        prefix_scores = lax.dot_general(
            q, keys, (((1,), (1,)), ((), ())), preferred_element_type=jnp.float32
        ) * score_scale
        suffix_scores = lax.dot_general(
            q, fresh, (((1,), (1,)), ((), ())), preferred_element_type=jnp.float32
        ) * score_scale
        prefix_mask = offsets >= threshold
        suffix_mask = (
            (column >= begin) & (column <= newest) & (rows - column < WINDOW_LENGTH)
        )
        top = jnp.maximum(
            jnp.max(jnp.where(prefix_mask, prefix_scores, MASKED_SCORE), axis=1, keepdims=True),
            jnp.max(jnp.where(suffix_mask, suffix_scores, MASKED_SCORE), axis=1, keepdims=True),
        )
        prefix_raw = jnp.where(prefix_mask, jnp.exp(prefix_scores - top), 0.0)
        suffix_raw = jnp.where(suffix_mask, jnp.exp(suffix_scores - top), 0.0)
        total = jnp.sum(prefix_raw, axis=1, keepdims=True) + jnp.sum(
            suffix_raw, axis=1, keepdims=True
        )
        weighted = jnp.dot(
            prefix_raw.astype(jnp.bfloat16), keys, preferred_element_type=jnp.float32
        ) + jnp.dot(suffix_raw.astype(jnp.bfloat16), fresh, preferred_element_type=jnp.float32)
        safe_total = jnp.where(in_request, total, 1.0)
        return jnp.where(in_request, weighted / safe_total, out_acc)

    out_acc = lax.fori_loop(
        r_first, r_last + 1, one_request, jnp.zeros((stacked, 2 * HEAD_SIZE), jnp.float32)
    )
    o_ref[...] = out_acc[:, HEAD_SIZE:].astype(o_ref.dtype).reshape(heads, block_rows, HEAD_SIZE)


def attend(bounds, query_pad, window_rows, fresh_rows):
    heads, row_count, width = query_pad.shape
    block_rows = math.gcd(row_count, BLOCK_ROWS)
    requests, window, _ = window_rows.shape
    return pl.pallas_call(
        attend_kernel,
        out_shape=jax.ShapeDtypeStruct((heads, row_count, HEAD_SIZE), jnp.bfloat16),
        grid_spec=pltpu.PrefetchScalarGridSpec(
            num_scalar_prefetch=1,
            grid=(row_count // block_rows,),
            in_specs=[
                pl.BlockSpec((heads, block_rows, width), lambda i, b: (0, i, 0)),
                pl.BlockSpec((requests, window, width), lambda i, b: (0, 0, 0)),
                pl.BlockSpec((row_count, width), lambda i, b: (0, 0)),
            ],
            out_specs=pl.BlockSpec((heads, block_rows, HEAD_SIZE), lambda i, b: (0, i, 0)),
        ),
        compiler_params=pltpu.CompilerParams(
            dimension_semantics=("arbitrary",), vmem_limit_bytes=48 * 1024 * 1024
        ),
    )(bounds, query_pad, window_rows, fresh_rows)


def solution(mesh):
    return jax.shard_map(
        body,
        mesh=mesh,
        in_specs=(
            P("seq", None),
            P(),
            P(None, "tensor"),
            P(),
            P(),
            P("seq", None, None, None),
            P(),
            P(),
            P(),
        ),
        out_specs=P("seq", "tensor"),
        check_vma=False,
    )
```

```python
import math

import jax
import jax.numpy as jnp
from jax import lax
from jax.sharding import PartitionSpec as P
from jax.experimental import pallas as pl
from jax.experimental.pallas import tpu as pltpu

QUERY_HEADS = 32
KEY_VALUE_HEADS = 4
HEAD_SIZE = 64
WINDOW_LENGTH = 2048
DEVICE_REQUESTS = 5
PPG = 64
WP = 16


MASKED_SCORE = -1e30


def normalize(tokens, norm_gain):
    widened = tokens.astype(jnp.float32)
    factor = lax.rsqrt(jnp.mean(widened * widened, axis=-1, keepdims=True) + 1e-05)
    return (widened * factor * norm_gain).astype(jnp.bfloat16)


def row_layout(lengths, row_total_count):
    request_ends = jnp.cumsum(lengths)
    starts = request_ends - lengths
    slot_ids = lax.iota(jnp.int32, row_total_count)
    row_request = jnp.sum((slot_ids[:, None] >= request_ends[None, :]).astype(jnp.int32), axis=1)
    row_live = slot_ids < request_ends[-1]
    choose = row_request[:, None] == lax.iota(jnp.int32, lengths.shape[0])[None, :]
    begins = jnp.sum(jnp.where(choose, starts[None, :], 0), axis=1)
    return (row_request, row_live, slot_ids - begins)


def lookup_rows(table, wanted):
    table_rows = table.shape[0]
    matches = wanted[:, None] == lax.iota(jnp.int32, table_rows)[None, :]
    return jnp.sum(jnp.where(matches[:, :, None], table[None, :, :], 0), axis=1)


def body(
    tokens,
    norm_gain,
    query_weight,
    key_value_matrix,
    out_weight,
    cache_pages,
    page_table,
    request_lengths,
    request_groups,
):
    seq_count = lax.axis_size("seq")
    seq_index = lax.axis_index("seq")
    tensor_rank_index = lax.axis_index("tensor")
    row_count = tokens.shape[0]
    resident_heads = query_weight.shape[1] // HEAD_SIZE
    key_value_head = tensor_rank_index * resident_heads // (QUERY_HEADS // KEY_VALUE_HEADS)
    group_count = page_table.shape[0]
    per_owner = WP // seq_count
    pages_here = cache_pages.shape[0]
    score_scale = HEAD_SIZE ** (-0.5)
    normed = normalize(tokens, norm_gain)
    query_rows = jnp.dot(normed, query_weight, preferred_element_type=jnp.float32).astype(
        jnp.bfloat16
    )
    query_rows = query_rows.reshape(row_count, resident_heads, HEAD_SIZE)
    head_weight = lax.dynamic_index_in_dim(key_value_matrix, key_value_head, 1, keepdims=False)
    new_token_rows = jnp.dot(normed, head_weight, preferred_element_type=jnp.float32).astype(
        jnp.bfloat16
    )
    lengths = lax.dynamic_slice_in_dim(
        request_lengths, seq_index * DEVICE_REQUESTS, DEVICE_REQUESTS
    )
    my_groups = lax.dynamic_slice_in_dim(
        request_groups, seq_index * DEVICE_REQUESTS, DEVICE_REQUESTS
    )
    tail_ids = page_table[:, PPG - WP :]
    holder = tail_ids // pages_here
    local_slot = tail_ids % pages_here
    held_slot = jnp.sum(jnp.where(holder == seq_index, local_slot, 0), axis=1)
    all_groups = request_groups.reshape(seq_count, DEVICE_REQUESTS)
    head_pages = lax.dynamic_index_in_dim(cache_pages, key_value_head, 1, keepdims=False)
    outgoing = head_pages[held_slot[all_groups]]
    incoming = lax.all_to_all(outgoing, "seq", 0, 0, tiled=True)
    page_source = holder[my_groups]
    window_rows = incoming[page_source, lax.iota(jnp.int32, DEVICE_REQUESTS)[:, None]]
    window_rows = window_rows.reshape(DEVICE_REQUESTS, WINDOW_LENGTH, 2 * HEAD_SIZE)
    starts = jnp.cumsum(lengths) - lengths
    bounds = jnp.concatenate([starts, starts + lengths]).astype(jnp.int32)
    fresh_pad = new_token_rows
    query_pad = jnp.concatenate(
        [query_rows, jnp.zeros_like(query_rows)], axis=-1
    ).transpose(1, 0, 2)
    attended = attend(bounds, query_pad, window_rows, fresh_pad)
    gathered_heads = lax.all_gather(attended, "tensor", axis=0, tiled=True)
    columns = out_weight.shape[1] // lax.axis_size("tensor")
    my_columns = lax.dynamic_slice_in_dim(out_weight, tensor_rank_index * columns, columns, 1)
    my_columns = my_columns.reshape(gathered_heads.shape[0], HEAD_SIZE, columns)
    projected = jnp.einsum(
        "hrd,hdc->rc", gathered_heads, my_columns, preferred_element_type=jnp.float32
    )
    return projected.astype(jnp.bfloat16)


BLOCK_ROWS = 64


def attend_kernel(bounds_ref, q_ref, win_ref, fresh_ref, o_ref):
    heads, block_rows, _ = q_ref.shape
    stacked = heads * block_rows
    request_count = win_ref.shape[0]
    window = win_ref.shape[1]
    row_count = fresh_ref.shape[0]
    first_row = pl.program_id(0) * block_rows
    score_scale = HEAD_SIZE ** (-0.5)
    q = q_ref[...].reshape(stacked, 2 * HEAD_SIZE)
    rows = first_row + lax.broadcasted_iota(jnp.int32, (heads, block_rows, 1), 1).reshape(stacked, 1)
    r_first = jnp.int32(0)
    r_last = jnp.int32(-1)
    for k in range(request_count):
        r_first = r_first + (bounds_ref[request_count + k] <= first_row).astype(jnp.int32)
        r_last = r_last + (bounds_ref[k] < first_row + block_rows).astype(jnp.int32)
    r_last = jnp.minimum(r_last, request_count - 1)
    offsets = lax.broadcasted_iota(jnp.int32, (stacked, window), 1)
    column = lax.broadcasted_iota(jnp.int32, (stacked, row_count), 1)
    fresh = fresh_ref[...]

    def one_request(r, out_acc):
        begin = bounds_ref[r]
        finish = bounds_ref[request_count + r]
        in_request = (rows >= begin) & (rows < finish)
        threshold = jnp.where(in_request, rows - begin + 1, window)
        newest = jnp.where(in_request, rows, -1)
        keys = win_ref[r]
        prefix_scores = lax.dot_general(
            q, keys, (((1,), (1,)), ((), ())), preferred_element_type=jnp.float32
        ) * score_scale
        suffix_scores = lax.dot_general(
            q, fresh, (((1,), (1,)), ((), ())), preferred_element_type=jnp.float32
        ) * score_scale
        prefix_mask = offsets >= threshold
        suffix_mask = (
            (column >= begin) & (column <= newest) & (rows - column < WINDOW_LENGTH)
        )
        top = jnp.maximum(
            jnp.max(jnp.where(prefix_mask, prefix_scores, MASKED_SCORE), axis=1, keepdims=True),
            jnp.max(jnp.where(suffix_mask, suffix_scores, MASKED_SCORE), axis=1, keepdims=True),
        )
        prefix_raw = jnp.where(prefix_mask, jnp.exp(prefix_scores - top), 0.0)
        suffix_raw = jnp.where(suffix_mask, jnp.exp(suffix_scores - top), 0.0)
        total = jnp.sum(prefix_raw, axis=1, keepdims=True) + jnp.sum(
            suffix_raw, axis=1, keepdims=True
        )
        weighted = jnp.dot(
            prefix_raw.astype(jnp.bfloat16), keys, preferred_element_type=jnp.float32
        ) + jnp.dot(suffix_raw.astype(jnp.bfloat16), fresh, preferred_element_type=jnp.float32)
        safe_total = jnp.where(in_request, total, 1.0)
        return jnp.where(in_request, weighted / safe_total, out_acc)

    out_acc = lax.fori_loop(
        r_first, r_last + 1, one_request, jnp.zeros((stacked, 2 * HEAD_SIZE), jnp.float32)
    )
    o_ref[...] = out_acc[:, HEAD_SIZE:].astype(o_ref.dtype).reshape(heads, block_rows, HEAD_SIZE)


def attend(bounds, query_pad, window_rows, fresh_rows):
    heads, row_count, width = query_pad.shape
    block_rows = math.gcd(row_count, BLOCK_ROWS)
    requests, window, _ = window_rows.shape
    return pl.pallas_call(
        attend_kernel,
        out_shape=jax.ShapeDtypeStruct((heads, row_count, HEAD_SIZE), jnp.bfloat16),
        grid_spec=pltpu.PrefetchScalarGridSpec(
            num_scalar_prefetch=1,
            grid=(row_count // block_rows,),
            in_specs=[
                pl.BlockSpec((heads, block_rows, width), lambda i, b: (0, i, 0)),
                pl.BlockSpec((requests, window, width), lambda i, b: (0, 0, 0)),
                pl.BlockSpec((row_count, width), lambda i, b: (0, 0)),
            ],
            out_specs=pl.BlockSpec((heads, block_rows, HEAD_SIZE), lambda i, b: (0, i, 0)),
        ),
        compiler_params=pltpu.CompilerParams(
            dimension_semantics=("arbitrary",), vmem_limit_bytes=48 * 1024 * 1024
        ),
    )(bounds, query_pad, window_rows, fresh_rows)


def solution(mesh):
    return jax.shard_map(
        body,
        mesh=mesh,
        in_specs=(
            P("seq", None),
            P(),
            P(None, "tensor"),
            P(),
            P(),
            P("seq", None, None, None),
            P(),
            P(),
            P(),
        ),
        out_specs=P("seq", "tensor"),
        check_vma=False,
    )
```

```python
import math

import jax
import jax.numpy as jnp
from jax import lax
from jax.sharding import PartitionSpec as P
from jax.experimental import pallas as pl
from jax.experimental.pallas import tpu as pltpu

QUERY_HEADS = 32
KEY_VALUE_HEADS = 4
HEAD_SIZE = 64
WINDOW_LENGTH = 2048
DEVICE_REQUESTS = 5
PPG = 64
WP = 16


MASKED_SCORE = -1e30


def normalize(tokens, norm_gain):
    widened = tokens.astype(jnp.float32)
    factor = lax.rsqrt(jnp.mean(widened * widened, axis=-1, keepdims=True) + 1e-05)
    return (widened * factor * norm_gain).astype(jnp.bfloat16)


def row_layout(lengths, row_total_count):
    request_ends = jnp.cumsum(lengths)
    starts = request_ends - lengths
    slot_ids = lax.iota(jnp.int32, row_total_count)
    row_request = jnp.sum((slot_ids[:, None] >= request_ends[None, :]).astype(jnp.int32), axis=1)
    row_live = slot_ids < request_ends[-1]
    choose = row_request[:, None] == lax.iota(jnp.int32, lengths.shape[0])[None, :]
    begins = jnp.sum(jnp.where(choose, starts[None, :], 0), axis=1)
    return (row_request, row_live, slot_ids - begins)


def lookup_rows(table, wanted):
    table_rows = table.shape[0]
    matches = wanted[:, None] == lax.iota(jnp.int32, table_rows)[None, :]
    return jnp.sum(jnp.where(matches[:, :, None], table[None, :, :], 0), axis=1)


def body(
    tokens,
    norm_gain,
    query_weight,
    key_value_matrix,
    out_weight,
    cache_pages,
    page_table,
    request_lengths,
    request_groups,
):
    seq_count = lax.axis_size("seq")
    seq_index = lax.axis_index("seq")
    core_index = lax.axis_index("tc")
    tensor_rank_index = lax.axis_index("tz") * lax.axis_size("tc") + core_index
    row_count = tokens.shape[0]
    resident_heads = query_weight.shape[1] // HEAD_SIZE
    key_value_head = tensor_rank_index * resident_heads // (QUERY_HEADS // KEY_VALUE_HEADS)
    group_count = page_table.shape[0]
    per_owner = WP // seq_count
    pages_here = cache_pages.shape[0]
    score_scale = HEAD_SIZE ** (-0.5)
    normed = normalize(tokens, norm_gain)
    query_rows = jnp.dot(normed, query_weight, preferred_element_type=jnp.float32).astype(
        jnp.bfloat16
    )
    query_rows = query_rows.reshape(row_count, resident_heads, HEAD_SIZE)
    head_weight = lax.dynamic_index_in_dim(key_value_matrix, key_value_head, 1, keepdims=False)
    new_token_rows = jnp.dot(normed, head_weight, preferred_element_type=jnp.float32).astype(
        jnp.bfloat16
    )
    lengths = lax.dynamic_slice_in_dim(
        request_lengths, seq_index * DEVICE_REQUESTS, DEVICE_REQUESTS
    )
    my_groups = lax.dynamic_slice_in_dim(
        request_groups, seq_index * DEVICE_REQUESTS, DEVICE_REQUESTS
    )
    tail_ids = page_table[:, PPG - WP :]
    holder = tail_ids // pages_here
    local_slot = tail_ids % pages_here
    held_slot = jnp.sum(jnp.where(holder == seq_index, local_slot, 0), axis=1)
    all_groups = request_groups.reshape(seq_count, DEVICE_REQUESTS)
    head_pages = lax.dynamic_index_in_dim(cache_pages, key_value_head, 1, keepdims=False)
    page_part = head_pages.shape[1] // lax.axis_size("tc")
    head_pages = lax.dynamic_slice_in_dim(head_pages, core_index * page_part, page_part, 1)
    outgoing = head_pages[held_slot[all_groups]]
    incoming = lax.all_to_all(outgoing, "seq", 0, 0, tiled=True)
    both_parts = lax.all_gather(incoming, "tc", axis=0)
    page_source = holder[my_groups]
    window_rows = both_parts[
        lax.iota(jnp.int32, both_parts.shape[0])[None, None, :],
        page_source[:, :, None],
        lax.iota(jnp.int32, DEVICE_REQUESTS)[:, None, None],
    ]
    window_rows = window_rows.reshape(DEVICE_REQUESTS, WINDOW_LENGTH, 2 * HEAD_SIZE)
    starts = jnp.cumsum(lengths) - lengths
    bounds = jnp.concatenate([starts, starts + lengths]).astype(jnp.int32)
    fresh_pad = new_token_rows
    query_pad = jnp.concatenate(
        [query_rows, jnp.zeros_like(query_rows)], axis=-1
    ).transpose(1, 0, 2)
    attended = attend(bounds, query_pad, window_rows, fresh_pad)
    along_z = lax.all_gather(attended, "tz", axis=0)
    all_heads = lax.all_gather(along_z, "tc", axis=0)
    columns = out_weight.shape[1] // (lax.axis_size("tz") * lax.axis_size("tc"))
    my_columns = lax.dynamic_slice_in_dim(out_weight, tensor_rank_index * columns, columns, 1)
    my_columns = my_columns.reshape(
        along_z.shape[0], all_heads.shape[0], resident_heads, HEAD_SIZE, columns
    )
    projected = jnp.einsum(
        "czhrd,zchdn->rn", all_heads, my_columns, preferred_element_type=jnp.float32
    )
    return projected.astype(jnp.bfloat16)


BLOCK_ROWS = 64


def attend_kernel(bounds_ref, q_ref, win_ref, fresh_ref, o_ref):
    heads, block_rows, _ = q_ref.shape
    stacked = heads * block_rows
    request_count = win_ref.shape[0]
    window = win_ref.shape[1]
    row_count = fresh_ref.shape[0]
    first_row = pl.program_id(0) * block_rows
    score_scale = HEAD_SIZE ** (-0.5)
    q = q_ref[...].reshape(stacked, 2 * HEAD_SIZE)
    rows = first_row + lax.broadcasted_iota(jnp.int32, (heads, block_rows, 1), 1).reshape(stacked, 1)
    r_first = jnp.int32(0)
    r_last = jnp.int32(-1)
    for k in range(request_count):
        r_first = r_first + (bounds_ref[request_count + k] <= first_row).astype(jnp.int32)
        r_last = r_last + (bounds_ref[k] < first_row + block_rows).astype(jnp.int32)
    r_last = jnp.minimum(r_last, request_count - 1)
    offsets = lax.broadcasted_iota(jnp.int32, (stacked, window), 1)
    column = lax.broadcasted_iota(jnp.int32, (stacked, row_count), 1)
    fresh = fresh_ref[...]

    def one_request(r, out_acc):
        begin = bounds_ref[r]
        finish = bounds_ref[request_count + r]
        in_request = (rows >= begin) & (rows < finish)
        threshold = jnp.where(in_request, rows - begin + 1, window)
        newest = jnp.where(in_request, rows, -1)
        keys = win_ref[r]
        prefix_scores = lax.dot_general(
            q, keys, (((1,), (1,)), ((), ())), preferred_element_type=jnp.float32
        ) * score_scale
        suffix_scores = lax.dot_general(
            q, fresh, (((1,), (1,)), ((), ())), preferred_element_type=jnp.float32
        ) * score_scale
        prefix_mask = offsets >= threshold
        suffix_mask = (
            (column >= begin) & (column <= newest) & (rows - column < WINDOW_LENGTH)
        )
        top = jnp.maximum(
            jnp.max(jnp.where(prefix_mask, prefix_scores, MASKED_SCORE), axis=1, keepdims=True),
            jnp.max(jnp.where(suffix_mask, suffix_scores, MASKED_SCORE), axis=1, keepdims=True),
        )
        prefix_raw = jnp.where(prefix_mask, jnp.exp(prefix_scores - top), 0.0)
        suffix_raw = jnp.where(suffix_mask, jnp.exp(suffix_scores - top), 0.0)
        total = jnp.sum(prefix_raw, axis=1, keepdims=True) + jnp.sum(
            suffix_raw, axis=1, keepdims=True
        )
        weighted = jnp.dot(
            prefix_raw.astype(jnp.bfloat16), keys, preferred_element_type=jnp.float32
        ) + jnp.dot(suffix_raw.astype(jnp.bfloat16), fresh, preferred_element_type=jnp.float32)
        safe_total = jnp.where(in_request, total, 1.0)
        return jnp.where(in_request, weighted / safe_total, out_acc)

    out_acc = lax.fori_loop(
        r_first, r_last + 1, one_request, jnp.zeros((stacked, 2 * HEAD_SIZE), jnp.float32)
    )
    o_ref[...] = out_acc[:, HEAD_SIZE:].astype(o_ref.dtype).reshape(heads, block_rows, HEAD_SIZE)


def attend(bounds, query_pad, window_rows, fresh_rows):
    heads, row_count, width = query_pad.shape
    block_rows = math.gcd(row_count, BLOCK_ROWS)
    requests, window, _ = window_rows.shape
    return pl.pallas_call(
        attend_kernel,
        out_shape=jax.ShapeDtypeStruct((heads, row_count, HEAD_SIZE), jnp.bfloat16),
        grid_spec=pltpu.PrefetchScalarGridSpec(
            num_scalar_prefetch=1,
            grid=(row_count // block_rows,),
            in_specs=[
                pl.BlockSpec((heads, block_rows, width), lambda i, b: (0, i, 0)),
                pl.BlockSpec((requests, window, width), lambda i, b: (0, 0, 0)),
                pl.BlockSpec((row_count, width), lambda i, b: (0, 0)),
            ],
            out_specs=pl.BlockSpec((heads, block_rows, HEAD_SIZE), lambda i, b: (0, i, 0)),
        ),
        compiler_params=pltpu.CompilerParams(
            dimension_semantics=("arbitrary",), vmem_limit_bytes=48 * 1024 * 1024
        ),
    )(bounds, query_pad, window_rows, fresh_rows)


def solution(mesh):
    cores = 2
    seq_size, tensor_size = mesh.devices.shape
    split_mesh = jax.sharding.Mesh(
        mesh.devices.reshape(seq_size, tensor_size // cores, cores), ("seq", "tz", "tc")
    )
    return jax.shard_map(
        body,
        mesh=split_mesh,
        in_specs=(
            P("seq", None),
            P(),
            P(None, ("tz", "tc")),
            P(),
            P(),
            P("seq", None, None, None),
            P(),
            P(),
            P(),
        ),
        out_specs=P("seq", ("tz", "tc")),
        check_vma=False,
    )
```

```python
import math

import jax
import jax.numpy as jnp
from jax import lax
from jax.sharding import PartitionSpec as P
from jax.experimental import pallas as pl
from jax.experimental.pallas import tpu as pltpu

QUERY_HEADS = 32
KEY_VALUE_HEADS = 4
HEAD_SIZE = 64
WINDOW_LENGTH = 2048
DEVICE_REQUESTS = 5
PPG = 64
WP = 16


MASKED_SCORE = -1e30


def normalize(tokens, norm_gain):
    widened = tokens.astype(jnp.float32)
    factor = lax.rsqrt(jnp.mean(widened * widened, axis=-1, keepdims=True) + 1e-05)
    return (widened * factor * norm_gain).astype(jnp.bfloat16)


def row_layout(lengths, row_total_count):
    request_ends = jnp.cumsum(lengths)
    starts = request_ends - lengths
    slot_ids = lax.iota(jnp.int32, row_total_count)
    row_request = jnp.sum((slot_ids[:, None] >= request_ends[None, :]).astype(jnp.int32), axis=1)
    row_live = slot_ids < request_ends[-1]
    choose = row_request[:, None] == lax.iota(jnp.int32, lengths.shape[0])[None, :]
    begins = jnp.sum(jnp.where(choose, starts[None, :], 0), axis=1)
    return (row_request, row_live, slot_ids - begins)


def lookup_rows(table, wanted):
    table_rows = table.shape[0]
    matches = wanted[:, None] == lax.iota(jnp.int32, table_rows)[None, :]
    return jnp.sum(jnp.where(matches[:, :, None], table[None, :, :], 0), axis=1)


def body(
    tokens,
    norm_gain,
    query_weight,
    key_value_matrix,
    out_weight,
    cache_pages,
    page_table,
    request_lengths,
    request_groups,
):
    seq_count = lax.axis_size("seq")
    seq_index = lax.axis_index("seq")
    core_index = lax.axis_index("tc")
    tensor_rank_index = lax.axis_index("tz") * lax.axis_size("tc") + core_index
    row_count = tokens.shape[0]
    resident_heads = query_weight.shape[1] // HEAD_SIZE
    key_value_head = tensor_rank_index * resident_heads // (QUERY_HEADS // KEY_VALUE_HEADS)
    group_count = page_table.shape[0]
    per_owner = WP // seq_count
    pages_here = cache_pages.shape[0]
    score_scale = HEAD_SIZE ** (-0.5)
    normed = normalize(tokens, norm_gain)
    query_rows = jnp.dot(normed, query_weight, preferred_element_type=jnp.float32).astype(
        jnp.bfloat16
    )
    query_rows = query_rows.reshape(row_count, resident_heads, HEAD_SIZE)
    head_weight = lax.dynamic_index_in_dim(key_value_matrix, key_value_head, 1, keepdims=False)
    new_token_rows = jnp.dot(normed, head_weight, preferred_element_type=jnp.float32).astype(
        jnp.bfloat16
    )
    lengths = lax.dynamic_slice_in_dim(
        request_lengths, seq_index * DEVICE_REQUESTS, DEVICE_REQUESTS
    )
    my_groups = lax.dynamic_slice_in_dim(
        request_groups, seq_index * DEVICE_REQUESTS, DEVICE_REQUESTS
    )
    tail_ids = page_table[:, PPG - WP :]
    holder = tail_ids // pages_here
    local_slot = tail_ids % pages_here
    held_slot = jnp.sum(jnp.where(holder == seq_index, local_slot, 0), axis=1)
    all_groups = request_groups.reshape(seq_count, DEVICE_REQUESTS)
    head_pages = lax.dynamic_index_in_dim(cache_pages, key_value_head, 1, keepdims=False)
    page_part = head_pages.shape[1] // lax.axis_size("tc")
    head_pages = lax.dynamic_slice_in_dim(head_pages, core_index * page_part, page_part, 1)
    outgoing = head_pages[held_slot[all_groups]]
    incoming = lax.all_to_all(outgoing, "seq", 0, 0, tiled=True)
    both_parts = lax.all_gather(incoming, "tc", axis=0)
    page_source = holder[my_groups]
    window_rows = both_parts[
        lax.iota(jnp.int32, both_parts.shape[0])[None, None, :],
        page_source[:, :, None],
        lax.iota(jnp.int32, DEVICE_REQUESTS)[:, None, None],
    ]
    window_rows = window_rows.reshape(DEVICE_REQUESTS, WINDOW_LENGTH, 2 * HEAD_SIZE)
    starts = jnp.cumsum(lengths) - lengths
    bounds = jnp.concatenate([starts, starts + lengths]).astype(jnp.int32)
    fresh_pad = new_token_rows
    query_pad = jnp.concatenate(
        [query_rows, jnp.zeros_like(query_rows)], axis=-1
    ).transpose(1, 0, 2)
    attended = attend(bounds, query_pad, window_rows, fresh_pad)
    all_heads = lax.all_gather(attended, ("tz", "tc"), axis=1, tiled=True)
    columns = out_weight.shape[1] // (lax.axis_size("tz") * lax.axis_size("tc"))
    my_columns = lax.dynamic_slice_in_dim(out_weight, tensor_rank_index * columns, columns, 1)
    projected = jnp.dot(all_heads, my_columns, preferred_element_type=jnp.float32)
    return projected.astype(jnp.bfloat16)


BLOCK_ROWS = 64


def attend_kernel(bounds_ref, q_ref, win_ref, fresh_ref, o_ref):
    heads, block_rows, _ = q_ref.shape
    stacked = heads * block_rows
    request_count = win_ref.shape[0]
    window = win_ref.shape[1]
    row_count = fresh_ref.shape[0]
    first_row = pl.program_id(0) * block_rows
    score_scale = HEAD_SIZE ** (-0.5)
    q = q_ref[...].reshape(stacked, 2 * HEAD_SIZE)
    rows = first_row + lax.broadcasted_iota(jnp.int32, (heads, block_rows, 1), 1).reshape(stacked, 1)
    r_first = jnp.int32(0)
    r_last = jnp.int32(-1)
    for k in range(request_count):
        r_first = r_first + (bounds_ref[request_count + k] <= first_row).astype(jnp.int32)
        r_last = r_last + (bounds_ref[k] < first_row + block_rows).astype(jnp.int32)
    r_last = jnp.minimum(r_last, request_count - 1)
    offsets = lax.broadcasted_iota(jnp.int32, (stacked, window), 1)
    column = lax.broadcasted_iota(jnp.int32, (stacked, row_count), 1)
    fresh = fresh_ref[...]

    def one_request(r, out_acc):
        begin = bounds_ref[r]
        finish = bounds_ref[request_count + r]
        in_request = (rows >= begin) & (rows < finish)
        threshold = jnp.where(in_request, rows - begin + 1, window)
        newest = jnp.where(in_request, rows, -1)
        keys = win_ref[r]
        prefix_scores = lax.dot_general(
            q, keys, (((1,), (1,)), ((), ())), preferred_element_type=jnp.float32
        ) * score_scale
        suffix_scores = lax.dot_general(
            q, fresh, (((1,), (1,)), ((), ())), preferred_element_type=jnp.float32
        ) * score_scale
        prefix_mask = offsets >= threshold
        suffix_mask = (
            (column >= begin) & (column <= newest) & (rows - column < WINDOW_LENGTH)
        )
        top = jnp.maximum(
            jnp.max(jnp.where(prefix_mask, prefix_scores, MASKED_SCORE), axis=1, keepdims=True),
            jnp.max(jnp.where(suffix_mask, suffix_scores, MASKED_SCORE), axis=1, keepdims=True),
        )
        prefix_raw = jnp.where(prefix_mask, jnp.exp(prefix_scores - top), 0.0)
        suffix_raw = jnp.where(suffix_mask, jnp.exp(suffix_scores - top), 0.0)
        total = jnp.sum(prefix_raw, axis=1, keepdims=True) + jnp.sum(
            suffix_raw, axis=1, keepdims=True
        )
        weighted = jnp.dot(
            prefix_raw.astype(jnp.bfloat16), keys, preferred_element_type=jnp.float32
        ) + jnp.dot(suffix_raw.astype(jnp.bfloat16), fresh, preferred_element_type=jnp.float32)
        safe_total = jnp.where(in_request, total, 1.0)
        return jnp.where(in_request, weighted / safe_total, out_acc)

    out_acc = lax.fori_loop(
        r_first, r_last + 1, one_request, jnp.zeros((stacked, 2 * HEAD_SIZE), jnp.float32)
    )
    result = out_acc[:, HEAD_SIZE:].astype(o_ref.dtype)
    for h in range(heads):
        o_ref[:, h * HEAD_SIZE : (h + 1) * HEAD_SIZE] = result[h * block_rows : (h + 1) * block_rows]


def attend(bounds, query_pad, window_rows, fresh_rows):
    heads, row_count, width = query_pad.shape
    block_rows = math.gcd(row_count, BLOCK_ROWS)
    requests, window, _ = window_rows.shape
    return pl.pallas_call(
        attend_kernel,
        out_shape=jax.ShapeDtypeStruct((row_count, heads * HEAD_SIZE), jnp.bfloat16),
        grid_spec=pltpu.PrefetchScalarGridSpec(
            num_scalar_prefetch=1,
            grid=(row_count // block_rows,),
            in_specs=[
                pl.BlockSpec((heads, block_rows, width), lambda i, b: (0, i, 0)),
                pl.BlockSpec((requests, window, width), lambda i, b: (0, 0, 0)),
                pl.BlockSpec((row_count, width), lambda i, b: (0, 0)),
            ],
            out_specs=pl.BlockSpec((block_rows, heads * HEAD_SIZE), lambda i, b: (i, 0)),
        ),
        compiler_params=pltpu.CompilerParams(
            dimension_semantics=("arbitrary",), vmem_limit_bytes=48 * 1024 * 1024
        ),
    )(bounds, query_pad, window_rows, fresh_rows)


def solution(mesh):
    cores = 2
    seq_size, tensor_size = mesh.devices.shape
    split_mesh = jax.sharding.Mesh(
        mesh.devices.reshape(seq_size, tensor_size // cores, cores), ("seq", "tz", "tc")
    )
    return jax.shard_map(
        body,
        mesh=split_mesh,
        in_specs=(
            P("seq", None),
            P(),
            P(None, ("tz", "tc")),
            P(),
            P(),
            P("seq", None, None, None),
            P(),
            P(),
            P(),
        ),
        out_specs=P("seq", ("tz", "tc")),
        check_vma=False,
    )
```

```python
import math

import jax
import jax.numpy as jnp
from jax import lax
from jax.sharding import PartitionSpec as P
from jax.experimental import pallas as pl
from jax.experimental.pallas import tpu as pltpu

QUERY_HEADS = 32
KEY_VALUE_HEADS = 4
HEAD_SIZE = 64
WINDOW_LENGTH = 2048
DEVICE_REQUESTS = 5
PPG = 64
WP = 16


MASKED_SCORE = -1e30


def normalize(tokens, norm_gain):
    widened = tokens.astype(jnp.float32)
    factor = lax.rsqrt(jnp.mean(widened * widened, axis=-1, keepdims=True) + 1e-05)
    return (widened * factor * norm_gain).astype(jnp.bfloat16)


def row_layout(lengths, row_total_count):
    request_ends = jnp.cumsum(lengths)
    starts = request_ends - lengths
    slot_ids = lax.iota(jnp.int32, row_total_count)
    row_request = jnp.sum((slot_ids[:, None] >= request_ends[None, :]).astype(jnp.int32), axis=1)
    row_live = slot_ids < request_ends[-1]
    choose = row_request[:, None] == lax.iota(jnp.int32, lengths.shape[0])[None, :]
    begins = jnp.sum(jnp.where(choose, starts[None, :], 0), axis=1)
    return (row_request, row_live, slot_ids - begins)


def lookup_rows(table, wanted):
    table_rows = table.shape[0]
    matches = wanted[:, None] == lax.iota(jnp.int32, table_rows)[None, :]
    return jnp.sum(jnp.where(matches[:, :, None], table[None, :, :], 0), axis=1)


def body(
    tokens,
    norm_gain,
    query_weight,
    key_value_matrix,
    out_weight,
    cache_pages,
    page_table,
    request_lengths,
    request_groups,
):
    seq_count = lax.axis_size("seq")
    seq_index = lax.axis_index("seq")
    core_index = lax.axis_index("tc")
    tensor_rank_index = lax.axis_index("tz") * lax.axis_size("tc") + core_index
    row_count = tokens.shape[0]
    resident_heads = query_weight.shape[1] // HEAD_SIZE
    key_value_head = tensor_rank_index * resident_heads // (QUERY_HEADS // KEY_VALUE_HEADS)
    group_count = page_table.shape[0]
    per_owner = WP // seq_count
    pages_here = cache_pages.shape[0]
    score_scale = HEAD_SIZE ** (-0.5)
    normed = normalize(tokens, norm_gain)
    query_rows = jnp.dot(normed, query_weight, preferred_element_type=jnp.float32).astype(
        jnp.bfloat16
    )
    query_rows = query_rows.reshape(row_count, resident_heads, HEAD_SIZE)
    head_weight = lax.dynamic_index_in_dim(key_value_matrix, key_value_head, 1, keepdims=False)
    new_token_rows = jnp.dot(normed, head_weight, preferred_element_type=jnp.float32).astype(
        jnp.bfloat16
    )
    lengths = lax.dynamic_slice_in_dim(
        request_lengths, seq_index * DEVICE_REQUESTS, DEVICE_REQUESTS
    )
    my_groups = lax.dynamic_slice_in_dim(
        request_groups, seq_index * DEVICE_REQUESTS, DEVICE_REQUESTS
    )
    tail_ids = page_table[:, PPG - WP :]
    holder = tail_ids // pages_here
    local_slot = tail_ids % pages_here
    held_slot = jnp.sum(jnp.where(holder == seq_index, local_slot, 0), axis=1)
    all_groups = request_groups.reshape(seq_count, DEVICE_REQUESTS)
    head_pages = lax.dynamic_index_in_dim(cache_pages, key_value_head, 1, keepdims=False)
    page_part = head_pages.shape[1] // lax.axis_size("tc")
    head_pages = lax.dynamic_slice_in_dim(head_pages, core_index * page_part, page_part, 1)
    outgoing = head_pages[held_slot[all_groups]]
    incoming = lax.all_to_all(outgoing, "seq", 0, 0, tiled=True)
    both_parts = lax.all_gather(incoming, "tc", axis=0)
    page_source = holder[my_groups]
    window_rows = both_parts[
        lax.iota(jnp.int32, both_parts.shape[0])[None, None, :],
        page_source[:, :, None],
        lax.iota(jnp.int32, DEVICE_REQUESTS)[:, None, None],
    ]
    window_rows = window_rows.reshape(DEVICE_REQUESTS, WINDOW_LENGTH, 2 * HEAD_SIZE)
    starts = jnp.cumsum(lengths) - lengths
    bounds = jnp.concatenate([starts, starts + lengths]).astype(jnp.int32)
    fresh_pad = new_token_rows
    query_pad = jnp.concatenate(
        [query_rows, jnp.zeros_like(query_rows)], axis=-1
    ).transpose(1, 0, 2)
    attended = attend(bounds, query_pad, window_rows, fresh_pad)
    along_z = lax.all_gather(attended, "tz", axis=1, tiled=True)
    all_heads = lax.all_gather(along_z, "tc", axis=1)
    z_count = lax.axis_size("tz")
    core_count = lax.axis_size("tc")
    columns = out_weight.shape[1] // (z_count * core_count)
    my_columns = lax.dynamic_slice_in_dim(out_weight, tensor_rank_index * columns, columns, 1)
    my_columns = my_columns.reshape(z_count, core_count, attended.shape[1], columns)
    all_heads = all_heads.reshape(row_count, core_count, z_count, attended.shape[1])
    projected = jnp.einsum(
        "rczj,zcjn->rn", all_heads, my_columns, preferred_element_type=jnp.float32
    )
    return projected.astype(jnp.bfloat16)


BLOCK_ROWS = 64


def attend_kernel(bounds_ref, q_ref, win_ref, fresh_ref, o_ref):
    heads, block_rows, _ = q_ref.shape
    stacked = heads * block_rows
    request_count = win_ref.shape[0]
    window = win_ref.shape[1]
    row_count = fresh_ref.shape[0]
    first_row = pl.program_id(0) * block_rows
    score_scale = HEAD_SIZE ** (-0.5)
    q = q_ref[...].reshape(stacked, 2 * HEAD_SIZE)
    rows = first_row + lax.broadcasted_iota(jnp.int32, (heads, block_rows, 1), 1).reshape(stacked, 1)
    r_first = jnp.int32(0)
    r_last = jnp.int32(-1)
    for k in range(request_count):
        r_first = r_first + (bounds_ref[request_count + k] <= first_row).astype(jnp.int32)
        r_last = r_last + (bounds_ref[k] < first_row + block_rows).astype(jnp.int32)
    r_last = jnp.minimum(r_last, request_count - 1)
    offsets = lax.broadcasted_iota(jnp.int32, (stacked, window), 1)
    column = lax.broadcasted_iota(jnp.int32, (stacked, row_count), 1)
    fresh = fresh_ref[...]

    def one_request(r, out_acc):
        begin = bounds_ref[r]
        finish = bounds_ref[request_count + r]
        in_request = (rows >= begin) & (rows < finish)
        threshold = jnp.where(in_request, rows - begin + 1, window)
        newest = jnp.where(in_request, rows, -1)
        keys = win_ref[r]
        prefix_scores = lax.dot_general(
            q, keys, (((1,), (1,)), ((), ())), preferred_element_type=jnp.float32
        ) * score_scale
        suffix_scores = lax.dot_general(
            q, fresh, (((1,), (1,)), ((), ())), preferred_element_type=jnp.float32
        ) * score_scale
        prefix_mask = offsets >= threshold
        suffix_mask = (
            (column >= begin) & (column <= newest) & (rows - column < WINDOW_LENGTH)
        )
        top = jnp.maximum(
            jnp.max(jnp.where(prefix_mask, prefix_scores, MASKED_SCORE), axis=1, keepdims=True),
            jnp.max(jnp.where(suffix_mask, suffix_scores, MASKED_SCORE), axis=1, keepdims=True),
        )
        prefix_raw = jnp.where(prefix_mask, jnp.exp(prefix_scores - top), 0.0)
        suffix_raw = jnp.where(suffix_mask, jnp.exp(suffix_scores - top), 0.0)
        total = jnp.sum(prefix_raw, axis=1, keepdims=True) + jnp.sum(
            suffix_raw, axis=1, keepdims=True
        )
        weighted = jnp.dot(
            prefix_raw.astype(jnp.bfloat16), keys, preferred_element_type=jnp.float32
        ) + jnp.dot(suffix_raw.astype(jnp.bfloat16), fresh, preferred_element_type=jnp.float32)
        safe_total = jnp.where(in_request, total, 1.0)
        return jnp.where(in_request, weighted / safe_total, out_acc)

    out_acc = lax.fori_loop(
        r_first, r_last + 1, one_request, jnp.zeros((stacked, 2 * HEAD_SIZE), jnp.float32)
    )
    result = out_acc[:, HEAD_SIZE:].astype(o_ref.dtype)
    for h in range(heads):
        o_ref[:, h * HEAD_SIZE : (h + 1) * HEAD_SIZE] = result[h * block_rows : (h + 1) * block_rows]


def attend(bounds, query_pad, window_rows, fresh_rows):
    heads, row_count, width = query_pad.shape
    block_rows = math.gcd(row_count, BLOCK_ROWS)
    requests, window, _ = window_rows.shape
    return pl.pallas_call(
        attend_kernel,
        out_shape=jax.ShapeDtypeStruct((row_count, heads * HEAD_SIZE), jnp.bfloat16),
        grid_spec=pltpu.PrefetchScalarGridSpec(
            num_scalar_prefetch=1,
            grid=(row_count // block_rows,),
            in_specs=[
                pl.BlockSpec((heads, block_rows, width), lambda i, b: (0, i, 0)),
                pl.BlockSpec((requests, window, width), lambda i, b: (0, 0, 0)),
                pl.BlockSpec((row_count, width), lambda i, b: (0, 0)),
            ],
            out_specs=pl.BlockSpec((block_rows, heads * HEAD_SIZE), lambda i, b: (i, 0)),
        ),
        compiler_params=pltpu.CompilerParams(
            dimension_semantics=("arbitrary",), vmem_limit_bytes=48 * 1024 * 1024
        ),
    )(bounds, query_pad, window_rows, fresh_rows)


def solution(mesh):
    cores = 2
    seq_size, tensor_size = mesh.devices.shape
    split_mesh = jax.sharding.Mesh(
        mesh.devices.reshape(seq_size, tensor_size // cores, cores), ("seq", "tz", "tc")
    )
    return jax.shard_map(
        body,
        mesh=split_mesh,
        in_specs=(
            P("seq", None),
            P(),
            P(None, ("tz", "tc")),
            P(),
            P(),
            P("seq", None, None, None),
            P(),
            P(),
            P(),
        ),
        out_specs=P("seq", ("tz", "tc")),
        check_vma=False,
    )
```

```python
import functools
import math

import jax
import jax.numpy as jnp
from jax import lax
from jax.sharding import PartitionSpec as P
from jax.experimental import pallas as pl
from jax.experimental.pallas import tpu as pltpu

QUERY_HEADS = 32
KEY_VALUE_HEADS = 4
HEAD_SIZE = 64
WINDOW_LENGTH = 2048
DEVICE_REQUESTS = 5
PPG = 64
WP = 16


MASKED_SCORE = -1e30


def normalize(tokens, norm_gain):
    widened = tokens.astype(jnp.float32)
    factor = lax.rsqrt(jnp.mean(widened * widened, axis=-1, keepdims=True) + 1e-05)
    return (widened * factor * norm_gain).astype(jnp.bfloat16)


def row_layout(lengths, row_total_count):
    request_ends = jnp.cumsum(lengths)
    starts = request_ends - lengths
    slot_ids = lax.iota(jnp.int32, row_total_count)
    row_request = jnp.sum((slot_ids[:, None] >= request_ends[None, :]).astype(jnp.int32), axis=1)
    row_live = slot_ids < request_ends[-1]
    choose = row_request[:, None] == lax.iota(jnp.int32, lengths.shape[0])[None, :]
    begins = jnp.sum(jnp.where(choose, starts[None, :], 0), axis=1)
    return (row_request, row_live, slot_ids - begins)


def lookup_rows(table, wanted):
    table_rows = table.shape[0]
    matches = wanted[:, None] == lax.iota(jnp.int32, table_rows)[None, :]
    return jnp.sum(jnp.where(matches[:, :, None], table[None, :, :], 0), axis=1)


def body(
    tokens,
    norm_gain,
    query_weight,
    key_value_matrix,
    out_weight,
    cache_pages,
    page_table,
    request_lengths,
    request_groups,
):
    seq_count = lax.axis_size("seq")
    seq_index = lax.axis_index("seq")
    core_index = lax.axis_index("tc")
    tensor_rank_index = lax.axis_index("tz") * lax.axis_size("tc") + core_index
    row_count = tokens.shape[0]
    resident_heads = query_weight.shape[1] // HEAD_SIZE
    key_value_head = tensor_rank_index * resident_heads // (QUERY_HEADS // KEY_VALUE_HEADS)
    group_count = page_table.shape[0]
    per_owner = WP // seq_count
    pages_here = cache_pages.shape[0]
    score_scale = HEAD_SIZE ** (-0.5)
    normed = normalize(tokens, norm_gain)
    query_rows = jnp.dot(normed, query_weight, preferred_element_type=jnp.float32).astype(
        jnp.bfloat16
    )
    query_rows = query_rows.reshape(row_count, resident_heads, HEAD_SIZE)
    head_weight = lax.dynamic_index_in_dim(key_value_matrix, key_value_head, 1, keepdims=False)
    new_token_rows = jnp.dot(normed, head_weight, preferred_element_type=jnp.float32).astype(
        jnp.bfloat16
    )
    lengths = lax.dynamic_slice_in_dim(
        request_lengths, seq_index * DEVICE_REQUESTS, DEVICE_REQUESTS
    )
    my_groups = lax.dynamic_slice_in_dim(
        request_groups, seq_index * DEVICE_REQUESTS, DEVICE_REQUESTS
    )
    tail_ids = page_table[:, PPG - WP :]
    holder = tail_ids // pages_here
    local_slot = tail_ids % pages_here
    held_slot = jnp.sum(jnp.where(holder == seq_index, local_slot, 0), axis=1)
    all_groups = request_groups.reshape(seq_count, DEVICE_REQUESTS)
    head_pages = lax.dynamic_index_in_dim(cache_pages, key_value_head, 1, keepdims=False)
    page_part = head_pages.shape[1] // lax.axis_size("tc")
    head_pages = lax.dynamic_slice_in_dim(head_pages, core_index * page_part, page_part, 1)
    outgoing = head_pages[held_slot[all_groups]]
    incoming = lax.all_to_all(outgoing, "seq", 0, 0, tiled=True)
    both_parts = lax.all_gather(incoming, "tc", axis=0)
    page_source = holder[my_groups]
    window_rows = both_parts[
        lax.iota(jnp.int32, both_parts.shape[0])[None, None, :],
        page_source[:, :, None],
        lax.iota(jnp.int32, DEVICE_REQUESTS)[:, None, None],
    ]
    window_rows = window_rows.reshape(DEVICE_REQUESTS, WINDOW_LENGTH, 2 * HEAD_SIZE)
    starts = jnp.cumsum(lengths) - lengths
    bounds = jnp.concatenate([starts, starts + lengths]).astype(jnp.int32)
    fresh_pad = new_token_rows
    query_pad = jnp.concatenate(
        [query_rows, jnp.zeros_like(query_rows)], axis=-1
    ).transpose(1, 0, 2)
    columns = out_weight.shape[1] // (lax.axis_size("tz") * lax.axis_size("tc"))
    my_columns = lax.dynamic_slice_in_dim(out_weight, tensor_rank_index * columns, columns, 1)
    chunk_rows = row_count // ROW_CHUNKS
    pieces = []
    for chunk in range(ROW_CHUNKS):
        attended = attend(bounds, query_pad, window_rows, fresh_pad, chunk * chunk_rows, chunk_rows)
        all_heads = lax.all_gather(attended, ("tz", "tc"), axis=1, tiled=True)
        pieces.append(jnp.dot(all_heads, my_columns, preferred_element_type=jnp.float32))
    projected = jnp.concatenate(pieces, axis=0)
    return projected.astype(jnp.bfloat16)


BLOCK_ROWS = 64
ROW_CHUNKS = 2


def attend_kernel(first_block, bounds_ref, q_ref, win_ref, fresh_ref, o_ref):
    heads, block_rows, _ = q_ref.shape
    stacked = heads * block_rows
    request_count = win_ref.shape[0]
    window = win_ref.shape[1]
    row_count = fresh_ref.shape[0]
    first_row = (pl.program_id(0) + first_block) * block_rows
    score_scale = HEAD_SIZE ** (-0.5)
    q = q_ref[...].reshape(stacked, 2 * HEAD_SIZE)
    rows = first_row + lax.broadcasted_iota(jnp.int32, (heads, block_rows, 1), 1).reshape(stacked, 1)
    r_first = jnp.int32(0)
    r_last = jnp.int32(-1)
    for k in range(request_count):
        r_first = r_first + (bounds_ref[request_count + k] <= first_row).astype(jnp.int32)
        r_last = r_last + (bounds_ref[k] < first_row + block_rows).astype(jnp.int32)
    r_last = jnp.minimum(r_last, request_count - 1)
    offsets = lax.broadcasted_iota(jnp.int32, (stacked, window), 1)
    column = lax.broadcasted_iota(jnp.int32, (stacked, row_count), 1)
    fresh = fresh_ref[...]

    def one_request(r, out_acc):
        begin = bounds_ref[r]
        finish = bounds_ref[request_count + r]
        in_request = (rows >= begin) & (rows < finish)
        threshold = jnp.where(in_request, rows - begin + 1, window)
        newest = jnp.where(in_request, rows, -1)
        keys = win_ref[r]
        prefix_scores = lax.dot_general(
            q, keys, (((1,), (1,)), ((), ())), preferred_element_type=jnp.float32
        ) * score_scale
        suffix_scores = lax.dot_general(
            q, fresh, (((1,), (1,)), ((), ())), preferred_element_type=jnp.float32
        ) * score_scale
        prefix_mask = offsets >= threshold
        suffix_mask = (
            (column >= begin) & (column <= newest) & (rows - column < WINDOW_LENGTH)
        )
        top = jnp.maximum(
            jnp.max(jnp.where(prefix_mask, prefix_scores, MASKED_SCORE), axis=1, keepdims=True),
            jnp.max(jnp.where(suffix_mask, suffix_scores, MASKED_SCORE), axis=1, keepdims=True),
        )
        prefix_raw = jnp.where(prefix_mask, jnp.exp(prefix_scores - top), 0.0)
        suffix_raw = jnp.where(suffix_mask, jnp.exp(suffix_scores - top), 0.0)
        total = jnp.sum(prefix_raw, axis=1, keepdims=True) + jnp.sum(
            suffix_raw, axis=1, keepdims=True
        )
        weighted = jnp.dot(
            prefix_raw.astype(jnp.bfloat16), keys, preferred_element_type=jnp.float32
        ) + jnp.dot(suffix_raw.astype(jnp.bfloat16), fresh, preferred_element_type=jnp.float32)
        safe_total = jnp.where(in_request, total, 1.0)
        return jnp.where(in_request, weighted / safe_total, out_acc)

    out_acc = lax.fori_loop(
        r_first, r_last + 1, one_request, jnp.zeros((stacked, 2 * HEAD_SIZE), jnp.float32)
    )
    result = out_acc[:, HEAD_SIZE:].astype(o_ref.dtype)
    for h in range(heads):
        o_ref[:, h * HEAD_SIZE : (h + 1) * HEAD_SIZE] = result[h * block_rows : (h + 1) * block_rows]


def attend(bounds, query_pad, window_rows, fresh_rows, first_row, rows):
    heads, row_count, width = query_pad.shape
    block_rows = math.gcd(rows, BLOCK_ROWS)
    first_block = first_row // block_rows
    requests, window, _ = window_rows.shape
    return pl.pallas_call(
        functools.partial(attend_kernel, first_block),
        out_shape=jax.ShapeDtypeStruct((rows, heads * HEAD_SIZE), jnp.bfloat16),
        grid_spec=pltpu.PrefetchScalarGridSpec(
            num_scalar_prefetch=1,
            grid=(rows // block_rows,),
            in_specs=[
                pl.BlockSpec((heads, block_rows, width), lambda i, b: (0, i + first_block, 0)),
                pl.BlockSpec((requests, window, width), lambda i, b: (0, 0, 0)),
                pl.BlockSpec((row_count, width), lambda i, b: (0, 0)),
            ],
            out_specs=pl.BlockSpec((block_rows, heads * HEAD_SIZE), lambda i, b: (i, 0)),
        ),
        compiler_params=pltpu.CompilerParams(
            dimension_semantics=("arbitrary",), vmem_limit_bytes=48 * 1024 * 1024
        ),
    )(bounds, query_pad, window_rows, fresh_rows)


def solution(mesh):
    cores = 2
    seq_size, tensor_size = mesh.devices.shape
    split_mesh = jax.sharding.Mesh(
        mesh.devices.reshape(seq_size, tensor_size // cores, cores), ("seq", "tz", "tc")
    )
    return jax.shard_map(
        body,
        mesh=split_mesh,
        in_specs=(
            P("seq", None),
            P(),
            P(None, ("tz", "tc")),
            P(),
            P(),
            P("seq", None, None, None),
            P(),
            P(),
            P(),
        ),
        out_specs=P("seq", ("tz", "tc")),
        check_vma=False,
    )
```

```python
import math

import jax
import jax.numpy as jnp
from jax import lax
from jax.sharding import PartitionSpec as P
from jax.experimental import pallas as pl
from jax.experimental.pallas import tpu as pltpu

QUERY_HEADS = 32
KEY_VALUE_HEADS = 4
HEAD_SIZE = 64
WINDOW_LENGTH = 2048
DEVICE_REQUESTS = 5
PPG = 64
WP = 16


MASKED_SCORE = -1e30


def normalize(tokens, norm_gain):
    widened = tokens.astype(jnp.float32)
    factor = lax.rsqrt(jnp.mean(widened * widened, axis=-1, keepdims=True) + 1e-05)
    return (widened * factor * norm_gain).astype(jnp.bfloat16)


def row_layout(lengths, row_total_count):
    request_ends = jnp.cumsum(lengths)
    starts = request_ends - lengths
    slot_ids = lax.iota(jnp.int32, row_total_count)
    row_request = jnp.sum((slot_ids[:, None] >= request_ends[None, :]).astype(jnp.int32), axis=1)
    row_live = slot_ids < request_ends[-1]
    choose = row_request[:, None] == lax.iota(jnp.int32, lengths.shape[0])[None, :]
    begins = jnp.sum(jnp.where(choose, starts[None, :], 0), axis=1)
    return (row_request, row_live, slot_ids - begins)


def lookup_rows(table, wanted):
    table_rows = table.shape[0]
    matches = wanted[:, None] == lax.iota(jnp.int32, table_rows)[None, :]
    return jnp.sum(jnp.where(matches[:, :, None], table[None, :, :], 0), axis=1)


def body(
    tokens,
    norm_gain,
    query_weight,
    key_value_matrix,
    out_weight,
    cache_pages,
    page_table,
    request_lengths,
    request_groups,
):
    seq_count = lax.axis_size("seq")
    seq_index = lax.axis_index("seq")
    core_index = lax.axis_index("tc")
    tensor_rank_index = lax.axis_index("tz") * lax.axis_size("tc") + core_index
    row_count = tokens.shape[0]
    resident_heads = query_weight.shape[1] // HEAD_SIZE
    key_value_head = tensor_rank_index * resident_heads // (QUERY_HEADS // KEY_VALUE_HEADS)
    group_count = page_table.shape[0]
    per_owner = WP // seq_count
    pages_here = cache_pages.shape[0]
    score_scale = HEAD_SIZE ** (-0.5)
    normed = normalize(tokens, norm_gain)
    query_rows = jnp.dot(normed, query_weight, preferred_element_type=jnp.float32).astype(
        jnp.bfloat16
    )
    query_rows = query_rows.reshape(row_count, resident_heads, HEAD_SIZE)
    head_weight = lax.dynamic_index_in_dim(key_value_matrix, key_value_head, 1, keepdims=False)
    new_token_rows = jnp.dot(normed, head_weight, preferred_element_type=jnp.float32).astype(
        jnp.bfloat16
    )
    lengths = lax.dynamic_slice_in_dim(
        request_lengths, seq_index * DEVICE_REQUESTS, DEVICE_REQUESTS
    )
    my_groups = lax.dynamic_slice_in_dim(
        request_groups, seq_index * DEVICE_REQUESTS, DEVICE_REQUESTS
    )
    tail_ids = page_table[:, PPG - WP :]
    holder = tail_ids // pages_here
    local_slot = tail_ids % pages_here
    held_slot = jnp.sum(jnp.where(holder == seq_index, local_slot, 0), axis=1)
    all_groups = request_groups.reshape(seq_count, DEVICE_REQUESTS)
    head_pages = lax.dynamic_index_in_dim(cache_pages, key_value_head, 1, keepdims=False)
    page_part = head_pages.shape[1] // lax.axis_size("tc")
    head_pages = lax.dynamic_slice_in_dim(head_pages, core_index * page_part, page_part, 1)
    outgoing = head_pages[held_slot[all_groups]]
    incoming = lax.all_to_all(outgoing, "seq", 0, 0, tiled=True)
    both_parts = lax.all_gather(incoming, "tc", axis=0)
    page_source = holder[my_groups]
    window_rows = both_parts[
        lax.iota(jnp.int32, both_parts.shape[0])[None, None, :],
        page_source[:, :, None],
        lax.iota(jnp.int32, DEVICE_REQUESTS)[:, None, None],
    ]
    window_rows = window_rows.reshape(DEVICE_REQUESTS, WINDOW_LENGTH, 2 * HEAD_SIZE)
    starts = jnp.cumsum(lengths) - lengths
    bounds = jnp.concatenate([starts, starts + lengths]).astype(jnp.int32)
    fresh_pad = new_token_rows
    query_pad = jnp.concatenate(
        [query_rows, jnp.zeros_like(query_rows)], axis=-1
    ).transpose(1, 0, 2)
    attended = attend(bounds, query_pad, window_rows, fresh_pad)
    tensor_count = lax.axis_size("tz") * lax.axis_size("tc")
    columns = out_weight.shape[1] // tensor_count
    block_width = attended.shape[1]
    my_columns = lax.dynamic_slice_in_dim(out_weight, tensor_rank_index * columns, columns, 1)
    projected = jnp.zeros((row_count, columns), jnp.float32)
    for shift in range(tensor_count):
        if shift == 0:
            arrived = attended
        else:
            arrived = lax.ppermute(
                attended,
                ("tz", "tc"),
                [(rank, (rank + shift) % tensor_count) for rank in range(tensor_count)],
            )
        source = (tensor_rank_index - shift) % tensor_count
        source_rows = lax.dynamic_slice_in_dim(my_columns, source * block_width, block_width, 0)
        projected = projected + jnp.dot(arrived, source_rows, preferred_element_type=jnp.float32)
    return projected.astype(jnp.bfloat16)


BLOCK_ROWS = 64


def attend_kernel(bounds_ref, q_ref, win_ref, fresh_ref, o_ref):
    heads, block_rows, _ = q_ref.shape
    stacked = heads * block_rows
    request_count = win_ref.shape[0]
    window = win_ref.shape[1]
    row_count = fresh_ref.shape[0]
    first_row = pl.program_id(0) * block_rows
    score_scale = HEAD_SIZE ** (-0.5)
    q = q_ref[...].reshape(stacked, 2 * HEAD_SIZE)
    rows = first_row + lax.broadcasted_iota(jnp.int32, (heads, block_rows, 1), 1).reshape(stacked, 1)
    r_first = jnp.int32(0)
    r_last = jnp.int32(-1)
    for k in range(request_count):
        r_first = r_first + (bounds_ref[request_count + k] <= first_row).astype(jnp.int32)
        r_last = r_last + (bounds_ref[k] < first_row + block_rows).astype(jnp.int32)
    r_last = jnp.minimum(r_last, request_count - 1)
    offsets = lax.broadcasted_iota(jnp.int32, (stacked, window), 1)
    column = lax.broadcasted_iota(jnp.int32, (stacked, row_count), 1)
    fresh = fresh_ref[...]

    def one_request(r, out_acc):
        begin = bounds_ref[r]
        finish = bounds_ref[request_count + r]
        in_request = (rows >= begin) & (rows < finish)
        threshold = jnp.where(in_request, rows - begin + 1, window)
        newest = jnp.where(in_request, rows, -1)
        keys = win_ref[r]
        prefix_scores = lax.dot_general(
            q, keys, (((1,), (1,)), ((), ())), preferred_element_type=jnp.float32
        ) * score_scale
        suffix_scores = lax.dot_general(
            q, fresh, (((1,), (1,)), ((), ())), preferred_element_type=jnp.float32
        ) * score_scale
        prefix_mask = offsets >= threshold
        suffix_mask = (
            (column >= begin) & (column <= newest) & (rows - column < WINDOW_LENGTH)
        )
        top = jnp.maximum(
            jnp.max(jnp.where(prefix_mask, prefix_scores, MASKED_SCORE), axis=1, keepdims=True),
            jnp.max(jnp.where(suffix_mask, suffix_scores, MASKED_SCORE), axis=1, keepdims=True),
        )
        prefix_raw = jnp.where(prefix_mask, jnp.exp(prefix_scores - top), 0.0)
        suffix_raw = jnp.where(suffix_mask, jnp.exp(suffix_scores - top), 0.0)
        total = jnp.sum(prefix_raw, axis=1, keepdims=True) + jnp.sum(
            suffix_raw, axis=1, keepdims=True
        )
        weighted = jnp.dot(
            prefix_raw.astype(jnp.bfloat16), keys, preferred_element_type=jnp.float32
        ) + jnp.dot(suffix_raw.astype(jnp.bfloat16), fresh, preferred_element_type=jnp.float32)
        safe_total = jnp.where(in_request, total, 1.0)
        return jnp.where(in_request, weighted / safe_total, out_acc)

    out_acc = lax.fori_loop(
        r_first, r_last + 1, one_request, jnp.zeros((stacked, 2 * HEAD_SIZE), jnp.float32)
    )
    result = out_acc[:, HEAD_SIZE:].astype(o_ref.dtype)
    for h in range(heads):
        o_ref[:, h * HEAD_SIZE : (h + 1) * HEAD_SIZE] = result[h * block_rows : (h + 1) * block_rows]


def attend(bounds, query_pad, window_rows, fresh_rows):
    heads, row_count, width = query_pad.shape
    block_rows = math.gcd(row_count, BLOCK_ROWS)
    requests, window, _ = window_rows.shape
    return pl.pallas_call(
        attend_kernel,
        out_shape=jax.ShapeDtypeStruct((row_count, heads * HEAD_SIZE), jnp.bfloat16),
        grid_spec=pltpu.PrefetchScalarGridSpec(
            num_scalar_prefetch=1,
            grid=(row_count // block_rows,),
            in_specs=[
                pl.BlockSpec((heads, block_rows, width), lambda i, b: (0, i, 0)),
                pl.BlockSpec((requests, window, width), lambda i, b: (0, 0, 0)),
                pl.BlockSpec((row_count, width), lambda i, b: (0, 0)),
            ],
            out_specs=pl.BlockSpec((block_rows, heads * HEAD_SIZE), lambda i, b: (i, 0)),
        ),
        compiler_params=pltpu.CompilerParams(
            dimension_semantics=("arbitrary",), vmem_limit_bytes=48 * 1024 * 1024
        ),
    )(bounds, query_pad, window_rows, fresh_rows)


def solution(mesh):
    cores = 2
    seq_size, tensor_size = mesh.devices.shape
    split_mesh = jax.sharding.Mesh(
        mesh.devices.reshape(seq_size, tensor_size // cores, cores), ("seq", "tz", "tc")
    )
    return jax.shard_map(
        body,
        mesh=split_mesh,
        in_specs=(
            P("seq", None),
            P(),
            P(None, ("tz", "tc")),
            P(),
            P(),
            P("seq", None, None, None),
            P(),
            P(),
            P(),
        ),
        out_specs=P("seq", ("tz", "tc")),
        check_vma=False,
    )
```

```python
import math

import jax
import jax.numpy as jnp
from jax import lax
from jax.sharding import PartitionSpec as P
from jax.experimental import pallas as pl
from jax.experimental.pallas import tpu as pltpu

QUERY_HEADS = 32
KEY_VALUE_HEADS = 4
HEAD_SIZE = 64
WINDOW_LENGTH = 2048
DEVICE_REQUESTS = 5
PPG = 64
WP = 16


MASKED_SCORE = -1e30


def normalize(tokens, norm_gain):
    widened = tokens.astype(jnp.float32)
    factor = lax.rsqrt(jnp.mean(widened * widened, axis=-1, keepdims=True) + 1e-05)
    return (widened * factor * norm_gain).astype(jnp.bfloat16)


def layer(
    tokens,
    norm_gain,
    query_weight,
    key_value_matrix,
    out_weight,
    cache_pages,
    page_table,
    request_lengths,
    request_groups,
):
    seq_count = lax.axis_size("seq")
    seq_index = lax.axis_index("seq")
    core_index = lax.axis_index("tc")
    tensor_rank_index = lax.axis_index("tz") * lax.axis_size("tc") + core_index
    row_count = tokens.shape[0]
    resident_heads = query_weight.shape[1] // HEAD_SIZE
    key_value_head = tensor_rank_index * resident_heads // (QUERY_HEADS // KEY_VALUE_HEADS)
    pages_here = cache_pages.shape[0]
    normed = normalize(tokens, norm_gain)
    query_rows = jnp.dot(normed, query_weight, preferred_element_type=jnp.float32).astype(
        jnp.bfloat16
    )
    query_rows = query_rows.reshape(row_count, resident_heads, HEAD_SIZE)
    head_weight = lax.dynamic_index_in_dim(key_value_matrix, key_value_head, 1, keepdims=False)
    new_token_rows = jnp.dot(normed, head_weight, preferred_element_type=jnp.float32).astype(
        jnp.bfloat16
    )
    lengths = lax.dynamic_slice_in_dim(
        request_lengths, seq_index * DEVICE_REQUESTS, DEVICE_REQUESTS
    )
    my_groups = lax.dynamic_slice_in_dim(
        request_groups, seq_index * DEVICE_REQUESTS, DEVICE_REQUESTS
    )
    tail_ids = page_table[:, PPG - WP :]
    holder = tail_ids // pages_here
    local_slot = tail_ids % pages_here
    held_slot = jnp.sum(jnp.where(holder == seq_index, local_slot, 0), axis=1)
    all_groups = request_groups.reshape(seq_count, DEVICE_REQUESTS)
    head_pages = lax.dynamic_index_in_dim(cache_pages, key_value_head, 1, keepdims=False)
    page_part = head_pages.shape[1] // lax.axis_size("tc")
    head_pages = lax.dynamic_slice_in_dim(head_pages, core_index * page_part, page_part, 1)
    outgoing = head_pages[held_slot[all_groups]]
    incoming = lax.all_to_all(outgoing, "seq", 0, 0, tiled=True)
    both_parts = lax.all_gather(incoming, "tc", axis=0)
    page_source = holder[my_groups]
    window_rows = both_parts[
        lax.iota(jnp.int32, both_parts.shape[0])[None, None, :],
        page_source[:, :, None],
        lax.iota(jnp.int32, DEVICE_REQUESTS)[:, None, None],
    ]
    window_rows = window_rows.reshape(DEVICE_REQUESTS, WINDOW_LENGTH, 2 * HEAD_SIZE)
    starts = jnp.cumsum(lengths) - lengths
    bounds = jnp.concatenate([starts, starts + lengths]).astype(jnp.int32)
    fresh_pad = new_token_rows
    query_pad = jnp.concatenate(
        [query_rows, jnp.zeros_like(query_rows)], axis=-1
    ).transpose(1, 0, 2)
    attended = attend(bounds, query_pad, window_rows, fresh_pad)
    all_heads = lax.all_gather(attended, ("tz", "tc"), axis=1, tiled=True)
    columns = out_weight.shape[1] // (lax.axis_size("tz") * lax.axis_size("tc"))
    my_columns = lax.dynamic_slice_in_dim(out_weight, tensor_rank_index * columns, columns, 1)
    projected = jnp.dot(all_heads, my_columns, preferred_element_type=jnp.float32)
    return projected.astype(jnp.bfloat16)


BLOCK_ROWS = 64


def attend_kernel(bounds_ref, q_ref, win_ref, fresh_ref, o_ref):
    heads, block_rows, _ = q_ref.shape
    stacked = heads * block_rows
    request_count = win_ref.shape[0]
    window = win_ref.shape[1]
    row_count = fresh_ref.shape[0]
    first_row = pl.program_id(0) * block_rows
    score_scale = HEAD_SIZE ** (-0.5)
    q = q_ref[...].reshape(stacked, 2 * HEAD_SIZE)
    rows = first_row + lax.broadcasted_iota(jnp.int32, (heads, block_rows, 1), 1).reshape(stacked, 1)
    r_first = jnp.int32(0)
    r_last = jnp.int32(-1)
    for k in range(request_count):
        r_first = r_first + (bounds_ref[request_count + k] <= first_row).astype(jnp.int32)
        r_last = r_last + (bounds_ref[k] < first_row + block_rows).astype(jnp.int32)
    r_last = jnp.minimum(r_last, request_count - 1)
    offsets = lax.broadcasted_iota(jnp.int32, (stacked, window), 1)
    column = lax.broadcasted_iota(jnp.int32, (stacked, row_count), 1)
    fresh = fresh_ref[...]

    def one_request(r, out_acc):
        begin = bounds_ref[r]
        finish = bounds_ref[request_count + r]
        in_request = (rows >= begin) & (rows < finish)
        threshold = jnp.where(in_request, rows - begin + 1, window)
        newest = jnp.where(in_request, rows, -1)
        keys = win_ref[r]
        prefix_scores = lax.dot_general(
            q, keys, (((1,), (1,)), ((), ())), preferred_element_type=jnp.float32
        ) * score_scale
        suffix_scores = lax.dot_general(
            q, fresh, (((1,), (1,)), ((), ())), preferred_element_type=jnp.float32
        ) * score_scale
        prefix_mask = offsets >= threshold
        suffix_mask = (
            (column >= begin) & (column <= newest) & (rows - column < WINDOW_LENGTH)
        )
        top = jnp.maximum(
            jnp.max(jnp.where(prefix_mask, prefix_scores, MASKED_SCORE), axis=1, keepdims=True),
            jnp.max(jnp.where(suffix_mask, suffix_scores, MASKED_SCORE), axis=1, keepdims=True),
        )
        prefix_raw = jnp.where(prefix_mask, jnp.exp(prefix_scores - top), 0.0)
        suffix_raw = jnp.where(suffix_mask, jnp.exp(suffix_scores - top), 0.0)
        total = jnp.sum(prefix_raw, axis=1, keepdims=True) + jnp.sum(
            suffix_raw, axis=1, keepdims=True
        )
        weighted = jnp.dot(
            prefix_raw.astype(jnp.bfloat16), keys, preferred_element_type=jnp.float32
        ) + jnp.dot(suffix_raw.astype(jnp.bfloat16), fresh, preferred_element_type=jnp.float32)
        safe_total = jnp.where(in_request, total, 1.0)
        return jnp.where(in_request, weighted / safe_total, out_acc)

    out_acc = lax.fori_loop(
        r_first, r_last + 1, one_request, jnp.zeros((stacked, 2 * HEAD_SIZE), jnp.float32)
    )
    result = out_acc[:, HEAD_SIZE:].astype(o_ref.dtype)
    for h in range(heads):
        o_ref[:, h * HEAD_SIZE : (h + 1) * HEAD_SIZE] = result[h * block_rows : (h + 1) * block_rows]


def attend(bounds, query_pad, window_rows, fresh_rows):
    heads, row_count, width = query_pad.shape
    block_rows = math.gcd(row_count, BLOCK_ROWS)
    requests, window, _ = window_rows.shape
    return pl.pallas_call(
        attend_kernel,
        out_shape=jax.ShapeDtypeStruct((row_count, heads * HEAD_SIZE), jnp.bfloat16),
        grid_spec=pltpu.PrefetchScalarGridSpec(
            num_scalar_prefetch=1,
            grid=(row_count // block_rows,),
            in_specs=[
                pl.BlockSpec((heads, block_rows, width), lambda i, b: (0, i, 0)),
                pl.BlockSpec((requests, window, width), lambda i, b: (0, 0, 0)),
                pl.BlockSpec((row_count, width), lambda i, b: (0, 0)),
            ],
            out_specs=pl.BlockSpec((block_rows, heads * HEAD_SIZE), lambda i, b: (i, 0)),
        ),
        compiler_params=pltpu.CompilerParams(
            dimension_semantics=("arbitrary",), vmem_limit_bytes=48 * 1024 * 1024
        ),
    )(bounds, query_pad, window_rows, fresh_rows)


def solution(mesh):
    cores = 2
    seq_size, tensor_size = mesh.devices.shape
    split_mesh = jax.sharding.Mesh(
        mesh.devices.reshape(seq_size, tensor_size // cores, cores), ("seq", "tz", "tc")
    )
    return jax.shard_map(
        layer,
        mesh=split_mesh,
        in_specs=(
            P("seq", None),
            P(),
            P(None, ("tz", "tc")),
            P(),
            P(),
            P("seq", None, None, None),
            P(),
            P(),
            P(),
        ),
        out_specs=P("seq", ("tz", "tc")),
        check_vma=False,
    )
```

```python
import math

import jax
import jax.numpy as jnp
from jax import lax
from jax.sharding import PartitionSpec as P
from jax.experimental import pallas as pl
from jax.experimental.pallas import tpu as pltpu

QUERY_HEADS = 32
KEY_VALUE_HEADS = 4
HEAD_SIZE = 64
WINDOW_LENGTH = 2048
DEVICE_REQUESTS = 5
PPG = 64
WP = 16


MASKED_SCORE = -1e30


def normalize(tokens, norm_gain):
    widened = tokens.astype(jnp.float32)
    factor = lax.rsqrt(jnp.mean(widened * widened, axis=-1, keepdims=True) + 1e-05)
    return (widened * factor * norm_gain).astype(jnp.bfloat16)


def layer(
    tokens,
    norm_gain,
    query_weight,
    key_value_matrix,
    out_weight,
    cache_pages,
    page_table,
    request_lengths,
    request_groups,
):
    seq_count = lax.axis_size("seq")
    seq_index = lax.axis_index("seq")
    core_index = lax.axis_index("tc")
    tensor_rank_index = lax.axis_index("tz") * lax.axis_size("tc") + core_index
    row_count = tokens.shape[0]
    resident_heads = query_weight.shape[1] // HEAD_SIZE
    key_value_head = tensor_rank_index * resident_heads // (QUERY_HEADS // KEY_VALUE_HEADS)
    pages_here = cache_pages.shape[0]
    normed = normalize(tokens, norm_gain)
    query_rows = jnp.dot(normed, query_weight, preferred_element_type=jnp.float32).astype(
        jnp.bfloat16
    )
    query_rows = query_rows.reshape(row_count, resident_heads, HEAD_SIZE)
    head_weight = lax.dynamic_index_in_dim(key_value_matrix, key_value_head, 1, keepdims=False)
    new_token_rows = jnp.dot(normed, head_weight, preferred_element_type=jnp.float32).astype(
        jnp.bfloat16
    )
    lengths = lax.dynamic_slice_in_dim(
        request_lengths, seq_index * DEVICE_REQUESTS, DEVICE_REQUESTS
    )
    my_groups = lax.dynamic_slice_in_dim(
        request_groups, seq_index * DEVICE_REQUESTS, DEVICE_REQUESTS
    )
    tail_ids = page_table[:, PPG - WP :]
    holder = tail_ids // pages_here
    local_slot = tail_ids % pages_here
    held_slot = jnp.sum(jnp.where(holder == seq_index, local_slot, 0), axis=1)
    all_groups = request_groups.reshape(seq_count, DEVICE_REQUESTS)
    head_pages = lax.dynamic_index_in_dim(cache_pages, key_value_head, 1, keepdims=False)
    page_part = head_pages.shape[1] // lax.axis_size("tc")
    head_pages = lax.dynamic_slice_in_dim(head_pages, core_index * page_part, page_part, 1)
    outgoing = head_pages[held_slot[all_groups]]
    incoming = lax.all_to_all(outgoing, "seq", 0, 0, tiled=True)
    core_count = lax.axis_size("tc")
    partner = lax.ppermute(incoming, "tc", [(0, 1), (1, 0)])
    both_parts = jnp.stack([incoming, partner])
    page_source = holder[my_groups]
    window_rows = both_parts[
        ((lax.iota(jnp.int32, core_count) + core_index) % core_count)[None, None, :],
        page_source[:, :, None],
        lax.iota(jnp.int32, DEVICE_REQUESTS)[:, None, None],
    ]
    window_rows = window_rows.reshape(DEVICE_REQUESTS, WINDOW_LENGTH, 2 * HEAD_SIZE)
    starts = jnp.cumsum(lengths) - lengths
    bounds = jnp.concatenate([starts, starts + lengths]).astype(jnp.int32)
    fresh_pad = new_token_rows
    query_pad = jnp.concatenate(
        [query_rows, jnp.zeros_like(query_rows)], axis=-1
    ).transpose(1, 0, 2)
    attended = attend(bounds, query_pad, window_rows, fresh_pad)
    all_heads = lax.all_gather(attended, ("tz", "tc"), axis=1, tiled=True)
    columns = out_weight.shape[1] // (lax.axis_size("tz") * lax.axis_size("tc"))
    my_columns = lax.dynamic_slice_in_dim(out_weight, tensor_rank_index * columns, columns, 1)
    projected = jnp.dot(all_heads, my_columns, preferred_element_type=jnp.float32)
    return projected.astype(jnp.bfloat16)


BLOCK_ROWS = 32


def attend_kernel(bounds_ref, q_ref, win_ref, fresh_ref, o_ref):
    heads, block_rows, _ = q_ref.shape
    stacked = heads * block_rows
    request_count = win_ref.shape[0]
    window = win_ref.shape[1]
    row_count = fresh_ref.shape[0]
    first_row = pl.program_id(0) * block_rows
    score_scale = HEAD_SIZE ** (-0.5)
    q = q_ref[...].reshape(stacked, 2 * HEAD_SIZE)
    rows = first_row + lax.broadcasted_iota(jnp.int32, (heads, block_rows, 1), 1).reshape(stacked, 1)
    r_first = jnp.int32(0)
    r_last = jnp.int32(-1)
    for k in range(request_count):
        r_first = r_first + (bounds_ref[request_count + k] <= first_row).astype(jnp.int32)
        r_last = r_last + (bounds_ref[k] < first_row + block_rows).astype(jnp.int32)
    r_last = jnp.minimum(r_last, request_count - 1)
    offsets = lax.broadcasted_iota(jnp.int32, (stacked, window), 1)
    column = lax.broadcasted_iota(jnp.int32, (stacked, row_count), 1)
    fresh = fresh_ref[...]

    def one_request(r, out_acc):
        begin = bounds_ref[r]
        finish = bounds_ref[request_count + r]
        in_request = (rows >= begin) & (rows < finish)
        threshold = jnp.where(in_request, rows - begin + 1, window)
        newest = jnp.where(in_request, rows, -1)
        keys = win_ref[r]
        prefix_scores = lax.dot_general(
            q, keys, (((1,), (1,)), ((), ())), preferred_element_type=jnp.float32
        ) * score_scale
        suffix_scores = lax.dot_general(
            q, fresh, (((1,), (1,)), ((), ())), preferred_element_type=jnp.float32
        ) * score_scale
        prefix_mask = offsets >= threshold
        suffix_mask = (
            (column >= begin) & (column <= newest) & (rows - column < WINDOW_LENGTH)
        )
        top = jnp.maximum(
            jnp.max(jnp.where(prefix_mask, prefix_scores, MASKED_SCORE), axis=1, keepdims=True),
            jnp.max(jnp.where(suffix_mask, suffix_scores, MASKED_SCORE), axis=1, keepdims=True),
        )
        prefix_raw = jnp.where(prefix_mask, jnp.exp(prefix_scores - top), 0.0)
        suffix_raw = jnp.where(suffix_mask, jnp.exp(suffix_scores - top), 0.0)
        total = jnp.sum(prefix_raw, axis=1, keepdims=True) + jnp.sum(
            suffix_raw, axis=1, keepdims=True
        )
        weighted = jnp.dot(
            prefix_raw.astype(jnp.bfloat16), keys, preferred_element_type=jnp.float32
        ) + jnp.dot(suffix_raw.astype(jnp.bfloat16), fresh, preferred_element_type=jnp.float32)
        safe_total = jnp.where(in_request, total, 1.0)
        return jnp.where(in_request, weighted / safe_total, out_acc)

    out_acc = lax.fori_loop(
        r_first, r_last + 1, one_request, jnp.zeros((stacked, 2 * HEAD_SIZE), jnp.float32)
    )
    result = out_acc[:, HEAD_SIZE:].astype(o_ref.dtype)
    for h in range(heads):
        o_ref[:, h * HEAD_SIZE : (h + 1) * HEAD_SIZE] = result[h * block_rows : (h + 1) * block_rows]


def attend(bounds, query_pad, window_rows, fresh_rows):
    heads, row_count, width = query_pad.shape
    block_rows = math.gcd(row_count, BLOCK_ROWS)
    requests, window, _ = window_rows.shape
    return pl.pallas_call(
        attend_kernel,
        out_shape=jax.ShapeDtypeStruct((row_count, heads * HEAD_SIZE), jnp.bfloat16),
        grid_spec=pltpu.PrefetchScalarGridSpec(
            num_scalar_prefetch=1,
            grid=(row_count // block_rows,),
            in_specs=[
                pl.BlockSpec((heads, block_rows, width), lambda i, b: (0, i, 0)),
                pl.BlockSpec((requests, window, width), lambda i, b: (0, 0, 0)),
                pl.BlockSpec((row_count, width), lambda i, b: (0, 0)),
            ],
            out_specs=pl.BlockSpec((block_rows, heads * HEAD_SIZE), lambda i, b: (i, 0)),
        ),
        compiler_params=pltpu.CompilerParams(
            dimension_semantics=("arbitrary",), vmem_limit_bytes=48 * 1024 * 1024
        ),
    )(bounds, query_pad, window_rows, fresh_rows)


def solution(mesh):
    cores = 2
    seq_size, tensor_size = mesh.devices.shape
    split_mesh = jax.sharding.Mesh(
        mesh.devices.reshape(seq_size, tensor_size // cores, cores), ("seq", "tz", "tc")
    )
    return jax.shard_map(
        layer,
        mesh=split_mesh,
        in_specs=(
            P("seq", None),
            P(),
            P(None, ("tz", "tc")),
            P(),
            P(),
            P("seq", None, None, None),
            P(),
            P(),
            P(),
        ),
        out_specs=P("seq", ("tz", "tc")),
        check_vma=False,
    )
```

```python
import math

import jax
import jax.numpy as jnp
from jax import lax
from jax.sharding import PartitionSpec as P
from jax.experimental import pallas as pl
from jax.experimental.pallas import tpu as pltpu

QUERY_HEADS = 32
KEY_VALUE_HEADS = 4
HEAD_SIZE = 64
WINDOW_LENGTH = 2048
DEVICE_REQUESTS = 5
PPG = 64
WP = 16


MASKED_SCORE = -1e30


def normalize(tokens, norm_gain):
    widened = tokens.astype(jnp.float32)
    factor = lax.rsqrt(jnp.mean(widened * widened, axis=-1, keepdims=True) + 1e-05)
    return (widened * factor * norm_gain).astype(jnp.bfloat16)


def layer(
    tokens,
    norm_gain,
    query_weight,
    key_value_matrix,
    out_weight,
    cache_pages,
    page_table,
    request_lengths,
    request_groups,
):
    seq_count = lax.axis_size("seq")
    seq_index = lax.axis_index("seq")
    core_index = lax.axis_index("tc")
    tensor_rank_index = lax.axis_index("tz") * lax.axis_size("tc") + core_index
    row_count = tokens.shape[0]
    resident_heads = query_weight.shape[1] // HEAD_SIZE
    key_value_head = tensor_rank_index * resident_heads // (QUERY_HEADS // KEY_VALUE_HEADS)
    pages_here = cache_pages.shape[0]
    normed = normalize(tokens, norm_gain)
    query_rows = jnp.dot(normed, query_weight, preferred_element_type=jnp.float32).astype(
        jnp.bfloat16
    )
    query_rows = query_rows.reshape(row_count, resident_heads, HEAD_SIZE)
    head_weight = lax.dynamic_index_in_dim(key_value_matrix, key_value_head, 1, keepdims=False)
    new_token_rows = jnp.dot(normed, head_weight, preferred_element_type=jnp.float32).astype(
        jnp.bfloat16
    )
    lengths = lax.dynamic_slice_in_dim(
        request_lengths, seq_index * DEVICE_REQUESTS, DEVICE_REQUESTS
    )
    my_groups = lax.dynamic_slice_in_dim(
        request_groups, seq_index * DEVICE_REQUESTS, DEVICE_REQUESTS
    )
    tail_ids = page_table[:, PPG - WP :]
    holder = tail_ids // pages_here
    local_slot = tail_ids % pages_here
    held_slot = jnp.sum(jnp.where(holder == seq_index, local_slot, 0), axis=1)
    all_groups = request_groups.reshape(seq_count, DEVICE_REQUESTS)
    head_pages = lax.dynamic_index_in_dim(cache_pages, key_value_head, 1, keepdims=False)
    page_part = head_pages.shape[1] // lax.axis_size("tc")
    head_pages = lax.dynamic_slice_in_dim(head_pages, core_index * page_part, page_part, 1)
    outgoing = head_pages[held_slot[all_groups]]
    incoming = lax.all_to_all(outgoing, "seq", 0, 0, tiled=True)
    core_count = lax.axis_size("tc")
    partner = lax.ppermute(incoming, "tc", [(0, 1), (1, 0)])
    both_parts = jnp.stack([incoming, partner])
    page_source = holder[my_groups]
    window_rows = both_parts[
        ((lax.iota(jnp.int32, core_count) + core_index) % core_count)[None, None, :],
        page_source[:, :, None],
        lax.iota(jnp.int32, DEVICE_REQUESTS)[:, None, None],
    ]
    window_rows = window_rows.reshape(DEVICE_REQUESTS, WINDOW_LENGTH, 2 * HEAD_SIZE)
    starts = jnp.cumsum(lengths) - lengths
    bounds = jnp.concatenate([starts, starts + lengths]).astype(jnp.int32)
    fresh_pad = new_token_rows
    query_pad = jnp.concatenate(
        [query_rows, jnp.zeros_like(query_rows)], axis=-1
    ).transpose(1, 0, 2)
    attended = attend(bounds, query_pad, window_rows, fresh_pad)
    swap = [(0, 1), (1, 0)]
    z_count = lax.axis_size("tz")
    z_index = lax.axis_index("tz")
    partner_heads = lax.ppermute(attended, "tc", swap)
    first_core = core_index == 0
    chip_heads = jnp.where(
        first_core,
        jnp.concatenate([attended, partner_heads], axis=1),
        jnp.concatenate([partner_heads, attended], axis=1),
    )
    half_rows = row_count // core_count
    my_half = lax.dynamic_slice_in_dim(chip_heads, core_index * half_rows, half_rows, 0)
    sent = jnp.broadcast_to(my_half[None], (z_count,) + my_half.shape)
    chips_heads = lax.all_to_all(sent, "tz", 0, 0, tiled=True)
    chip_width = out_weight.shape[1] // z_count
    chip_columns = lax.dynamic_slice_in_dim(out_weight, z_index * chip_width, chip_width, 1)
    chip_columns = chip_columns.reshape(z_count, my_half.shape[1], chip_width)
    half_out = jnp.einsum(
        "zrj,zjn->rn", chips_heads, chip_columns, preferred_element_type=jnp.float32
    ).astype(jnp.bfloat16)
    columns = chip_width // core_count
    keep = lax.dynamic_slice_in_dim(half_out, core_index * columns, columns, 1)
    give = lax.dynamic_slice_in_dim(half_out, (1 - core_index) * columns, columns, 1)
    got = lax.ppermute(give, "tc", swap)
    projected = jnp.where(
        first_core, jnp.concatenate([keep, got], axis=0), jnp.concatenate([got, keep], axis=0)
    )
    return projected


BLOCK_ROWS = 64


def attend_kernel(bounds_ref, q_ref, win_ref, fresh_ref, o_ref):
    heads, block_rows, _ = q_ref.shape
    stacked = heads * block_rows
    request_count = win_ref.shape[0]
    window = win_ref.shape[1]
    row_count = fresh_ref.shape[0]
    first_row = pl.program_id(0) * block_rows
    score_scale = HEAD_SIZE ** (-0.5)
    q = q_ref[...].reshape(stacked, 2 * HEAD_SIZE)
    rows = first_row + lax.broadcasted_iota(jnp.int32, (heads, block_rows, 1), 1).reshape(stacked, 1)
    r_first = jnp.int32(0)
    r_last = jnp.int32(-1)
    for k in range(request_count):
        r_first = r_first + (bounds_ref[request_count + k] <= first_row).astype(jnp.int32)
        r_last = r_last + (bounds_ref[k] < first_row + block_rows).astype(jnp.int32)
    r_last = jnp.minimum(r_last, request_count - 1)
    offsets = lax.broadcasted_iota(jnp.int32, (stacked, window), 1)
    column = lax.broadcasted_iota(jnp.int32, (stacked, row_count), 1)
    fresh = fresh_ref[...]

    def one_request(r, out_acc):
        begin = bounds_ref[r]
        finish = bounds_ref[request_count + r]
        in_request = (rows >= begin) & (rows < finish)
        threshold = jnp.where(in_request, rows - begin + 1, window)
        newest = jnp.where(in_request, rows, -1)
        keys = win_ref[r]
        prefix_scores = lax.dot_general(
            q, keys, (((1,), (1,)), ((), ())), preferred_element_type=jnp.float32
        ) * score_scale
        suffix_scores = lax.dot_general(
            q, fresh, (((1,), (1,)), ((), ())), preferred_element_type=jnp.float32
        ) * score_scale
        prefix_mask = offsets >= threshold
        suffix_mask = (
            (column >= begin) & (column <= newest) & (rows - column < WINDOW_LENGTH)
        )
        top = jnp.maximum(
            jnp.max(jnp.where(prefix_mask, prefix_scores, MASKED_SCORE), axis=1, keepdims=True),
            jnp.max(jnp.where(suffix_mask, suffix_scores, MASKED_SCORE), axis=1, keepdims=True),
        )
        prefix_raw = jnp.where(prefix_mask, jnp.exp(prefix_scores - top), 0.0)
        suffix_raw = jnp.where(suffix_mask, jnp.exp(suffix_scores - top), 0.0)
        total = jnp.sum(prefix_raw, axis=1, keepdims=True) + jnp.sum(
            suffix_raw, axis=1, keepdims=True
        )
        weighted = jnp.dot(
            prefix_raw.astype(jnp.bfloat16), keys, preferred_element_type=jnp.float32
        ) + jnp.dot(suffix_raw.astype(jnp.bfloat16), fresh, preferred_element_type=jnp.float32)
        safe_total = jnp.where(in_request, total, 1.0)
        return jnp.where(in_request, weighted / safe_total, out_acc)

    out_acc = lax.fori_loop(
        r_first, r_last + 1, one_request, jnp.zeros((stacked, 2 * HEAD_SIZE), jnp.float32)
    )
    result = out_acc[:, HEAD_SIZE:].astype(o_ref.dtype)
    for h in range(heads):
        o_ref[:, h * HEAD_SIZE : (h + 1) * HEAD_SIZE] = result[h * block_rows : (h + 1) * block_rows]


def attend(bounds, query_pad, window_rows, fresh_rows):
    heads, row_count, width = query_pad.shape
    block_rows = math.gcd(row_count, BLOCK_ROWS)
    requests, window, _ = window_rows.shape
    return pl.pallas_call(
        attend_kernel,
        out_shape=jax.ShapeDtypeStruct((row_count, heads * HEAD_SIZE), jnp.bfloat16),
        grid_spec=pltpu.PrefetchScalarGridSpec(
            num_scalar_prefetch=1,
            grid=(row_count // block_rows,),
            in_specs=[
                pl.BlockSpec((heads, block_rows, width), lambda i, b: (0, i, 0)),
                pl.BlockSpec((requests, window, width), lambda i, b: (0, 0, 0)),
                pl.BlockSpec((row_count, width), lambda i, b: (0, 0)),
            ],
            out_specs=pl.BlockSpec((block_rows, heads * HEAD_SIZE), lambda i, b: (i, 0)),
        ),
        compiler_params=pltpu.CompilerParams(
            dimension_semantics=("arbitrary",), vmem_limit_bytes=48 * 1024 * 1024
        ),
    )(bounds, query_pad, window_rows, fresh_rows)


def solution(mesh):
    cores = 2
    seq_size, tensor_size = mesh.devices.shape
    split_mesh = jax.sharding.Mesh(
        mesh.devices.reshape(seq_size, tensor_size // cores, cores), ("seq", "tz", "tc")
    )
    return jax.shard_map(
        layer,
        mesh=split_mesh,
        in_specs=(
            P("seq", None),
            P(),
            P(None, ("tz", "tc")),
            P(),
            P(),
            P("seq", None, None, None),
            P(),
            P(),
            P(),
        ),
        out_specs=P("seq", ("tz", "tc")),
        check_vma=False,
    )
```

```python
import functools
import math

import jax
import jax.numpy as jnp
from jax import lax
from jax.sharding import PartitionSpec as P
from jax.experimental import pallas as pl
from jax.experimental.pallas import tpu as pltpu

QUERY_HEADS = 32
KEY_VALUE_HEADS = 4
HEAD_SIZE = 64
WINDOW_LENGTH = 2048
DEVICE_REQUESTS = 5
PPG = 64
WP = 16


MASKED_SCORE = -1e30


def normalize(tokens, norm_gain):
    widened = tokens.astype(jnp.float32)
    factor = lax.rsqrt(jnp.mean(widened * widened, axis=-1, keepdims=True) + 1e-05)
    return (widened * factor * norm_gain).astype(jnp.bfloat16)


def layer(
    tokens,
    norm_gain,
    query_weight,
    key_value_matrix,
    out_weight,
    cache_pages,
    page_table,
    request_lengths,
    request_groups,
):
    seq_count = lax.axis_size("seq")
    seq_index = lax.axis_index("seq")
    core_index = lax.axis_index("tc")
    tensor_rank_index = lax.axis_index("tz") * lax.axis_size("tc") + core_index
    row_count = tokens.shape[0]
    resident_heads = query_weight.shape[1] // HEAD_SIZE
    key_value_head = tensor_rank_index * resident_heads // (QUERY_HEADS // KEY_VALUE_HEADS)
    pages_here = cache_pages.shape[0]
    normed = normalize(tokens, norm_gain)
    query_rows = jnp.dot(normed, query_weight, preferred_element_type=jnp.float32).astype(
        jnp.bfloat16
    )
    query_rows = query_rows.reshape(row_count, resident_heads, HEAD_SIZE)
    head_weight = lax.dynamic_index_in_dim(key_value_matrix, key_value_head, 1, keepdims=False)
    new_token_rows = jnp.dot(normed, head_weight, preferred_element_type=jnp.float32).astype(
        jnp.bfloat16
    )
    lengths = lax.dynamic_slice_in_dim(
        request_lengths, seq_index * DEVICE_REQUESTS, DEVICE_REQUESTS
    )
    my_groups = lax.dynamic_slice_in_dim(
        request_groups, seq_index * DEVICE_REQUESTS, DEVICE_REQUESTS
    )
    tail_ids = page_table[:, PPG - WP :]
    holder = tail_ids // pages_here
    local_slot = tail_ids % pages_here
    held_slot = jnp.sum(jnp.where(holder == seq_index, local_slot, 0), axis=1)
    all_groups = request_groups.reshape(seq_count, DEVICE_REQUESTS)
    head_pages = lax.dynamic_index_in_dim(cache_pages, key_value_head, 1, keepdims=False)
    page_part = head_pages.shape[1] // lax.axis_size("tc")
    head_pages = lax.dynamic_slice_in_dim(head_pages, core_index * page_part, page_part, 1)
    outgoing = head_pages[held_slot[all_groups].T]
    incoming = lax.all_to_all(outgoing, "seq", 1, 1, tiled=True)
    core_count = lax.axis_size("tc")
    partner = lax.ppermute(incoming, "tc", [(0, 1), (1, 0)])
    source_ids = lax.iota(jnp.int32, seq_count)
    page_order = jnp.sum(
        jnp.where(
            holder[:, :, None] == source_ids[None, None, :],
            lax.iota(jnp.int32, holder.shape[1])[None, :, None],
            0,
        ),
        axis=1,
    )
    page_start = page_order[my_groups][:, :, None] * (page_part * core_count)
    within = lax.iota(jnp.int32, page_part)[None, None, :]
    key_parts = []
    for part, half in ((incoming, core_index), (partner, (core_index + 1) % core_count)):
        positions = (page_start + half * page_part + within).reshape(DEVICE_REQUESTS, 1, -1)
        keys = part.reshape(DEVICE_REQUESTS, -1, 2 * HEAD_SIZE)
        key_parts.append((keys, positions))
    starts = jnp.cumsum(lengths) - lengths
    bounds = jnp.concatenate([starts, starts + lengths]).astype(jnp.int32)
    fresh_pad = new_token_rows
    query_pad = jnp.concatenate(
        [query_rows, jnp.zeros_like(query_rows)], axis=-1
    ).transpose(1, 0, 2)
    swap = [(0, 1), (1, 0)]
    z_count = lax.axis_size("tz")
    z_index = lax.axis_index("tz")
    first_core = core_index == 0
    chip_width = out_weight.shape[1] // z_count
    chip_columns = lax.dynamic_slice_in_dim(out_weight, z_index * chip_width, chip_width, 1)
    chip_columns = chip_columns.reshape(z_count, -1, chip_width)
    columns = chip_width // core_count
    chunk_rows = row_count // ROW_CHUNKS
    pieces = []
    for chunk in range(ROW_CHUNKS):
        attended = attend(
            bounds, query_pad, key_parts, fresh_pad, WINDOW_LENGTH, chunk * chunk_rows, chunk_rows
        )
        partner_heads = lax.ppermute(attended, "tc", swap)
        chip_heads = jnp.where(
            first_core,
            jnp.concatenate([attended, partner_heads], axis=1),
            jnp.concatenate([partner_heads, attended], axis=1),
        )
        half_rows = chunk_rows // core_count
        my_half = lax.dynamic_slice_in_dim(chip_heads, core_index * half_rows, half_rows, 0)
        sent = jnp.broadcast_to(my_half[None], (z_count,) + my_half.shape)
        chips_heads = lax.all_to_all(sent, "tz", 0, 0, tiled=True)
        half_out = jnp.einsum(
            "zrj,zjn->rn", chips_heads, chip_columns, preferred_element_type=jnp.float32
        ).astype(jnp.bfloat16)
        keep = lax.dynamic_slice_in_dim(half_out, core_index * columns, columns, 1)
        give = lax.dynamic_slice_in_dim(half_out, (1 - core_index) * columns, columns, 1)
        got = lax.ppermute(give, "tc", swap)
        pieces.append(
            jnp.where(
                first_core,
                jnp.concatenate([keep, got], axis=0),
                jnp.concatenate([got, keep], axis=0),
            )
        )
    projected = jnp.concatenate(pieces, axis=0)
    return projected


BLOCK_ROWS = 64
ROW_CHUNKS = 2


def attend_kernel(window, first_block, bounds_ref, q_ref, *refs):
    part_refs = list(zip(refs[0:-2:2], refs[1:-2:2]))
    fresh_ref, o_ref = refs[-2], refs[-1]
    heads, block_rows, _ = q_ref.shape
    stacked = heads * block_rows
    request_count = part_refs[0][0].shape[0]
    row_count = fresh_ref.shape[0]
    first_row = (pl.program_id(0) + first_block) * block_rows
    score_scale = HEAD_SIZE ** (-0.5)
    q = q_ref[...].reshape(stacked, 2 * HEAD_SIZE)
    rows = first_row + lax.broadcasted_iota(jnp.int32, (heads, block_rows, 1), 1).reshape(stacked, 1)
    r_first = jnp.int32(0)
    r_last = jnp.int32(-1)
    for k in range(request_count):
        r_first = r_first + (bounds_ref[request_count + k] <= first_row).astype(jnp.int32)
        r_last = r_last + (bounds_ref[k] < first_row + block_rows).astype(jnp.int32)
    r_last = jnp.minimum(r_last, request_count - 1)
    column = lax.broadcasted_iota(jnp.int32, (stacked, row_count), 1)
    fresh = fresh_ref[...]

    def scores_of(keys):
        return lax.dot_general(
            q, keys, (((1,), (1,)), ((), ())), preferred_element_type=jnp.float32
        ) * score_scale

    def one_request(r, out_acc):
        begin = bounds_ref[r]
        finish = bounds_ref[request_count + r]
        in_request = (rows >= begin) & (rows < finish)
        threshold = jnp.where(in_request, rows - begin + 1, window)
        newest = jnp.where(in_request, rows, -1)
        suffix_mask = (
            (column >= begin) & (column <= newest) & (rows - column < WINDOW_LENGTH)
        )
        pieces = [(fresh, scores_of(fresh), suffix_mask)]
        for keys_ref, positions_ref in part_refs:
            keys = keys_ref[r]
            pieces.append((keys, scores_of(keys), positions_ref[r] >= threshold))
        top = jnp.full((stacked, 1), MASKED_SCORE, jnp.float32)
        for _, scores, mask in pieces:
            top = jnp.maximum(
                top, jnp.max(jnp.where(mask, scores, MASKED_SCORE), axis=1, keepdims=True)
            )
        total = jnp.zeros_like(top)
        weighted = jnp.zeros((stacked, 2 * HEAD_SIZE), jnp.float32)
        for keys, scores, mask in pieces:
            raw = jnp.where(mask, jnp.exp(scores - top), 0.0)
            total = total + jnp.sum(raw, axis=1, keepdims=True)
            weighted = weighted + jnp.dot(
                raw.astype(jnp.bfloat16), keys, preferred_element_type=jnp.float32
            )
        safe_total = jnp.where(in_request, total, 1.0)
        return jnp.where(in_request, weighted / safe_total, out_acc)

    out_acc = lax.fori_loop(
        r_first, r_last + 1, one_request, jnp.zeros((stacked, 2 * HEAD_SIZE), jnp.float32)
    )
    result = out_acc[:, HEAD_SIZE:].astype(o_ref.dtype)
    for h in range(heads):
        o_ref[:, h * HEAD_SIZE : (h + 1) * HEAD_SIZE] = result[h * block_rows : (h + 1) * block_rows]


def attend(bounds, query_pad, key_parts, fresh_rows, window, first_row, rows):
    heads, row_count, width = query_pad.shape
    block_rows = math.gcd(rows, BLOCK_ROWS)
    first_block = first_row // block_rows
    part_specs = []
    part_args = []
    for keys, positions in key_parts:
        part_specs.append(pl.BlockSpec(keys.shape, lambda i, b: (0, 0, 0)))
        part_specs.append(pl.BlockSpec(positions.shape, lambda i, b: (0, 0, 0)))
        part_args.extend([keys, positions])
    return pl.pallas_call(
        functools.partial(attend_kernel, window, first_block),
        out_shape=jax.ShapeDtypeStruct((rows, heads * HEAD_SIZE), jnp.bfloat16),
        grid_spec=pltpu.PrefetchScalarGridSpec(
            num_scalar_prefetch=1,
            grid=(rows // block_rows,),
            in_specs=[
                pl.BlockSpec((heads, block_rows, width), lambda i, b: (0, i + first_block, 0))
            ]
            + part_specs
            + [pl.BlockSpec((row_count, width), lambda i, b: (0, 0))],
            out_specs=pl.BlockSpec((block_rows, heads * HEAD_SIZE), lambda i, b: (i, 0)),
        ),
        compiler_params=pltpu.CompilerParams(
            dimension_semantics=("arbitrary",), vmem_limit_bytes=48 * 1024 * 1024
        ),
    )(bounds, query_pad, *part_args, fresh_rows)


def solution(mesh):
    cores = 2
    seq_size, tensor_size = mesh.devices.shape
    split_mesh = jax.sharding.Mesh(
        mesh.devices.reshape(seq_size, tensor_size // cores, cores), ("seq", "tz", "tc")
    )
    return jax.shard_map(
        layer,
        mesh=split_mesh,
        in_specs=(
            P("seq", None),
            P(),
            P(None, ("tz", "tc")),
            P(),
            P(),
            P("seq", None, None, None),
            P(),
            P(),
            P(),
        ),
        out_specs=P("seq", ("tz", "tc")),
        check_vma=False,
    )
```

```python
import functools
import math

import jax
import jax.numpy as jnp
from jax import lax
from jax.sharding import PartitionSpec as P
from jax.experimental import pallas as pl
from jax.experimental.pallas import tpu as pltpu

QUERY_HEADS = 32
KEY_VALUE_HEADS = 4
HEAD_SIZE = 64
WINDOW_LENGTH = 2048
DEVICE_REQUESTS = 5
PPG = 64
WP = 16


MASKED_SCORE = -1e30


def normalize(tokens, norm_gain):
    widened = tokens.astype(jnp.float32)
    factor = lax.rsqrt(jnp.mean(widened * widened, axis=-1, keepdims=True) + 1e-05)
    return (widened * factor * norm_gain).astype(jnp.bfloat16)


def layer(
    tokens,
    norm_gain,
    query_weight,
    key_value_matrix,
    out_weight,
    cache_pages,
    page_table,
    request_lengths,
    request_groups,
):
    seq_count = lax.axis_size("seq")
    seq_index = lax.axis_index("seq")
    core_index = lax.axis_index("tc")
    tensor_rank_index = lax.axis_index("tz") * lax.axis_size("tc") + core_index
    row_count = tokens.shape[0]
    resident_heads = query_weight.shape[1] // HEAD_SIZE
    key_value_head = tensor_rank_index * resident_heads // (QUERY_HEADS // KEY_VALUE_HEADS)
    pages_here = cache_pages.shape[0]
    normed = normalize(tokens, norm_gain)
    query_rows = jnp.dot(normed, query_weight, preferred_element_type=jnp.float32).astype(
        jnp.bfloat16
    )
    query_rows = query_rows.reshape(row_count, resident_heads, HEAD_SIZE)
    head_weight = lax.dynamic_index_in_dim(key_value_matrix, key_value_head, 1, keepdims=False)
    new_token_rows = jnp.dot(normed, head_weight, preferred_element_type=jnp.float32).astype(
        jnp.bfloat16
    )
    lengths = lax.dynamic_slice_in_dim(
        request_lengths, seq_index * DEVICE_REQUESTS, DEVICE_REQUESTS
    )
    my_groups = lax.dynamic_slice_in_dim(
        request_groups, seq_index * DEVICE_REQUESTS, DEVICE_REQUESTS
    )
    tail_ids = page_table[:, PPG - WP :]
    holder = tail_ids // pages_here
    local_slot = tail_ids % pages_here
    held_slot = jnp.sum(jnp.where(holder == seq_index, local_slot, 0), axis=1)
    all_groups = request_groups.reshape(seq_count, DEVICE_REQUESTS)
    head_pages = lax.dynamic_index_in_dim(cache_pages, key_value_head, 1, keepdims=False)
    page_part = head_pages.shape[1] // lax.axis_size("tc")
    head_pages = lax.dynamic_slice_in_dim(head_pages, core_index * page_part, page_part, 1)
    outgoing = head_pages[held_slot[all_groups]]
    incoming = lax.all_to_all(outgoing, "seq", 0, 0, tiled=True)
    core_count = lax.axis_size("tc")
    partner = lax.ppermute(incoming, "tc", [(0, 1), (1, 0)])
    source_ids = lax.iota(jnp.int32, seq_count)
    page_order = jnp.sum(
        jnp.where(
            holder[:, :, None] == source_ids[None, None, :],
            lax.iota(jnp.int32, holder.shape[1])[None, :, None],
            0,
        ),
        axis=1,
    )
    page_start = page_order[my_groups][:, :, None] * (page_part * core_count)
    within = lax.iota(jnp.int32, page_part)[None, None, :]
    key_parts = []
    for part, half in ((incoming, core_index), (partner, (core_index + 1) % core_count)):
        positions = (page_start + half * page_part + within).reshape(DEVICE_REQUESTS, 1, -1)
        key_parts.append((part, positions))
    starts = jnp.cumsum(lengths) - lengths
    bounds = jnp.concatenate([starts, starts + lengths]).astype(jnp.int32)
    fresh_pad = new_token_rows
    query_pad = jnp.concatenate(
        [query_rows, jnp.zeros_like(query_rows)], axis=-1
    ).transpose(1, 0, 2)
    attended = attend(bounds, query_pad, key_parts, fresh_pad, WINDOW_LENGTH)
    swap = [(0, 1), (1, 0)]
    z_count = lax.axis_size("tz")
    z_index = lax.axis_index("tz")
    partner_heads = lax.ppermute(attended, "tc", swap)
    first_core = core_index == 0
    chip_heads = jnp.where(
        first_core,
        jnp.concatenate([attended, partner_heads], axis=1),
        jnp.concatenate([partner_heads, attended], axis=1),
    )
    half_rows = row_count // core_count
    my_half = lax.dynamic_slice_in_dim(chip_heads, core_index * half_rows, half_rows, 0)
    sent = jnp.broadcast_to(my_half[None], (z_count,) + my_half.shape)
    chips_heads = lax.all_to_all(sent, "tz", 0, 0, tiled=True)
    chip_width = out_weight.shape[1] // z_count
    chip_columns = lax.dynamic_slice_in_dim(out_weight, z_index * chip_width, chip_width, 1)
    chip_columns = chip_columns.reshape(z_count, my_half.shape[1], chip_width)
    half_out = jnp.einsum(
        "zrj,zjn->rn", chips_heads, chip_columns, preferred_element_type=jnp.float32
    ).astype(jnp.bfloat16)
    columns = chip_width // core_count
    keep = lax.dynamic_slice_in_dim(half_out, core_index * columns, columns, 1)
    give = lax.dynamic_slice_in_dim(half_out, (1 - core_index) * columns, columns, 1)
    got = lax.ppermute(give, "tc", swap)
    projected = jnp.where(
        first_core, jnp.concatenate([keep, got], axis=0), jnp.concatenate([got, keep], axis=0)
    )
    return projected


BLOCK_ROWS = 64


def attend_kernel(window, bounds_ref, q_ref, *refs):
    part_refs = list(zip(refs[0:-2:2], refs[1:-2:2]))
    fresh_ref, o_ref = refs[-2], refs[-1]
    heads, block_rows, _ = q_ref.shape
    stacked = heads * block_rows
    request_count = part_refs[0][0].shape[1]
    row_count = fresh_ref.shape[0]
    first_row = pl.program_id(0) * block_rows
    score_scale = HEAD_SIZE ** (-0.5)
    q = q_ref[...].reshape(stacked, 2 * HEAD_SIZE)
    rows = first_row + lax.broadcasted_iota(jnp.int32, (heads, block_rows, 1), 1).reshape(stacked, 1)
    r_first = jnp.int32(0)
    r_last = jnp.int32(-1)
    for k in range(request_count):
        r_first = r_first + (bounds_ref[request_count + k] <= first_row).astype(jnp.int32)
        r_last = r_last + (bounds_ref[k] < first_row + block_rows).astype(jnp.int32)
    r_last = jnp.minimum(r_last, request_count - 1)
    column = lax.broadcasted_iota(jnp.int32, (stacked, row_count), 1)
    fresh = fresh_ref[...]

    def scores_of(keys):
        return lax.dot_general(
            q, keys, (((1,), (1,)), ((), ())), preferred_element_type=jnp.float32
        ) * score_scale

    def one_request(r, out_acc):
        begin = bounds_ref[r]
        finish = bounds_ref[request_count + r]
        in_request = (rows >= begin) & (rows < finish)
        threshold = jnp.where(in_request, rows - begin + 1, window)
        newest = jnp.where(in_request, rows, -1)
        suffix_mask = (
            (column >= begin) & (column <= newest) & (rows - column < WINDOW_LENGTH)
        )
        pieces = [(fresh, scores_of(fresh), suffix_mask)]
        for keys_ref, positions_ref in part_refs:
            keys = keys_ref[:, r].reshape(-1, 2 * HEAD_SIZE)
            pieces.append((keys, scores_of(keys), positions_ref[r] >= threshold))
        top = jnp.full((stacked, 1), MASKED_SCORE, jnp.float32)
        for _, scores, mask in pieces:
            top = jnp.maximum(
                top, jnp.max(jnp.where(mask, scores, MASKED_SCORE), axis=1, keepdims=True)
            )
        total = jnp.zeros_like(top)
        weighted = jnp.zeros((stacked, 2 * HEAD_SIZE), jnp.float32)
        for keys, scores, mask in pieces:
            raw = jnp.where(mask, jnp.exp(scores - top), 0.0)
            total = total + jnp.sum(raw, axis=1, keepdims=True)
            weighted = weighted + jnp.dot(
                raw.astype(jnp.bfloat16), keys, preferred_element_type=jnp.float32
            )
        safe_total = jnp.where(in_request, total, 1.0)
        return jnp.where(in_request, weighted / safe_total, out_acc)

    out_acc = lax.fori_loop(
        r_first, r_last + 1, one_request, jnp.zeros((stacked, 2 * HEAD_SIZE), jnp.float32)
    )
    result = out_acc[:, HEAD_SIZE:].astype(o_ref.dtype)
    for h in range(heads):
        o_ref[:, h * HEAD_SIZE : (h + 1) * HEAD_SIZE] = result[h * block_rows : (h + 1) * block_rows]


def attend(bounds, query_pad, key_parts, fresh_rows, window):
    heads, row_count, width = query_pad.shape
    block_rows = math.gcd(row_count, BLOCK_ROWS)
    part_specs = []
    part_args = []
    for keys, positions in key_parts:
        part_specs.append(pl.BlockSpec(keys.shape, lambda i, b: (0, 0, 0, 0)))
        part_specs.append(pl.BlockSpec(positions.shape, lambda i, b: (0, 0, 0)))
        part_args.extend([keys, positions])
    return pl.pallas_call(
        functools.partial(attend_kernel, window),
        out_shape=jax.ShapeDtypeStruct((row_count, heads * HEAD_SIZE), jnp.bfloat16),
        grid_spec=pltpu.PrefetchScalarGridSpec(
            num_scalar_prefetch=1,
            grid=(row_count // block_rows,),
            in_specs=[pl.BlockSpec((heads, block_rows, width), lambda i, b: (0, i, 0))]
            + part_specs
            + [pl.BlockSpec((row_count, width), lambda i, b: (0, 0))],
            out_specs=pl.BlockSpec((block_rows, heads * HEAD_SIZE), lambda i, b: (i, 0)),
        ),
        compiler_params=pltpu.CompilerParams(
            dimension_semantics=("arbitrary",), vmem_limit_bytes=48 * 1024 * 1024
        ),
    )(bounds, query_pad, *part_args, fresh_rows)


def solution(mesh):
    cores = 2
    seq_size, tensor_size = mesh.devices.shape
    split_mesh = jax.sharding.Mesh(
        mesh.devices.reshape(seq_size, tensor_size // cores, cores), ("seq", "tz", "tc")
    )
    return jax.shard_map(
        layer,
        mesh=split_mesh,
        in_specs=(
            P("seq", None),
            P(),
            P(None, ("tz", "tc")),
            P(),
            P(),
            P("seq", None, None, None),
            P(),
            P(),
            P(),
        ),
        out_specs=P("seq", ("tz", "tc")),
        check_vma=False,
    )
```

```python
import functools
import math

import jax
import jax.numpy as jnp
from jax import lax
from jax.sharding import PartitionSpec as P
from jax.experimental import pallas as pl
from jax.experimental.pallas import tpu as pltpu

QUERY_HEADS = 32
KEY_VALUE_HEADS = 4
HEAD_SIZE = 64
WINDOW_LENGTH = 2048
DEVICE_REQUESTS = 5
PPG = 64
WP = 16


MASKED_SCORE = -1e30


def normalize(tokens, norm_gain):
    widened = tokens.astype(jnp.float32)
    factor = lax.rsqrt(jnp.mean(widened * widened, axis=-1, keepdims=True) + 1e-05)
    return (widened * factor * norm_gain).astype(jnp.bfloat16)


def layer(
    tokens,
    norm_gain,
    query_weight,
    key_value_matrix,
    out_weight,
    cache_pages,
    page_table,
    request_lengths,
    request_groups,
):
    seq_count = lax.axis_size("seq")
    seq_index = lax.axis_index("seq")
    core_index = lax.axis_index("tc")
    tensor_rank_index = lax.axis_index("tz") * lax.axis_size("tc") + core_index
    row_count = tokens.shape[0]
    resident_heads = query_weight.shape[1] // HEAD_SIZE
    key_value_head = tensor_rank_index * resident_heads // (QUERY_HEADS // KEY_VALUE_HEADS)
    pages_here = cache_pages.shape[0]
    normed = normalize(tokens, norm_gain)
    query_rows = jnp.dot(normed, query_weight, preferred_element_type=jnp.float32).astype(
        jnp.bfloat16
    )
    query_rows = query_rows.reshape(row_count, resident_heads, HEAD_SIZE)
    head_weight = lax.dynamic_index_in_dim(key_value_matrix, key_value_head, 1, keepdims=False)
    new_token_rows = jnp.dot(normed, head_weight, preferred_element_type=jnp.float32).astype(
        jnp.bfloat16
    )
    lengths = lax.dynamic_slice_in_dim(
        request_lengths, seq_index * DEVICE_REQUESTS, DEVICE_REQUESTS
    )
    my_groups = lax.dynamic_slice_in_dim(
        request_groups, seq_index * DEVICE_REQUESTS, DEVICE_REQUESTS
    )
    tail_ids = page_table[:, PPG - WP :]
    holder = tail_ids // pages_here
    local_slot = tail_ids % pages_here
    held_slot = jnp.sum(jnp.where(holder == seq_index, local_slot, 0), axis=1)
    all_groups = request_groups.reshape(seq_count, DEVICE_REQUESTS)
    page_part = cache_pages.shape[2] // lax.axis_size("tc")
    part_rows = core_index * page_part + lax.iota(jnp.int32, page_part)
    outgoing = cache_pages[
        held_slot[all_groups].T[:, :, None], key_value_head, part_rows[None, None, :]
    ]
    incoming = lax.all_to_all(outgoing, "seq", 1, 1, tiled=True)
    core_count = lax.axis_size("tc")
    partner = lax.ppermute(incoming, "tc", [(0, 1), (1, 0)])
    source_ids = lax.iota(jnp.int32, seq_count)
    page_order = jnp.sum(
        jnp.where(
            holder[:, :, None] == source_ids[None, None, :],
            lax.iota(jnp.int32, holder.shape[1])[None, :, None],
            0,
        ),
        axis=1,
    )
    page_start = page_order[my_groups][:, :, None] * (page_part * core_count)
    within = lax.iota(jnp.int32, page_part)[None, None, :]
    key_parts = []
    for part, half in ((incoming, core_index), (partner, (core_index + 1) % core_count)):
        positions = (page_start + half * page_part + within).reshape(DEVICE_REQUESTS, 1, -1)
        keys = part.reshape(DEVICE_REQUESTS, -1, 2 * HEAD_SIZE)
        key_parts.append((keys, positions))
    starts = jnp.cumsum(lengths) - lengths
    bounds = jnp.concatenate([starts, starts + lengths]).astype(jnp.int32)
    fresh_pad = new_token_rows
    query_pad = jnp.concatenate(
        [query_rows, jnp.zeros_like(query_rows)], axis=-1
    ).transpose(1, 0, 2)
    attended = attend(bounds, query_pad, key_parts, fresh_pad, WINDOW_LENGTH)
    swap = [(0, 1), (1, 0)]
    z_count = lax.axis_size("tz")
    z_index = lax.axis_index("tz")
    partner_heads = lax.ppermute(attended, "tc", swap)
    first_core = core_index == 0
    chip_heads = jnp.where(
        first_core,
        jnp.concatenate([attended, partner_heads], axis=1),
        jnp.concatenate([partner_heads, attended], axis=1),
    )
    half_rows = row_count // core_count
    my_half = lax.dynamic_slice_in_dim(chip_heads, core_index * half_rows, half_rows, 0)
    sent = jnp.broadcast_to(my_half[None], (z_count,) + my_half.shape)
    chips_heads = lax.all_to_all(sent, "tz", 0, 0, tiled=True)
    chip_width = out_weight.shape[1] // z_count
    chip_columns = lax.dynamic_slice_in_dim(out_weight, z_index * chip_width, chip_width, 1)
    chip_columns = chip_columns.reshape(z_count, my_half.shape[1], chip_width)
    half_out = jnp.einsum(
        "zrj,zjn->rn", chips_heads, chip_columns, preferred_element_type=jnp.float32
    ).astype(jnp.bfloat16)
    columns = chip_width // core_count
    keep = lax.dynamic_slice_in_dim(half_out, core_index * columns, columns, 1)
    give = lax.dynamic_slice_in_dim(half_out, (1 - core_index) * columns, columns, 1)
    got = lax.ppermute(give, "tc", swap)
    projected = jnp.where(
        first_core, jnp.concatenate([keep, got], axis=0), jnp.concatenate([got, keep], axis=0)
    )
    return projected


BLOCK_ROWS = 64


def attend_kernel(window, bounds_ref, q_ref, *refs):
    part_refs = list(zip(refs[0:-2:2], refs[1:-2:2]))
    fresh_ref, o_ref = refs[-2], refs[-1]
    heads, block_rows, _ = q_ref.shape
    stacked = heads * block_rows
    request_count = part_refs[0][0].shape[0]
    row_count = fresh_ref.shape[0]
    first_row = pl.program_id(0) * block_rows
    score_scale = HEAD_SIZE ** (-0.5)
    q = q_ref[...].reshape(stacked, 2 * HEAD_SIZE)
    rows = first_row + lax.broadcasted_iota(jnp.int32, (heads, block_rows, 1), 1).reshape(stacked, 1)
    r_first = jnp.int32(0)
    r_last = jnp.int32(-1)
    for k in range(request_count):
        r_first = r_first + (bounds_ref[request_count + k] <= first_row).astype(jnp.int32)
        r_last = r_last + (bounds_ref[k] < first_row + block_rows).astype(jnp.int32)
    r_last = jnp.minimum(r_last, request_count - 1)
    column = lax.broadcasted_iota(jnp.int32, (stacked, row_count), 1)
    fresh = fresh_ref[...]

    def scores_of(keys):
        return lax.dot_general(
            q, keys, (((1,), (1,)), ((), ())), preferred_element_type=jnp.float32
        ) * score_scale

    def one_request(r, out_acc):
        begin = bounds_ref[r]
        finish = bounds_ref[request_count + r]
        in_request = (rows >= begin) & (rows < finish)
        threshold = jnp.where(in_request, rows - begin + 1, window)
        newest = jnp.where(in_request, rows, -1)
        suffix_mask = (
            (column >= begin) & (column <= newest) & (rows - column < WINDOW_LENGTH)
        )
        pieces = [(fresh, scores_of(fresh), suffix_mask)]
        for keys_ref, positions_ref in part_refs:
            keys = keys_ref[r]
            pieces.append((keys, scores_of(keys), positions_ref[r] >= threshold))
        top = jnp.full((stacked, 1), MASKED_SCORE, jnp.float32)
        for _, scores, mask in pieces:
            top = jnp.maximum(
                top, jnp.max(jnp.where(mask, scores, MASKED_SCORE), axis=1, keepdims=True)
            )
        total = jnp.zeros_like(top)
        weighted = jnp.zeros((stacked, 2 * HEAD_SIZE), jnp.float32)
        for keys, scores, mask in pieces:
            raw = jnp.where(mask, jnp.exp(scores - top), 0.0)
            total = total + jnp.sum(raw, axis=1, keepdims=True)
            weighted = weighted + jnp.dot(
                raw.astype(jnp.bfloat16), keys, preferred_element_type=jnp.float32
            )
        safe_total = jnp.where(in_request, total, 1.0)
        return jnp.where(in_request, weighted / safe_total, out_acc)

    out_acc = lax.fori_loop(
        r_first, r_last + 1, one_request, jnp.zeros((stacked, 2 * HEAD_SIZE), jnp.float32)
    )
    result = out_acc[:, HEAD_SIZE:].astype(o_ref.dtype)
    for h in range(heads):
        o_ref[:, h * HEAD_SIZE : (h + 1) * HEAD_SIZE] = result[h * block_rows : (h + 1) * block_rows]


def attend(bounds, query_pad, key_parts, fresh_rows, window):
    heads, row_count, width = query_pad.shape
    block_rows = math.gcd(row_count, BLOCK_ROWS)
    part_specs = []
    part_args = []
    for keys, positions in key_parts:
        part_specs.append(pl.BlockSpec(keys.shape, lambda i, b: (0, 0, 0)))
        part_specs.append(pl.BlockSpec(positions.shape, lambda i, b: (0, 0, 0)))
        part_args.extend([keys, positions])
    return pl.pallas_call(
        functools.partial(attend_kernel, window),
        out_shape=jax.ShapeDtypeStruct((row_count, heads * HEAD_SIZE), jnp.bfloat16),
        grid_spec=pltpu.PrefetchScalarGridSpec(
            num_scalar_prefetch=1,
            grid=(row_count // block_rows,),
            in_specs=[pl.BlockSpec((heads, block_rows, width), lambda i, b: (0, i, 0))]
            + part_specs
            + [pl.BlockSpec((row_count, width), lambda i, b: (0, 0))],
            out_specs=pl.BlockSpec((block_rows, heads * HEAD_SIZE), lambda i, b: (i, 0)),
        ),
        compiler_params=pltpu.CompilerParams(
            dimension_semantics=("arbitrary",), vmem_limit_bytes=48 * 1024 * 1024
        ),
    )(bounds, query_pad, *part_args, fresh_rows)


def solution(mesh):
    cores = 2
    seq_size, tensor_size = mesh.devices.shape
    split_mesh = jax.sharding.Mesh(
        mesh.devices.reshape(seq_size, tensor_size // cores, cores), ("seq", "tz", "tc")
    )
    return jax.shard_map(
        layer,
        mesh=split_mesh,
        in_specs=(
            P("seq", None),
            P(),
            P(None, ("tz", "tc")),
            P(),
            P(),
            P("seq", None, None, None),
            P(),
            P(),
            P(),
        ),
        out_specs=P("seq", ("tz", "tc")),
        check_vma=False,
    )
```

```python
import functools
import math

import jax
import jax.numpy as jnp
from jax import lax
from jax.sharding import PartitionSpec as P
from jax.experimental import pallas as pl
from jax.experimental.pallas import tpu as pltpu

QUERY_HEADS = 32
KEY_VALUE_HEADS = 4
HEAD_SIZE = 64
WINDOW_LENGTH = 2048
DEVICE_REQUESTS = 5
PPG = 64
WP = 16


MASKED_SCORE = -1e30


def normalize(tokens, norm_gain):
    widened = tokens.astype(jnp.float32)
    factor = lax.rsqrt(jnp.mean(widened * widened, axis=-1, keepdims=True) + 1e-05)
    return (widened * factor * norm_gain).astype(jnp.bfloat16)


def layer(
    tokens,
    norm_gain,
    query_weight,
    key_value_matrix,
    out_weight,
    cache_pages,
    page_table,
    request_lengths,
    request_groups,
):
    seq_count = lax.axis_size("seq")
    seq_index = lax.axis_index("seq")
    core_index = lax.axis_index("tc")
    tensor_rank_index = lax.axis_index("tz") * lax.axis_size("tc") + core_index
    row_count = tokens.shape[0]
    resident_heads = query_weight.shape[1] // HEAD_SIZE
    key_value_head = tensor_rank_index * resident_heads // (QUERY_HEADS // KEY_VALUE_HEADS)
    pages_here = cache_pages.shape[0]
    normed = normalize(tokens, norm_gain)
    query_rows = jnp.dot(normed, query_weight, preferred_element_type=jnp.float32).astype(
        jnp.bfloat16
    )
    query_rows = query_rows.reshape(row_count, resident_heads, HEAD_SIZE)
    head_weight = lax.dynamic_index_in_dim(key_value_matrix, key_value_head, 1, keepdims=False)
    new_token_rows = jnp.dot(normed, head_weight, preferred_element_type=jnp.float32).astype(
        jnp.bfloat16
    )
    lengths = lax.dynamic_slice_in_dim(
        request_lengths, seq_index * DEVICE_REQUESTS, DEVICE_REQUESTS
    )
    my_groups = lax.dynamic_slice_in_dim(
        request_groups, seq_index * DEVICE_REQUESTS, DEVICE_REQUESTS
    )
    tail_ids = page_table[:, PPG - WP :]
    holder = tail_ids // pages_here
    local_slot = tail_ids % pages_here
    held_slot = jnp.sum(jnp.where(holder == seq_index, local_slot, 0), axis=1)
    all_groups = request_groups.reshape(seq_count, DEVICE_REQUESTS)
    head_pages = lax.dynamic_index_in_dim(cache_pages, key_value_head, 1, keepdims=False)
    page_part = head_pages.shape[1] // lax.axis_size("tc")
    head_pages = lax.dynamic_slice_in_dim(head_pages, core_index * page_part, page_part, 1)
    outgoing = head_pages[held_slot[all_groups].T]
    incoming = lax.all_to_all(outgoing, "seq", 1, 1, tiled=True)
    core_count = lax.axis_size("tc")
    partner = lax.ppermute(incoming, "tc", [(0, 1), (1, 0)])
    source_ids = lax.iota(jnp.int32, seq_count)
    page_order = jnp.sum(
        jnp.where(
            holder[:, :, None] == source_ids[None, None, :],
            lax.iota(jnp.int32, holder.shape[1])[None, :, None],
            0,
        ),
        axis=1,
    )
    page_start = page_order[my_groups][:, :, None] * (page_part * core_count)
    within = lax.iota(jnp.int32, page_part)[None, None, :]
    key_parts = []
    for part, half in ((incoming, core_index), (partner, (core_index + 1) % core_count)):
        positions = (page_start + half * page_part + within).reshape(DEVICE_REQUESTS, 1, -1)
        keys = part.reshape(DEVICE_REQUESTS, -1, 2 * HEAD_SIZE)
        key_parts.append((keys, positions))
    starts = jnp.cumsum(lengths) - lengths
    bounds = jnp.concatenate([starts, starts + lengths]).astype(jnp.int32)
    fresh_pad = new_token_rows
    query_pad = jnp.concatenate(
        [query_rows, jnp.zeros_like(query_rows)], axis=-1
    ).transpose(1, 0, 2)
    attended = attend(bounds, query_pad, key_parts, fresh_pad, WINDOW_LENGTH)
    swap = [(0, 1), (1, 0)]
    z_count = lax.axis_size("tz")
    z_index = lax.axis_index("tz")
    partner_heads = lax.ppermute(attended, "tc", swap)
    first_core = core_index == 0
    chip_heads = jnp.where(
        first_core,
        jnp.concatenate([attended, partner_heads], axis=1),
        jnp.concatenate([partner_heads, attended], axis=1),
    )
    half_rows = row_count // core_count
    my_half = lax.dynamic_slice_in_dim(chip_heads, core_index * half_rows, half_rows, 0)
    sent = jnp.broadcast_to(my_half[None], (z_count,) + my_half.shape)
    chips_heads = lax.all_to_all(sent, "tz", 0, 0, tiled=True)
    chip_width = out_weight.shape[1] // z_count
    chip_columns = lax.dynamic_slice_in_dim(out_weight, z_index * chip_width, chip_width, 1)
    chip_columns = chip_columns.reshape(z_count, my_half.shape[1], chip_width)
    half_out = jnp.einsum(
        "zrj,zjn->rn", chips_heads, chip_columns, preferred_element_type=jnp.float32
    ).astype(jnp.bfloat16)
    columns = chip_width // core_count
    keep = lax.dynamic_slice_in_dim(half_out, core_index * columns, columns, 1)
    give = lax.dynamic_slice_in_dim(half_out, (1 - core_index) * columns, columns, 1)
    got = lax.ppermute(give, "tc", swap)
    projected = jnp.where(
        first_core, jnp.concatenate([keep, got], axis=0), jnp.concatenate([got, keep], axis=0)
    )
    return projected


BLOCK_ROWS = 128


def attend_kernel(window, bounds_ref, q_ref, *refs):
    part_refs = list(zip(refs[0:-2:2], refs[1:-2:2]))
    fresh_ref, o_ref = refs[-2], refs[-1]
    heads, block_rows, _ = q_ref.shape
    stacked = heads * block_rows
    request_count = part_refs[0][0].shape[0]
    row_count = fresh_ref.shape[0]
    first_row = pl.program_id(0) * block_rows
    score_scale = HEAD_SIZE ** (-0.5)
    q = q_ref[...].reshape(stacked, 2 * HEAD_SIZE)
    rows = first_row + lax.broadcasted_iota(jnp.int32, (heads, block_rows, 1), 1).reshape(stacked, 1)
    r_first = jnp.int32(0)
    r_last = jnp.int32(-1)
    for k in range(request_count):
        r_first = r_first + (bounds_ref[request_count + k] <= first_row).astype(jnp.int32)
        r_last = r_last + (bounds_ref[k] < first_row + block_rows).astype(jnp.int32)
    r_last = jnp.minimum(r_last, request_count - 1)
    column = lax.broadcasted_iota(jnp.int32, (stacked, row_count), 1)
    fresh = fresh_ref[...]

    def scores_of(keys):
        return lax.dot_general(
            q, keys, (((1,), (1,)), ((), ())), preferred_element_type=jnp.float32
        ) * score_scale

    def one_request(r, out_acc):
        begin = bounds_ref[r]
        finish = bounds_ref[request_count + r]
        in_request = (rows >= begin) & (rows < finish)
        threshold = jnp.where(in_request, rows - begin + 1, window)
        newest = jnp.where(in_request, rows, -1)
        suffix_mask = (
            (column >= begin) & (column <= newest) & (rows - column < WINDOW_LENGTH)
        )
        pieces = [(fresh, scores_of(fresh), suffix_mask)]
        for keys_ref, positions_ref in part_refs:
            keys = keys_ref[r]
            pieces.append((keys, scores_of(keys), positions_ref[r] >= threshold))
        top = jnp.full((stacked, 1), MASKED_SCORE, jnp.float32)
        for _, scores, mask in pieces:
            top = jnp.maximum(
                top, jnp.max(jnp.where(mask, scores, MASKED_SCORE), axis=1, keepdims=True)
            )
        total = jnp.zeros_like(top)
        weighted = jnp.zeros((stacked, 2 * HEAD_SIZE), jnp.float32)
        for keys, scores, mask in pieces:
            raw = jnp.where(mask, jnp.exp(scores - top), 0.0)
            total = total + jnp.sum(raw, axis=1, keepdims=True)
            weighted = weighted + jnp.dot(
                raw.astype(jnp.bfloat16), keys, preferred_element_type=jnp.float32
            )
        safe_total = jnp.where(in_request, total, 1.0)
        return jnp.where(in_request, weighted / safe_total, out_acc)

    out_acc = lax.fori_loop(
        r_first, r_last + 1, one_request, jnp.zeros((stacked, 2 * HEAD_SIZE), jnp.float32)
    )
    result = out_acc[:, HEAD_SIZE:].astype(o_ref.dtype)
    for h in range(heads):
        o_ref[:, h * HEAD_SIZE : (h + 1) * HEAD_SIZE] = result[h * block_rows : (h + 1) * block_rows]


def attend(bounds, query_pad, key_parts, fresh_rows, window):
    heads, row_count, width = query_pad.shape
    block_rows = math.gcd(row_count, BLOCK_ROWS)
    part_specs = []
    part_args = []
    for keys, positions in key_parts:
        part_specs.append(pl.BlockSpec(keys.shape, lambda i, b: (0, 0, 0)))
        part_specs.append(pl.BlockSpec(positions.shape, lambda i, b: (0, 0, 0)))
        part_args.extend([keys, positions])
    return pl.pallas_call(
        functools.partial(attend_kernel, window),
        out_shape=jax.ShapeDtypeStruct((row_count, heads * HEAD_SIZE), jnp.bfloat16),
        grid_spec=pltpu.PrefetchScalarGridSpec(
            num_scalar_prefetch=1,
            grid=(row_count // block_rows,),
            in_specs=[pl.BlockSpec((heads, block_rows, width), lambda i, b: (0, i, 0))]
            + part_specs
            + [pl.BlockSpec((row_count, width), lambda i, b: (0, 0))],
            out_specs=pl.BlockSpec((block_rows, heads * HEAD_SIZE), lambda i, b: (i, 0)),
        ),
        compiler_params=pltpu.CompilerParams(
            dimension_semantics=("arbitrary",), vmem_limit_bytes=48 * 1024 * 1024
        ),
    )(bounds, query_pad, *part_args, fresh_rows)


def solution(mesh):
    cores = 2
    seq_size, tensor_size = mesh.devices.shape
    split_mesh = jax.sharding.Mesh(
        mesh.devices.reshape(seq_size, tensor_size // cores, cores), ("seq", "tz", "tc")
    )
    return jax.shard_map(
        layer,
        mesh=split_mesh,
        in_specs=(
            P("seq", None),
            P(),
            P(None, ("tz", "tc")),
            P(),
            P(),
            P("seq", None, None, None),
            P(),
            P(),
            P(),
        ),
        out_specs=P("seq", ("tz", "tc")),
        check_vma=False,
    )
```

```python
import functools
import math

import jax
import jax.numpy as jnp
from jax import lax
from jax.sharding import PartitionSpec as P
from jax.experimental import pallas as pl
from jax.experimental.pallas import tpu as pltpu

QUERY_HEADS = 32
KEY_VALUE_HEADS = 4
HEAD_SIZE = 64
WINDOW_LENGTH = 2048
DEVICE_REQUESTS = 5
PPG = 64
WP = 16


MASKED_SCORE = -1e30


def normalize(tokens, norm_gain):
    widened = tokens.astype(jnp.float32)
    factor = lax.rsqrt(jnp.mean(widened * widened, axis=-1, keepdims=True) + 1e-05)
    return (widened * factor * norm_gain).astype(jnp.bfloat16)


def layer(
    tokens,
    norm_gain,
    query_weight,
    key_value_matrix,
    out_weight,
    cache_pages,
    page_table,
    request_lengths,
    request_groups,
):
    seq_count = lax.axis_size("seq")
    seq_index = lax.axis_index("seq")
    core_index = lax.axis_index("tc")
    tensor_rank_index = lax.axis_index("tz") * lax.axis_size("tc") + core_index
    row_count = tokens.shape[0]
    resident_heads = query_weight.shape[1] // HEAD_SIZE
    key_value_head = tensor_rank_index * resident_heads // (QUERY_HEADS // KEY_VALUE_HEADS)
    pages_here = cache_pages.shape[0]
    normed = normalize(tokens, norm_gain)
    query_rows = jnp.dot(normed, query_weight, preferred_element_type=jnp.float32).astype(
        jnp.bfloat16
    )
    query_rows = query_rows.reshape(row_count, resident_heads, HEAD_SIZE)
    head_weight = lax.dynamic_index_in_dim(key_value_matrix, key_value_head, 1, keepdims=False)
    new_token_rows = jnp.dot(normed, head_weight, preferred_element_type=jnp.float32).astype(
        jnp.bfloat16
    )
    lengths = lax.dynamic_slice_in_dim(
        request_lengths, seq_index * DEVICE_REQUESTS, DEVICE_REQUESTS
    )
    my_groups = lax.dynamic_slice_in_dim(
        request_groups, seq_index * DEVICE_REQUESTS, DEVICE_REQUESTS
    )
    tail_ids = page_table[:, PPG - WP :]
    holder = tail_ids // pages_here
    local_slot = tail_ids % pages_here
    held_slot = jnp.sum(jnp.where(holder == seq_index, local_slot, 0), axis=1)
    all_groups = request_groups.reshape(seq_count, DEVICE_REQUESTS)
    head_pages = lax.dynamic_index_in_dim(cache_pages, key_value_head, 1, keepdims=False)
    page_part = head_pages.shape[1] // lax.axis_size("tc")
    head_pages = lax.dynamic_slice_in_dim(head_pages, core_index * page_part, page_part, 1)
    outgoing = head_pages[held_slot[all_groups].T]
    incoming = lax.all_to_all(outgoing, "seq", 1, 1, tiled=True)
    core_count = lax.axis_size("tc")
    partner = lax.ppermute(incoming, "tc", [(0, 1), (1, 0)])
    source_ids = lax.iota(jnp.int32, seq_count)
    page_order = jnp.sum(
        jnp.where(
            holder[:, :, None] == source_ids[None, None, :],
            lax.iota(jnp.int32, holder.shape[1])[None, :, None],
            0,
        ),
        axis=1,
    )
    page_start = page_order[my_groups][:, :, None] * (page_part * core_count)
    within = lax.iota(jnp.int32, page_part)[None, None, :]
    key_parts = []
    for part, half in ((incoming, core_index), (partner, (core_index + 1) % core_count)):
        positions = (page_start + half * page_part + within).reshape(DEVICE_REQUESTS, 1, -1)
        keys = part.reshape(DEVICE_REQUESTS, -1, 2 * HEAD_SIZE)
        key_parts.append((keys, positions))
    starts = jnp.cumsum(lengths) - lengths
    bounds = jnp.concatenate([starts, starts + lengths]).astype(jnp.int32)
    fresh_pad = new_token_rows
    query_pad = jnp.concatenate(
        [query_rows, jnp.zeros_like(query_rows)], axis=-1
    ).transpose(1, 0, 2)
    attended = attend(bounds, query_pad, key_parts, fresh_pad, WINDOW_LENGTH)
    swap = [(0, 1), (1, 0)]
    z_count = lax.axis_size("tz")
    z_index = lax.axis_index("tz")
    partner_heads = lax.ppermute(attended, "tc", swap)
    first_core = core_index == 0
    chip_heads = jnp.where(
        first_core,
        jnp.concatenate([attended, partner_heads], axis=1),
        jnp.concatenate([partner_heads, attended], axis=1),
    )
    half_rows = row_count // core_count
    my_half = lax.dynamic_slice_in_dim(chip_heads, core_index * half_rows, half_rows, 0)
    sent = jnp.broadcast_to(my_half[None], (z_count,) + my_half.shape)
    chips_heads = lax.all_to_all(sent, "tz", 0, 0, tiled=True)
    chip_width = out_weight.shape[1] // z_count
    chip_columns = lax.dynamic_slice_in_dim(out_weight, z_index * chip_width, chip_width, 1)
    chip_columns = chip_columns.reshape(z_count, my_half.shape[1], chip_width)
    half_out = jnp.einsum(
        "zrj,zjn->rn", chips_heads, chip_columns, preferred_element_type=jnp.float32
    ).astype(jnp.bfloat16)
    columns = chip_width // core_count
    keep = lax.dynamic_slice_in_dim(half_out, core_index * columns, columns, 1)
    give = lax.dynamic_slice_in_dim(half_out, (1 - core_index) * columns, columns, 1)
    got = lax.ppermute(give, "tc", swap)
    projected = jnp.where(
        first_core, jnp.concatenate([keep, got], axis=0), jnp.concatenate([got, keep], axis=0)
    )
    return projected


BLOCK_ROWS = 64


def attend_kernel(window, bounds_ref, q_ref, *refs):
    part_refs = list(zip(refs[0:-2:2], refs[1:-2:2]))
    fresh_ref, o_ref = refs[-2], refs[-1]
    heads, block_rows, _ = q_ref.shape
    stacked = heads * block_rows
    request_count = part_refs[0][0].shape[0]
    row_count = fresh_ref.shape[0]
    first_row = pl.program_id(0) * block_rows
    score_scale = HEAD_SIZE ** (-0.5)
    q = q_ref[...].reshape(stacked, 2 * HEAD_SIZE)
    rows = first_row + lax.broadcasted_iota(jnp.int32, (heads, block_rows, 1), 1).reshape(stacked, 1)
    r_first = jnp.int32(0)
    r_last = jnp.int32(-1)
    for k in range(request_count):
        r_first = r_first + (bounds_ref[request_count + k] <= first_row).astype(jnp.int32)
        r_last = r_last + (bounds_ref[k] < first_row + block_rows).astype(jnp.int32)
    r_last = jnp.minimum(r_last, request_count - 1)
    half_count = row_count // 2

    def scores_of(keys):
        return lax.dot_general(
            q, keys, (((1,), (1,)), ((), ())), preferred_element_type=jnp.float32
        ) * score_scale

    def one_request(r, out_acc):
        begin = bounds_ref[r]
        finish = bounds_ref[request_count + r]
        last_needed = jnp.minimum(finish, first_row + block_rows)
        branch = jnp.where(
            last_needed <= half_count, 0, jnp.where(begin >= half_count, 1, 2)
        ).astype(jnp.int32)
        branches = [
            functools.partial(request_terms, 0, half_count),
            functools.partial(request_terms, half_count, row_count),
            functools.partial(request_terms, 0, row_count),
        ]
        return lax.switch(branch, branches, r, begin, finish, out_acc)

    def request_terms(low, high, r, begin, finish, out_acc):
        fresh = fresh_ref[low:high, :]
        column = low + lax.broadcasted_iota(jnp.int32, (stacked, high - low), 1)
        in_request = (rows >= begin) & (rows < finish)
        threshold = jnp.where(in_request, rows - begin + 1, window)
        newest = jnp.where(in_request, rows, -1)
        suffix_mask = (
            (column >= begin) & (column <= newest) & (rows - column < WINDOW_LENGTH)
        )
        pieces = [(fresh, scores_of(fresh), suffix_mask)]
        for keys_ref, positions_ref in part_refs:
            keys = keys_ref[r]
            pieces.append((keys, scores_of(keys), positions_ref[r] >= threshold))
        top = jnp.full((stacked, 1), MASKED_SCORE, jnp.float32)
        for _, scores, mask in pieces:
            top = jnp.maximum(
                top, jnp.max(jnp.where(mask, scores, MASKED_SCORE), axis=1, keepdims=True)
            )
        total = jnp.zeros_like(top)
        weighted = jnp.zeros((stacked, 2 * HEAD_SIZE), jnp.float32)
        for keys, scores, mask in pieces:
            raw = jnp.where(mask, jnp.exp(scores - top), 0.0)
            total = total + jnp.sum(raw, axis=1, keepdims=True)
            weighted = weighted + jnp.dot(
                raw.astype(jnp.bfloat16), keys, preferred_element_type=jnp.float32
            )
        safe_total = jnp.where(in_request, total, 1.0)
        return jnp.where(in_request, weighted / safe_total, out_acc)

    out_acc = lax.fori_loop(
        r_first, r_last + 1, one_request, jnp.zeros((stacked, 2 * HEAD_SIZE), jnp.float32)
    )
    result = out_acc[:, HEAD_SIZE:].astype(o_ref.dtype)
    for h in range(heads):
        o_ref[:, h * HEAD_SIZE : (h + 1) * HEAD_SIZE] = result[h * block_rows : (h + 1) * block_rows]


def attend(bounds, query_pad, key_parts, fresh_rows, window):
    heads, row_count, width = query_pad.shape
    block_rows = math.gcd(row_count, BLOCK_ROWS)
    part_specs = []
    part_args = []
    for keys, positions in key_parts:
        part_specs.append(pl.BlockSpec(keys.shape, lambda i, b: (0, 0, 0)))
        part_specs.append(pl.BlockSpec(positions.shape, lambda i, b: (0, 0, 0)))
        part_args.extend([keys, positions])
    return pl.pallas_call(
        functools.partial(attend_kernel, window),
        out_shape=jax.ShapeDtypeStruct((row_count, heads * HEAD_SIZE), jnp.bfloat16),
        grid_spec=pltpu.PrefetchScalarGridSpec(
            num_scalar_prefetch=1,
            grid=(row_count // block_rows,),
            in_specs=[pl.BlockSpec((heads, block_rows, width), lambda i, b: (0, i, 0))]
            + part_specs
            + [pl.BlockSpec((row_count, width), lambda i, b: (0, 0))],
            out_specs=pl.BlockSpec((block_rows, heads * HEAD_SIZE), lambda i, b: (i, 0)),
        ),
        compiler_params=pltpu.CompilerParams(
            dimension_semantics=("arbitrary",), vmem_limit_bytes=48 * 1024 * 1024
        ),
    )(bounds, query_pad, *part_args, fresh_rows)


def solution(mesh):
    cores = 2
    seq_size, tensor_size = mesh.devices.shape
    split_mesh = jax.sharding.Mesh(
        mesh.devices.reshape(seq_size, tensor_size // cores, cores), ("seq", "tz", "tc")
    )
    return jax.shard_map(
        layer,
        mesh=split_mesh,
        in_specs=(
            P("seq", None),
            P(),
            P(None, ("tz", "tc")),
            P(),
            P(),
            P("seq", None, None, None),
            P(),
            P(),
            P(),
        ),
        out_specs=P("seq", ("tz", "tc")),
        check_vma=False,
    )
```

```python
import functools
import math

import jax
import jax.numpy as jnp
from jax import lax
from jax.sharding import PartitionSpec as P
from jax.experimental import pallas as pl
from jax.experimental.pallas import tpu as pltpu

QUERY_HEADS = 32
KEY_VALUE_HEADS = 4
HEAD_SIZE = 64
WINDOW_LENGTH = 2048
DEVICE_REQUESTS = 5
PPG = 64
WP = 16


MASKED_SCORE = -1e30


def normalize(tokens, norm_gain):
    widened = tokens.astype(jnp.float32)
    factor = lax.rsqrt(jnp.mean(widened * widened, axis=-1, keepdims=True) + 1e-05)
    return (widened * factor * norm_gain).astype(jnp.bfloat16)


def layer(
    tokens,
    norm_gain,
    query_weight,
    key_value_matrix,
    out_weight,
    cache_pages,
    page_table,
    request_lengths,
    request_groups,
):
    seq_count = lax.axis_size("seq")
    seq_index = lax.axis_index("seq")
    core_index = lax.axis_index("tc")
    tensor_rank_index = lax.axis_index("tz") * lax.axis_size("tc") + core_index
    row_count = tokens.shape[0]
    resident_heads = query_weight.shape[1] // HEAD_SIZE
    key_value_head = tensor_rank_index * resident_heads // (QUERY_HEADS // KEY_VALUE_HEADS)
    pages_here = cache_pages.shape[0]
    normed = normalize(tokens, norm_gain)
    query_rows = jnp.dot(normed, query_weight, preferred_element_type=jnp.float32).astype(
        jnp.bfloat16
    )
    query_rows = query_rows.reshape(row_count, resident_heads, HEAD_SIZE)
    head_weight = lax.dynamic_index_in_dim(key_value_matrix, key_value_head, 1, keepdims=False)
    new_token_rows = jnp.dot(normed, head_weight, preferred_element_type=jnp.float32).astype(
        jnp.bfloat16
    )
    lengths = lax.dynamic_slice_in_dim(
        request_lengths, seq_index * DEVICE_REQUESTS, DEVICE_REQUESTS
    )
    my_groups = lax.dynamic_slice_in_dim(
        request_groups, seq_index * DEVICE_REQUESTS, DEVICE_REQUESTS
    )
    tail_ids = page_table[:, PPG - WP :]
    holder = tail_ids // pages_here
    local_slot = tail_ids % pages_here
    held_slot = jnp.sum(jnp.where(holder == seq_index, local_slot, 0), axis=1)
    all_groups = request_groups.reshape(seq_count, DEVICE_REQUESTS)
    head_pages = lax.dynamic_index_in_dim(cache_pages, key_value_head, 1, keepdims=False)
    page_part = head_pages.shape[1] // lax.axis_size("tc")
    head_pages = lax.dynamic_slice_in_dim(head_pages, core_index * page_part, page_part, 1)
    outgoing = head_pages[held_slot[all_groups].T]
    incoming = lax.all_to_all(outgoing, "seq", 1, 1, tiled=True)
    core_count = lax.axis_size("tc")
    partner = lax.ppermute(incoming, "tc", [(0, 1), (1, 0)])
    source_ids = lax.iota(jnp.int32, seq_count)
    page_order = jnp.sum(
        jnp.where(
            holder[:, :, None] == source_ids[None, None, :],
            lax.iota(jnp.int32, holder.shape[1])[None, :, None],
            0,
        ),
        axis=1,
    )
    page_start = page_order[my_groups][:, :, None] * (page_part * core_count)
    within = lax.iota(jnp.int32, page_part)[None, None, :]
    key_parts = []
    for part, half in ((incoming, core_index), (partner, (core_index + 1) % core_count)):
        positions = (page_start + half * page_part + within).reshape(DEVICE_REQUESTS, 1, -1)
        keys = part.reshape(DEVICE_REQUESTS, -1, 2 * HEAD_SIZE)
        key_parts.append((keys, positions))
    starts = jnp.cumsum(lengths) - lengths
    bounds = jnp.concatenate([starts, starts + lengths]).astype(jnp.int32)
    fresh_pad = new_token_rows
    query_pad = query_rows.transpose(1, 0, 2)
    attended = attend(bounds, query_pad, key_parts, fresh_pad, WINDOW_LENGTH)
    swap = [(0, 1), (1, 0)]
    z_count = lax.axis_size("tz")
    z_index = lax.axis_index("tz")
    partner_heads = lax.ppermute(attended, "tc", swap)
    first_core = core_index == 0
    chip_heads = jnp.where(
        first_core,
        jnp.concatenate([attended, partner_heads], axis=1),
        jnp.concatenate([partner_heads, attended], axis=1),
    )
    half_rows = row_count // core_count
    my_half = lax.dynamic_slice_in_dim(chip_heads, core_index * half_rows, half_rows, 0)
    sent = jnp.broadcast_to(my_half[None], (z_count,) + my_half.shape)
    chips_heads = lax.all_to_all(sent, "tz", 0, 0, tiled=True)
    chip_width = out_weight.shape[1] // z_count
    chip_columns = lax.dynamic_slice_in_dim(out_weight, z_index * chip_width, chip_width, 1)
    chip_columns = chip_columns.reshape(z_count, my_half.shape[1], chip_width)
    half_out = jnp.einsum(
        "zrj,zjn->rn", chips_heads, chip_columns, preferred_element_type=jnp.float32
    ).astype(jnp.bfloat16)
    columns = chip_width // core_count
    keep = lax.dynamic_slice_in_dim(half_out, core_index * columns, columns, 1)
    give = lax.dynamic_slice_in_dim(half_out, (1 - core_index) * columns, columns, 1)
    got = lax.ppermute(give, "tc", swap)
    projected = jnp.where(
        first_core, jnp.concatenate([keep, got], axis=0), jnp.concatenate([got, keep], axis=0)
    )
    return projected


BLOCK_ROWS = 64


def attend_kernel(window, part_count, bounds_ref, q_ref, *refs):
    part_refs = list(zip(refs[0 : 2 * part_count : 2], refs[1 : 2 * part_count : 2]))
    fresh_ref, o_ref, fresh_t_ref = refs[2 * part_count : 2 * part_count + 3]
    key_t_refs = refs[2 * part_count + 3 :]
    heads, block_rows, _ = q_ref.shape
    stacked = heads * block_rows
    request_count = part_refs[0][0].shape[0]
    row_count = fresh_ref.shape[0]
    first_row = pl.program_id(0) * block_rows
    score_scale = HEAD_SIZE ** (-0.5)
    q = q_ref[...].reshape(stacked, HEAD_SIZE)

    @pl.when(pl.program_id(0) == 0)
    def _():
        fresh_t_ref[...] = fresh_ref[:, :HEAD_SIZE].astype(jnp.float32).T.astype(jnp.bfloat16)
        for (keys_ref, _), key_t_ref in zip(part_refs, key_t_refs):
            for r in range(request_count):
                key_t_ref[r] = (
                    keys_ref[r][:, :HEAD_SIZE].astype(jnp.float32).T.astype(jnp.bfloat16)
                )

    rows = first_row + lax.broadcasted_iota(jnp.int32, (heads, block_rows, 1), 1).reshape(stacked, 1)
    r_first = jnp.int32(0)
    r_last = jnp.int32(-1)
    for k in range(request_count):
        r_first = r_first + (bounds_ref[request_count + k] <= first_row).astype(jnp.int32)
        r_last = r_last + (bounds_ref[k] < first_row + block_rows).astype(jnp.int32)
    r_last = jnp.minimum(r_last, request_count - 1)
    column = lax.broadcasted_iota(jnp.int32, (stacked, row_count), 1)
    fresh = fresh_ref[...]

    def scores_of(keys_t):
        return jnp.dot(q, keys_t, preferred_element_type=jnp.float32) * score_scale

    def one_request(r, out_acc):
        begin = bounds_ref[r]
        finish = bounds_ref[request_count + r]
        in_request = (rows >= begin) & (rows < finish)
        threshold = jnp.where(in_request, rows - begin + 1, window)
        newest = jnp.where(in_request, rows, -1)
        suffix_mask = (
            (column >= begin) & (column <= newest) & (rows - column < WINDOW_LENGTH)
        )
        pieces = [(fresh, scores_of(fresh_t_ref[...]), suffix_mask)]
        for (keys_ref, positions_ref), key_t_ref in zip(part_refs, key_t_refs):
            keys = keys_ref[r]
            pieces.append((keys, scores_of(key_t_ref[r]), positions_ref[r] >= threshold))
        top = jnp.full((stacked, 1), MASKED_SCORE, jnp.float32)
        for _, scores, mask in pieces:
            top = jnp.maximum(
                top, jnp.max(jnp.where(mask, scores, MASKED_SCORE), axis=1, keepdims=True)
            )
        total = jnp.zeros_like(top)
        weighted = jnp.zeros((stacked, 2 * HEAD_SIZE), jnp.float32)
        for keys, scores, mask in pieces:
            raw = jnp.where(mask, jnp.exp(scores - top), 0.0)
            total = total + jnp.sum(raw, axis=1, keepdims=True)
            weighted = weighted + jnp.dot(
                raw.astype(jnp.bfloat16), keys, preferred_element_type=jnp.float32
            )
        safe_total = jnp.where(in_request, total, 1.0)
        return jnp.where(in_request, weighted / safe_total, out_acc)

    out_acc = lax.fori_loop(
        r_first, r_last + 1, one_request, jnp.zeros((stacked, 2 * HEAD_SIZE), jnp.float32)
    )
    result = out_acc[:, HEAD_SIZE:].astype(o_ref.dtype)
    for h in range(heads):
        o_ref[:, h * HEAD_SIZE : (h + 1) * HEAD_SIZE] = result[h * block_rows : (h + 1) * block_rows]


def attend(bounds, query_pad, key_parts, fresh_rows, window):
    heads, row_count, width = query_pad.shape
    block_rows = math.gcd(row_count, BLOCK_ROWS)
    part_specs = []
    part_args = []
    for keys, positions in key_parts:
        part_specs.append(pl.BlockSpec(keys.shape, lambda i, b: (0, 0, 0)))
        part_specs.append(pl.BlockSpec(positions.shape, lambda i, b: (0, 0, 0)))
        part_args.extend([keys, positions])
    return pl.pallas_call(
        functools.partial(attend_kernel, window, len(key_parts)),
        out_shape=jax.ShapeDtypeStruct((row_count, heads * HEAD_SIZE), jnp.bfloat16),
        grid_spec=pltpu.PrefetchScalarGridSpec(
            num_scalar_prefetch=1,
            grid=(row_count // block_rows,),
            in_specs=[pl.BlockSpec((heads, block_rows, width), lambda i, b: (0, i, 0))]
            + part_specs
            + [pl.BlockSpec(fresh_rows.shape, lambda i, b: (0, 0))],
            out_specs=pl.BlockSpec((block_rows, heads * HEAD_SIZE), lambda i, b: (i, 0)),
            scratch_shapes=[pltpu.VMEM((HEAD_SIZE, fresh_rows.shape[0]), jnp.bfloat16)]
            + [
                pltpu.VMEM((keys.shape[0], HEAD_SIZE, keys.shape[1]), jnp.bfloat16)
                for keys, _ in key_parts
            ],
        ),
        compiler_params=pltpu.CompilerParams(
            dimension_semantics=("arbitrary",), vmem_limit_bytes=48 * 1024 * 1024
        ),
    )(bounds, query_pad, *part_args, fresh_rows)


def solution(mesh):
    cores = 2
    seq_size, tensor_size = mesh.devices.shape
    split_mesh = jax.sharding.Mesh(
        mesh.devices.reshape(seq_size, tensor_size // cores, cores), ("seq", "tz", "tc")
    )
    return jax.shard_map(
        layer,
        mesh=split_mesh,
        in_specs=(
            P("seq", None),
            P(),
            P(None, ("tz", "tc")),
            P(),
            P(),
            P("seq", None, None, None),
            P(),
            P(),
            P(),
        ),
        out_specs=P("seq", ("tz", "tc")),
        check_vma=False,
    )
```

```python
import functools
import math

import jax
import jax.numpy as jnp
from jax import lax
from jax.sharding import PartitionSpec as P
from jax.experimental import pallas as pl
from jax.experimental.pallas import tpu as pltpu

QUERY_HEADS = 32
KEY_VALUE_HEADS = 4
HEAD_SIZE = 64
WINDOW_LENGTH = 2048
DEVICE_REQUESTS = 5
PPG = 64
WP = 16


MASKED_SCORE = -1e30


def normalize(tokens, norm_gain):
    widened = tokens.astype(jnp.float32)
    factor = lax.rsqrt(jnp.mean(widened * widened, axis=-1, keepdims=True) + 1e-05)
    return (widened * factor * norm_gain).astype(jnp.bfloat16)


def layer(
    tokens,
    norm_gain,
    query_weight,
    key_value_matrix,
    out_weight,
    cache_pages,
    page_table,
    request_lengths,
    request_groups,
):
    seq_count = lax.axis_size("seq")
    seq_index = lax.axis_index("seq")
    core_index = lax.axis_index("tc")
    tensor_rank_index = lax.axis_index("tz") * lax.axis_size("tc") + core_index
    row_count = tokens.shape[0]
    resident_heads = query_weight.shape[1] // HEAD_SIZE
    key_value_head = tensor_rank_index * resident_heads // (QUERY_HEADS // KEY_VALUE_HEADS)
    pages_here = cache_pages.shape[0]
    normed = normalize(tokens, norm_gain)
    query_rows = jnp.dot(normed, query_weight, preferred_element_type=jnp.float32).astype(
        jnp.bfloat16
    )
    query_rows = query_rows.reshape(row_count, resident_heads, HEAD_SIZE)
    head_weight = lax.dynamic_index_in_dim(key_value_matrix, key_value_head, 1, keepdims=False)
    new_token_rows = jnp.dot(normed, head_weight, preferred_element_type=jnp.float32).astype(
        jnp.bfloat16
    )
    lengths = lax.dynamic_slice_in_dim(
        request_lengths, seq_index * DEVICE_REQUESTS, DEVICE_REQUESTS
    )
    my_groups = lax.dynamic_slice_in_dim(
        request_groups, seq_index * DEVICE_REQUESTS, DEVICE_REQUESTS
    )
    tail_ids = page_table[:, PPG - WP :]
    holder = tail_ids // pages_here
    local_slot = tail_ids % pages_here
    held_slot = jnp.sum(jnp.where(holder == seq_index, local_slot, 0), axis=1)
    all_groups = request_groups.reshape(seq_count, DEVICE_REQUESTS)
    head_pages = lax.dynamic_index_in_dim(cache_pages, key_value_head, 1, keepdims=False)
    page_part = head_pages.shape[1] // lax.axis_size("tc")
    head_pages = lax.dynamic_slice_in_dim(head_pages, core_index * page_part, page_part, 1)
    outgoing = head_pages[held_slot[all_groups].T]
    incoming = lax.all_to_all(outgoing, "seq", 1, 1, tiled=True)
    core_count = lax.axis_size("tc")
    partner = lax.ppermute(incoming, "tc", [(0, 1), (1, 0)])
    source_ids = lax.iota(jnp.int32, seq_count)
    page_order = jnp.sum(
        jnp.where(
            holder[:, :, None] == source_ids[None, None, :],
            lax.iota(jnp.int32, holder.shape[1])[None, :, None],
            0,
        ),
        axis=1,
    )
    page_start = page_order[my_groups][:, :, None] * (page_part * core_count)
    within = lax.iota(jnp.int32, page_part)[None, None, :]
    key_parts = []
    for part, half in ((incoming, core_index), (partner, (core_index + 1) % core_count)):
        positions = (page_start + half * page_part + within).reshape(DEVICE_REQUESTS, 1, -1)
        keys = part.reshape(DEVICE_REQUESTS, -1, 2 * HEAD_SIZE)
        key_parts.append((keys, positions))
    starts = jnp.cumsum(lengths) - lengths
    bounds = jnp.concatenate([starts, starts + lengths]).astype(jnp.int32)
    fresh_pad = new_token_rows
    query_pad = query_rows.transpose(1, 0, 2)
    attended = attend(bounds, query_pad, key_parts, fresh_pad, WINDOW_LENGTH)
    swap = [(0, 1), (1, 0)]
    z_count = lax.axis_size("tz")
    z_index = lax.axis_index("tz")
    partner_heads = lax.ppermute(attended, "tc", swap)
    first_core = core_index == 0
    chip_heads = jnp.where(
        first_core,
        jnp.concatenate([attended, partner_heads], axis=1),
        jnp.concatenate([partner_heads, attended], axis=1),
    )
    half_rows = row_count // core_count
    my_half = lax.dynamic_slice_in_dim(chip_heads, core_index * half_rows, half_rows, 0)
    sent = jnp.broadcast_to(my_half[None], (z_count,) + my_half.shape)
    chips_heads = lax.all_to_all(sent, "tz", 0, 0, tiled=True)
    chip_width = out_weight.shape[1] // z_count
    chip_columns = lax.dynamic_slice_in_dim(out_weight, z_index * chip_width, chip_width, 1)
    chip_columns = chip_columns.reshape(z_count, my_half.shape[1], chip_width)
    half_out = jnp.einsum(
        "zrj,zjn->rn", chips_heads, chip_columns, preferred_element_type=jnp.float32
    ).astype(jnp.bfloat16)
    columns = chip_width // core_count
    keep = lax.dynamic_slice_in_dim(half_out, core_index * columns, columns, 1)
    give = lax.dynamic_slice_in_dim(half_out, (1 - core_index) * columns, columns, 1)
    got = lax.ppermute(give, "tc", swap)
    projected = jnp.where(
        first_core, jnp.concatenate([keep, got], axis=0), jnp.concatenate([got, keep], axis=0)
    )
    return projected


BLOCK_ROWS = 64


def attend_kernel(window, part_count, bounds_ref, q_ref, *refs):
    part_refs = list(zip(refs[0 : 2 * part_count : 2], refs[1 : 2 * part_count : 2]))
    fresh_ref, o_ref, fresh_t_ref = refs[2 * part_count : 2 * part_count + 3]
    key_t_refs = refs[2 * part_count + 3 :]
    heads, block_rows, _ = q_ref.shape
    stacked = heads * block_rows
    request_count = part_refs[0][0].shape[0]
    row_count = fresh_ref.shape[0]
    first_row = pl.program_id(0) * block_rows
    score_scale = HEAD_SIZE ** (-0.5)
    q = q_ref[...].reshape(stacked, HEAD_SIZE)

    @pl.when(pl.program_id(0) == 0)
    def _():
        fresh_t_ref[...] = fresh_ref[:, :HEAD_SIZE].astype(jnp.float32).T.astype(jnp.bfloat16)
        for (keys_ref, _), key_t_ref in zip(part_refs, key_t_refs):
            for r in range(request_count):
                key_t_ref[r] = (
                    keys_ref[r][:, :HEAD_SIZE].astype(jnp.float32).T.astype(jnp.bfloat16)
                )

    rows = first_row + lax.broadcasted_iota(jnp.int32, (heads, block_rows, 1), 1).reshape(stacked, 1)
    r_first = jnp.int32(0)
    r_last = jnp.int32(-1)
    for k in range(request_count):
        r_first = r_first + (bounds_ref[request_count + k] <= first_row).astype(jnp.int32)
        r_last = r_last + (bounds_ref[k] < first_row + block_rows).astype(jnp.int32)
    r_last = jnp.minimum(r_last, request_count - 1)

    chunk = 128

    def one_request(r, out_acc):
        begin = bounds_ref[r]
        finish = bounds_ref[request_count + r]
        in_request = (rows >= begin) & (rows < finish)
        threshold = jnp.where(in_request, rows - begin + 1, window)
        newest = jnp.where(in_request, rows, -1)
        lane = lax.broadcasted_iota(jnp.int32, (1, chunk), 1)

        def fresh_piece(c):
            start = pl.multiple_of(c * chunk, chunk)
            scores = jnp.dot(
                q, fresh_t_ref[:, pl.ds(start, chunk)], preferred_element_type=jnp.float32
            ) * score_scale
            column = start + lane
            mask = (column >= begin) & (column <= newest) & (rows - column < WINDOW_LENGTH)
            return scores, mask, fresh_ref[pl.ds(start, chunk), :]

        def part_piece(p, c):
            keys_ref, positions_ref = part_refs[p]
            start = pl.multiple_of(c * chunk, chunk)
            scores = jnp.dot(
                q, key_t_refs[p][r, :, pl.ds(start, chunk)], preferred_element_type=jnp.float32
            ) * score_scale
            mask = positions_ref[r, :, pl.ds(start, chunk)] >= threshold
            return scores, mask, keys_ref[r, pl.ds(start, chunk), :]

        piece_makers = [(fresh_piece, row_count // chunk)] + [
            (functools.partial(part_piece, p), part_refs[p][0].shape[1] // chunk)
            for p in range(len(part_refs))
        ]

        top = jnp.full((stacked, 1), MASKED_SCORE, jnp.float32)
        for make, count in piece_makers:

            def max_step(c, top, make=make):
                scores, mask, _ = make(c)
                return jnp.maximum(
                    top, jnp.max(jnp.where(mask, scores, MASKED_SCORE), axis=1, keepdims=True)
                )

            top = lax.fori_loop(0, count, max_step, top)

        total = jnp.zeros((stacked, 1), jnp.float32)
        weighted = jnp.zeros((stacked, 2 * HEAD_SIZE), jnp.float32)
        for make, count in piece_makers:

            def sum_step(c, carry, make=make):
                total, weighted = carry
                scores, mask, keys = make(c)
                raw = jnp.where(mask, jnp.exp(scores - top), 0.0)
                total = total + jnp.sum(raw, axis=1, keepdims=True)
                weighted = weighted + jnp.dot(
                    raw.astype(jnp.bfloat16), keys, preferred_element_type=jnp.float32
                )
                return total, weighted

            total, weighted = lax.fori_loop(0, count, sum_step, (total, weighted))
        safe_total = jnp.where(in_request, total, 1.0)
        return jnp.where(in_request, weighted / safe_total, out_acc)

    out_acc = lax.fori_loop(
        r_first, r_last + 1, one_request, jnp.zeros((stacked, 2 * HEAD_SIZE), jnp.float32)
    )
    result = out_acc[:, HEAD_SIZE:].astype(o_ref.dtype)
    for h in range(heads):
        o_ref[:, h * HEAD_SIZE : (h + 1) * HEAD_SIZE] = result[h * block_rows : (h + 1) * block_rows]


def attend(bounds, query_pad, key_parts, fresh_rows, window):
    heads, row_count, width = query_pad.shape
    block_rows = math.gcd(row_count, BLOCK_ROWS)
    part_specs = []
    part_args = []
    for keys, positions in key_parts:
        part_specs.append(pl.BlockSpec(keys.shape, lambda i, b: (0, 0, 0)))
        part_specs.append(pl.BlockSpec(positions.shape, lambda i, b: (0, 0, 0)))
        part_args.extend([keys, positions])
    return pl.pallas_call(
        functools.partial(attend_kernel, window, len(key_parts)),
        out_shape=jax.ShapeDtypeStruct((row_count, heads * HEAD_SIZE), jnp.bfloat16),
        grid_spec=pltpu.PrefetchScalarGridSpec(
            num_scalar_prefetch=1,
            grid=(row_count // block_rows,),
            in_specs=[pl.BlockSpec((heads, block_rows, width), lambda i, b: (0, i, 0))]
            + part_specs
            + [pl.BlockSpec(fresh_rows.shape, lambda i, b: (0, 0))],
            out_specs=pl.BlockSpec((block_rows, heads * HEAD_SIZE), lambda i, b: (i, 0)),
            scratch_shapes=[pltpu.VMEM((HEAD_SIZE, fresh_rows.shape[0]), jnp.bfloat16)]
            + [
                pltpu.VMEM((keys.shape[0], HEAD_SIZE, keys.shape[1]), jnp.bfloat16)
                for keys, _ in key_parts
            ],
        ),
        compiler_params=pltpu.CompilerParams(
            dimension_semantics=("arbitrary",), vmem_limit_bytes=48 * 1024 * 1024
        ),
    )(bounds, query_pad, *part_args, fresh_rows)


def solution(mesh):
    cores = 2
    seq_size, tensor_size = mesh.devices.shape
    split_mesh = jax.sharding.Mesh(
        mesh.devices.reshape(seq_size, tensor_size // cores, cores), ("seq", "tz", "tc")
    )
    return jax.shard_map(
        layer,
        mesh=split_mesh,
        in_specs=(
            P("seq", None),
            P(),
            P(None, ("tz", "tc")),
            P(),
            P(),
            P("seq", None, None, None),
            P(),
            P(),
            P(),
        ),
        out_specs=P("seq", ("tz", "tc")),
        check_vma=False,
    )
```

```python
import functools
import math

import jax
import jax.numpy as jnp
from jax import lax
from jax.sharding import PartitionSpec as P
from jax.experimental import pallas as pl
from jax.experimental.pallas import tpu as pltpu

QUERY_HEADS = 32
KEY_VALUE_HEADS = 4
HEAD_SIZE = 64
WINDOW_LENGTH = 2048
DEVICE_REQUESTS = 5
PPG = 64
WP = 16


MASKED_SCORE = -1e30


def normalize(tokens, norm_gain):
    widened = tokens.astype(jnp.float32)
    factor = lax.rsqrt(jnp.mean(widened * widened, axis=-1, keepdims=True) + 1e-05)
    return (widened * factor * norm_gain).astype(jnp.bfloat16)


def layer(
    tokens,
    norm_gain,
    query_weight,
    key_value_matrix,
    out_weight,
    cache_pages,
    page_table,
    request_lengths,
    request_groups,
):
    seq_count = lax.axis_size("seq")
    seq_index = lax.axis_index("seq")
    core_index = lax.axis_index("tc")
    tensor_rank_index = lax.axis_index("tz") * lax.axis_size("tc") + core_index
    row_count = tokens.shape[0]
    resident_heads = query_weight.shape[1] // HEAD_SIZE
    key_value_head = tensor_rank_index * resident_heads // (QUERY_HEADS // KEY_VALUE_HEADS)
    pages_here = cache_pages.shape[0]
    normed = normalize(tokens, norm_gain)
    query_rows = jnp.dot(normed, query_weight, preferred_element_type=jnp.float32).astype(
        jnp.bfloat16
    )
    query_rows = query_rows.reshape(row_count, resident_heads, HEAD_SIZE)
    head_weight = lax.dynamic_index_in_dim(key_value_matrix, key_value_head, 1, keepdims=False)
    new_token_rows = jnp.dot(normed, head_weight, preferred_element_type=jnp.float32).astype(
        jnp.bfloat16
    )
    lengths = lax.dynamic_slice_in_dim(
        request_lengths, seq_index * DEVICE_REQUESTS, DEVICE_REQUESTS
    )
    my_groups = lax.dynamic_slice_in_dim(
        request_groups, seq_index * DEVICE_REQUESTS, DEVICE_REQUESTS
    )
    tail_ids = page_table[:, PPG - WP :]
    holder = tail_ids // pages_here
    local_slot = tail_ids % pages_here
    held_slot = jnp.sum(jnp.where(holder == seq_index, local_slot, 0), axis=1)
    all_groups = request_groups.reshape(seq_count, DEVICE_REQUESTS)
    head_pages = lax.dynamic_index_in_dim(cache_pages, key_value_head, 1, keepdims=False)
    page_part = head_pages.shape[1] // lax.axis_size("tc")
    head_pages = lax.dynamic_slice_in_dim(head_pages, core_index * page_part, page_part, 1)
    outgoing = head_pages[held_slot[all_groups]]
    incoming = lax.all_to_all(outgoing, "seq", 0, 0, tiled=True)
    core_count = lax.axis_size("tc")
    partner = lax.ppermute(incoming, "tc", [(0, 1), (1, 0)])
    source_ids = lax.iota(jnp.int32, seq_count)
    page_order = jnp.sum(
        jnp.where(
            holder[:, :, None] == source_ids[None, None, :],
            lax.iota(jnp.int32, holder.shape[1])[None, :, None],
            0,
        ),
        axis=1,
    )
    page_start = page_order[my_groups][:, :, None] * (page_part * core_count)
    within = lax.iota(jnp.int32, page_part)[None, None, :]
    key_parts = []
    for part, half in ((incoming, core_index), (partner, (core_index + 1) % core_count)):
        positions = (page_start + half * page_part + within).reshape(DEVICE_REQUESTS, 1, -1)
        keys = part.transpose(1, 0, 2, 3).reshape(DEVICE_REQUESTS, -1, 2 * HEAD_SIZE)
        key_parts.append((keys, positions))
    starts = jnp.cumsum(lengths) - lengths
    bounds = jnp.concatenate([starts, starts + lengths]).astype(jnp.int32)
    fresh_pad = new_token_rows
    query_pad = jnp.concatenate(
        [query_rows, jnp.zeros_like(query_rows)], axis=-1
    ).transpose(1, 0, 2)
    attended = attend(bounds, query_pad, key_parts, fresh_pad, WINDOW_LENGTH)
    swap = [(0, 1), (1, 0)]
    z_count = lax.axis_size("tz")
    z_index = lax.axis_index("tz")
    partner_heads = lax.ppermute(attended, "tc", swap)
    first_core = core_index == 0
    chip_heads = jnp.where(
        first_core,
        jnp.concatenate([attended, partner_heads], axis=1),
        jnp.concatenate([partner_heads, attended], axis=1),
    )
    half_rows = row_count // core_count
    my_half = lax.dynamic_slice_in_dim(chip_heads, core_index * half_rows, half_rows, 0)
    sent = jnp.broadcast_to(my_half[None], (z_count,) + my_half.shape)
    chips_heads = lax.all_to_all(sent, "tz", 0, 0, tiled=True)
    chip_width = out_weight.shape[1] // z_count
    chip_columns = lax.dynamic_slice_in_dim(out_weight, z_index * chip_width, chip_width, 1)
    chip_columns = chip_columns.reshape(z_count, my_half.shape[1], chip_width)
    half_out = jnp.einsum(
        "zrj,zjn->rn", chips_heads, chip_columns, preferred_element_type=jnp.float32
    ).astype(jnp.bfloat16)
    columns = chip_width // core_count
    keep = lax.dynamic_slice_in_dim(half_out, core_index * columns, columns, 1)
    give = lax.dynamic_slice_in_dim(half_out, (1 - core_index) * columns, columns, 1)
    got = lax.ppermute(give, "tc", swap)
    projected = jnp.where(
        first_core, jnp.concatenate([keep, got], axis=0), jnp.concatenate([got, keep], axis=0)
    )
    return projected


BLOCK_ROWS = 64


def attend_kernel(window, bounds_ref, q_ref, *refs):
    part_refs = list(zip(refs[0:-2:2], refs[1:-2:2]))
    fresh_ref, o_ref = refs[-2], refs[-1]
    heads, block_rows, _ = q_ref.shape
    stacked = heads * block_rows
    request_count = part_refs[0][0].shape[0]
    row_count = fresh_ref.shape[0]
    first_row = pl.program_id(0) * block_rows
    score_scale = HEAD_SIZE ** (-0.5)
    q = q_ref[...].reshape(stacked, 2 * HEAD_SIZE)
    rows = first_row + lax.broadcasted_iota(jnp.int32, (heads, block_rows, 1), 1).reshape(stacked, 1)
    r_first = jnp.int32(0)
    r_last = jnp.int32(-1)
    for k in range(request_count):
        r_first = r_first + (bounds_ref[request_count + k] <= first_row).astype(jnp.int32)
        r_last = r_last + (bounds_ref[k] < first_row + block_rows).astype(jnp.int32)
    r_last = jnp.minimum(r_last, request_count - 1)
    column = lax.broadcasted_iota(jnp.int32, (stacked, row_count), 1)
    fresh = fresh_ref[...]

    def scores_of(keys):
        return lax.dot_general(
            q, keys, (((1,), (1,)), ((), ())), preferred_element_type=jnp.float32
        ) * score_scale

    def one_request(r, out_acc):
        begin = bounds_ref[r]
        finish = bounds_ref[request_count + r]
        in_request = (rows >= begin) & (rows < finish)
        threshold = jnp.where(in_request, rows - begin + 1, window)
        newest = jnp.where(in_request, rows, -1)
        suffix_mask = (
            (column >= begin) & (column <= newest) & (rows - column < WINDOW_LENGTH)
        )
        pieces = [(fresh, scores_of(fresh), suffix_mask)]
        for keys_ref, positions_ref in part_refs:
            keys = keys_ref[r]
            pieces.append((keys, scores_of(keys), positions_ref[r] >= threshold))
        top = jnp.full((stacked, 1), MASKED_SCORE, jnp.float32)
        for _, scores, mask in pieces:
            top = jnp.maximum(
                top, jnp.max(jnp.where(mask, scores, MASKED_SCORE), axis=1, keepdims=True)
            )
        total = jnp.zeros_like(top)
        weighted = jnp.zeros((stacked, 2 * HEAD_SIZE), jnp.float32)
        for keys, scores, mask in pieces:
            raw = jnp.where(mask, jnp.exp(scores - top), 0.0)
            total = total + jnp.sum(raw, axis=1, keepdims=True)
            weighted = weighted + jnp.dot(
                raw.astype(jnp.bfloat16), keys, preferred_element_type=jnp.float32
            )
        safe_total = jnp.where(in_request, total, 1.0)
        return jnp.where(in_request, weighted / safe_total, out_acc)

    out_acc = lax.fori_loop(
        r_first, r_last + 1, one_request, jnp.zeros((stacked, 2 * HEAD_SIZE), jnp.float32)
    )
    result = out_acc[:, HEAD_SIZE:].astype(o_ref.dtype)
    for h in range(heads):
        o_ref[:, h * HEAD_SIZE : (h + 1) * HEAD_SIZE] = result[h * block_rows : (h + 1) * block_rows]


def attend(bounds, query_pad, key_parts, fresh_rows, window):
    heads, row_count, width = query_pad.shape
    block_rows = math.gcd(row_count, BLOCK_ROWS)
    part_specs = []
    part_args = []
    for keys, positions in key_parts:
        part_specs.append(pl.BlockSpec(keys.shape, lambda i, b: (0, 0, 0)))
        part_specs.append(pl.BlockSpec(positions.shape, lambda i, b: (0, 0, 0)))
        part_args.extend([keys, positions])
    return pl.pallas_call(
        functools.partial(attend_kernel, window),
        out_shape=jax.ShapeDtypeStruct((row_count, heads * HEAD_SIZE), jnp.bfloat16),
        grid_spec=pltpu.PrefetchScalarGridSpec(
            num_scalar_prefetch=1,
            grid=(row_count // block_rows,),
            in_specs=[pl.BlockSpec((heads, block_rows, width), lambda i, b: (0, i, 0))]
            + part_specs
            + [pl.BlockSpec((row_count, width), lambda i, b: (0, 0))],
            out_specs=pl.BlockSpec((block_rows, heads * HEAD_SIZE), lambda i, b: (i, 0)),
        ),
        compiler_params=pltpu.CompilerParams(
            dimension_semantics=("arbitrary",), vmem_limit_bytes=48 * 1024 * 1024
        ),
    )(bounds, query_pad, *part_args, fresh_rows)


def solution(mesh):
    cores = 2
    seq_size, tensor_size = mesh.devices.shape
    split_mesh = jax.sharding.Mesh(
        mesh.devices.reshape(seq_size, tensor_size // cores, cores), ("seq", "tz", "tc")
    )
    return jax.shard_map(
        layer,
        mesh=split_mesh,
        in_specs=(
            P("seq", None),
            P(),
            P(None, ("tz", "tc")),
            P(),
            P(),
            P("seq", None, None, None),
            P(),
            P(),
            P(),
        ),
        out_specs=P("seq", ("tz", "tc")),
        check_vma=False,
    )
```

```python
import functools
import math

import jax
import jax.numpy as jnp
from jax import lax
from jax.sharding import PartitionSpec as P
from jax.experimental import pallas as pl
from jax.experimental.pallas import tpu as pltpu

QUERY_HEADS = 32
KEY_VALUE_HEADS = 4
HEAD_SIZE = 64
WINDOW_LENGTH = 2048
DEVICE_REQUESTS = 5
PPG = 64
WP = 16


MASKED_SCORE = -1e30


def normalize(tokens, norm_gain):
    widened = tokens.astype(jnp.float32)
    factor = lax.rsqrt(jnp.mean(widened * widened, axis=-1, keepdims=True) + 1e-05)
    return (widened * factor * norm_gain).astype(jnp.bfloat16)


def layer(
    tokens,
    norm_gain,
    query_weight,
    key_value_matrix,
    out_weight,
    cache_pages,
    page_table,
    request_lengths,
    request_groups,
):
    seq_count = lax.axis_size("seq")
    seq_index = lax.axis_index("seq")
    core_index = lax.axis_index("tc")
    tensor_rank_index = lax.axis_index("tz") * lax.axis_size("tc") + core_index
    row_count = tokens.shape[0]
    resident_heads = query_weight.shape[1] // HEAD_SIZE
    key_value_head = tensor_rank_index * resident_heads // (QUERY_HEADS // KEY_VALUE_HEADS)
    pages_here = cache_pages.shape[0]
    normed = normalize(tokens, norm_gain)
    query_rows = jnp.dot(normed, query_weight, preferred_element_type=jnp.float32).astype(
        jnp.bfloat16
    )
    query_rows = query_rows.reshape(row_count, resident_heads, HEAD_SIZE)
    head_weight = lax.dynamic_index_in_dim(key_value_matrix, key_value_head, 1, keepdims=False)
    new_token_rows = jnp.dot(normed, head_weight, preferred_element_type=jnp.float32).astype(
        jnp.bfloat16
    )
    lengths = lax.dynamic_slice_in_dim(
        request_lengths, seq_index * DEVICE_REQUESTS, DEVICE_REQUESTS
    )
    my_groups = lax.dynamic_slice_in_dim(
        request_groups, seq_index * DEVICE_REQUESTS, DEVICE_REQUESTS
    )
    tail_ids = page_table[:, PPG - WP :]
    holder = tail_ids // pages_here
    local_slot = tail_ids % pages_here
    held_slot = jnp.sum(jnp.where(holder == seq_index, local_slot, 0), axis=1)
    all_groups = request_groups.reshape(seq_count, DEVICE_REQUESTS)
    page_part = cache_pages.shape[2] // lax.axis_size("tc")
    outgoing = lax.dynamic_slice_in_dim(
        cache_pages[held_slot[all_groups], key_value_head], core_index * page_part, page_part, 2
    )
    incoming = lax.all_to_all(outgoing, "seq", 0, 0, tiled=True)
    core_count = lax.axis_size("tc")
    partner = lax.ppermute(incoming, "tc", [(0, 1), (1, 0)])
    source_ids = lax.iota(jnp.int32, seq_count)
    page_order = jnp.sum(
        jnp.where(
            holder[:, :, None] == source_ids[None, None, :],
            lax.iota(jnp.int32, holder.shape[1])[None, :, None],
            0,
        ),
        axis=1,
    )
    page_start = page_order[my_groups][:, :, None] * (page_part * core_count)
    within = lax.iota(jnp.int32, page_part)[None, None, :]
    key_parts = []
    for part, half in ((incoming, core_index), (partner, (core_index + 1) % core_count)):
        positions = (page_start + half * page_part + within).reshape(DEVICE_REQUESTS, 1, -1)
        keys = part.transpose(1, 0, 2, 3).reshape(DEVICE_REQUESTS, -1, 2 * HEAD_SIZE)
        key_parts.append((keys, positions))
    starts = jnp.cumsum(lengths) - lengths
    bounds = jnp.concatenate([starts, starts + lengths]).astype(jnp.int32)
    fresh_pad = new_token_rows
    query_pad = jnp.concatenate(
        [query_rows, jnp.zeros_like(query_rows)], axis=-1
    ).transpose(1, 0, 2)
    attended = attend(bounds, query_pad, key_parts, fresh_pad, WINDOW_LENGTH)
    swap = [(0, 1), (1, 0)]
    z_count = lax.axis_size("tz")
    z_index = lax.axis_index("tz")
    partner_heads = lax.ppermute(attended, "tc", swap)
    first_core = core_index == 0
    chip_heads = jnp.where(
        first_core,
        jnp.concatenate([attended, partner_heads], axis=1),
        jnp.concatenate([partner_heads, attended], axis=1),
    )
    half_rows = row_count // core_count
    my_half = lax.dynamic_slice_in_dim(chip_heads, core_index * half_rows, half_rows, 0)
    sent = jnp.broadcast_to(my_half[None], (z_count,) + my_half.shape)
    chips_heads = lax.all_to_all(sent, "tz", 0, 0, tiled=True)
    chip_width = out_weight.shape[1] // z_count
    chip_columns = lax.dynamic_slice_in_dim(out_weight, z_index * chip_width, chip_width, 1)
    chip_columns = chip_columns.reshape(z_count, my_half.shape[1], chip_width)
    half_out = jnp.einsum(
        "zrj,zjn->rn", chips_heads, chip_columns, preferred_element_type=jnp.float32
    ).astype(jnp.bfloat16)
    columns = chip_width // core_count
    keep = lax.dynamic_slice_in_dim(half_out, core_index * columns, columns, 1)
    give = lax.dynamic_slice_in_dim(half_out, (1 - core_index) * columns, columns, 1)
    got = lax.ppermute(give, "tc", swap)
    projected = jnp.where(
        first_core, jnp.concatenate([keep, got], axis=0), jnp.concatenate([got, keep], axis=0)
    )
    return projected


BLOCK_ROWS = 64


def attend_kernel(window, bounds_ref, q_ref, *refs):
    part_refs = list(zip(refs[0:-2:2], refs[1:-2:2]))
    fresh_ref, o_ref = refs[-2], refs[-1]
    heads, block_rows, _ = q_ref.shape
    stacked = heads * block_rows
    request_count = part_refs[0][0].shape[0]
    row_count = fresh_ref.shape[0]
    first_row = pl.program_id(0) * block_rows
    score_scale = HEAD_SIZE ** (-0.5)
    q = q_ref[...].reshape(stacked, 2 * HEAD_SIZE)
    rows = first_row + lax.broadcasted_iota(jnp.int32, (heads, block_rows, 1), 1).reshape(stacked, 1)
    r_first = jnp.int32(0)
    r_last = jnp.int32(-1)
    for k in range(request_count):
        r_first = r_first + (bounds_ref[request_count + k] <= first_row).astype(jnp.int32)
        r_last = r_last + (bounds_ref[k] < first_row + block_rows).astype(jnp.int32)
    r_last = jnp.minimum(r_last, request_count - 1)
    column = lax.broadcasted_iota(jnp.int32, (stacked, row_count), 1)
    fresh = fresh_ref[...]

    def scores_of(keys):
        return lax.dot_general(
            q, keys, (((1,), (1,)), ((), ())), preferred_element_type=jnp.float32
        ) * score_scale

    def one_request(r, out_acc):
        begin = bounds_ref[r]
        finish = bounds_ref[request_count + r]
        in_request = (rows >= begin) & (rows < finish)
        threshold = jnp.where(in_request, rows - begin + 1, window)
        newest = jnp.where(in_request, rows, -1)
        suffix_mask = (
            (column >= begin) & (column <= newest) & (rows - column < WINDOW_LENGTH)
        )
        pieces = [(fresh, scores_of(fresh), suffix_mask)]
        for keys_ref, positions_ref in part_refs:
            keys = keys_ref[r]
            pieces.append((keys, scores_of(keys), positions_ref[r] >= threshold))
        top = jnp.full((stacked, 1), MASKED_SCORE, jnp.float32)
        for _, scores, mask in pieces:
            top = jnp.maximum(
                top, jnp.max(jnp.where(mask, scores, MASKED_SCORE), axis=1, keepdims=True)
            )
        total = jnp.zeros_like(top)
        weighted = jnp.zeros((stacked, 2 * HEAD_SIZE), jnp.float32)
        for keys, scores, mask in pieces:
            raw = jnp.where(mask, jnp.exp(scores - top), 0.0)
            total = total + jnp.sum(raw, axis=1, keepdims=True)
            weighted = weighted + jnp.dot(
                raw.astype(jnp.bfloat16), keys, preferred_element_type=jnp.float32
            )
        safe_total = jnp.where(in_request, total, 1.0)
        return jnp.where(in_request, weighted / safe_total, out_acc)

    out_acc = lax.fori_loop(
        r_first, r_last + 1, one_request, jnp.zeros((stacked, 2 * HEAD_SIZE), jnp.float32)
    )
    result = out_acc[:, HEAD_SIZE:].astype(o_ref.dtype)
    for h in range(heads):
        o_ref[:, h * HEAD_SIZE : (h + 1) * HEAD_SIZE] = result[h * block_rows : (h + 1) * block_rows]


def attend(bounds, query_pad, key_parts, fresh_rows, window):
    heads, row_count, width = query_pad.shape
    block_rows = math.gcd(row_count, BLOCK_ROWS)
    part_specs = []
    part_args = []
    for keys, positions in key_parts:
        part_specs.append(pl.BlockSpec(keys.shape, lambda i, b: (0, 0, 0)))
        part_specs.append(pl.BlockSpec(positions.shape, lambda i, b: (0, 0, 0)))
        part_args.extend([keys, positions])
    return pl.pallas_call(
        functools.partial(attend_kernel, window),
        out_shape=jax.ShapeDtypeStruct((row_count, heads * HEAD_SIZE), jnp.bfloat16),
        grid_spec=pltpu.PrefetchScalarGridSpec(
            num_scalar_prefetch=1,
            grid=(row_count // block_rows,),
            in_specs=[pl.BlockSpec((heads, block_rows, width), lambda i, b: (0, i, 0))]
            + part_specs
            + [pl.BlockSpec((row_count, width), lambda i, b: (0, 0))],
            out_specs=pl.BlockSpec((block_rows, heads * HEAD_SIZE), lambda i, b: (i, 0)),
        ),
        compiler_params=pltpu.CompilerParams(
            dimension_semantics=("arbitrary",), vmem_limit_bytes=48 * 1024 * 1024
        ),
    )(bounds, query_pad, *part_args, fresh_rows)


def solution(mesh):
    cores = 2
    seq_size, tensor_size = mesh.devices.shape
    split_mesh = jax.sharding.Mesh(
        mesh.devices.reshape(seq_size, tensor_size // cores, cores), ("seq", "tz", "tc")
    )
    return jax.shard_map(
        layer,
        mesh=split_mesh,
        in_specs=(
            P("seq", None),
            P(),
            P(None, ("tz", "tc")),
            P(),
            P(),
            P("seq", None, None, None),
            P(),
            P(),
            P(),
        ),
        out_specs=P("seq", ("tz", "tc")),
        check_vma=False,
    )
```

```python
import functools
import math

import jax
import jax.numpy as jnp
from jax import lax
from jax.sharding import PartitionSpec as P
from jax.experimental import pallas as pl
from jax.experimental.pallas import tpu as pltpu

QUERY_HEADS = 32
KEY_VALUE_HEADS = 4
HEAD_SIZE = 64
WINDOW_LENGTH = 2048
DEVICE_REQUESTS = 5
PPG = 64
WP = 16


MASKED_SCORE = -1e30


def normalize(tokens, norm_gain):
    widened = tokens.astype(jnp.float32)
    factor = lax.rsqrt(jnp.mean(widened * widened, axis=-1, keepdims=True) + 1e-05)
    return (widened * factor * norm_gain).astype(jnp.bfloat16)


def layer(
    tokens,
    norm_gain,
    query_weight,
    key_value_matrix,
    out_weight,
    cache_pages,
    page_table,
    request_lengths,
    request_groups,
):
    seq_count = lax.axis_size("seq")
    seq_index = lax.axis_index("seq")
    core_index = lax.axis_index("tc")
    tensor_rank_index = lax.axis_index("tz") * lax.axis_size("tc") + core_index
    row_count = tokens.shape[0]
    resident_heads = query_weight.shape[1] // HEAD_SIZE
    key_value_head = tensor_rank_index * resident_heads // (QUERY_HEADS // KEY_VALUE_HEADS)
    pages_here = cache_pages.shape[0]
    normed = normalize(tokens, norm_gain)
    query_rows = jnp.dot(normed, query_weight, preferred_element_type=jnp.float32).astype(
        jnp.bfloat16
    )
    query_rows = query_rows.reshape(row_count, resident_heads, HEAD_SIZE)
    head_weight = lax.dynamic_index_in_dim(key_value_matrix, key_value_head, 1, keepdims=False)
    new_token_rows = jnp.dot(normed, head_weight, preferred_element_type=jnp.float32).astype(
        jnp.bfloat16
    )
    lengths = lax.dynamic_slice_in_dim(
        request_lengths, seq_index * DEVICE_REQUESTS, DEVICE_REQUESTS
    )
    my_groups = lax.dynamic_slice_in_dim(
        request_groups, seq_index * DEVICE_REQUESTS, DEVICE_REQUESTS
    )
    tail_ids = page_table[:, PPG - WP :]
    holder = tail_ids // pages_here
    local_slot = tail_ids % pages_here
    held_slot = jnp.sum(jnp.where(holder == seq_index, local_slot, 0), axis=1)
    all_groups = request_groups.reshape(seq_count, DEVICE_REQUESTS)
    head_pages = lax.dynamic_index_in_dim(cache_pages, key_value_head, 1, keepdims=False)
    page_part = head_pages.shape[1] // lax.axis_size("tc")
    head_pages = lax.dynamic_slice_in_dim(head_pages, core_index * page_part, page_part, 1)
    outgoing = head_pages[held_slot[all_groups]]
    incoming = lax.all_to_all(outgoing, "seq", 0, 0, tiled=True)
    core_count = lax.axis_size("tc")
    partner = lax.ppermute(incoming, "tc", [(0, 1), (1, 0)])
    source_ids = lax.iota(jnp.int32, seq_count)
    page_order = jnp.sum(
        jnp.where(
            holder[:, :, None] == source_ids[None, None, :],
            lax.iota(jnp.int32, holder.shape[1])[None, :, None],
            0,
        ),
        axis=1,
    )
    page_start = page_order[my_groups][:, :, None] * (page_part * core_count)
    within = lax.iota(jnp.int32, page_part)[None, None, :]
    key_parts = []
    for part, half in ((incoming, core_index), (partner, (core_index + 1) % core_count)):
        positions = (page_start + half * page_part + within).reshape(DEVICE_REQUESTS, 1, -1)
        keys = part.transpose(1, 0, 2, 3).reshape(DEVICE_REQUESTS, -1, 2 * HEAD_SIZE)
        key_parts.append((keys, positions))
    starts = jnp.cumsum(lengths) - lengths
    bounds = jnp.concatenate([starts, starts + lengths]).astype(jnp.int32)
    fresh_pad = new_token_rows
    query_pad = jnp.concatenate(
        [query_rows, jnp.zeros_like(query_rows)], axis=-1
    ).transpose(1, 0, 2)
    attended = attend(bounds, query_pad, key_parts, fresh_pad, WINDOW_LENGTH)
    swap = [(0, 1), (1, 0)]
    z_count = lax.axis_size("tz")
    z_index = lax.axis_index("tz")
    first_core = core_index == 0
    half_rows = row_count // core_count
    own_rows = lax.dynamic_slice_in_dim(attended, core_index * half_rows, half_rows, 0)
    partner_rows = lax.dynamic_slice_in_dim(
        attended, (1 - core_index) * half_rows, half_rows, 0
    )
    partner_heads = lax.ppermute(partner_rows, "tc", swap)
    my_half = jnp.where(
        first_core,
        jnp.concatenate([own_rows, partner_heads], axis=1),
        jnp.concatenate([partner_heads, own_rows], axis=1),
    )
    sent = jnp.broadcast_to(my_half[None], (z_count,) + my_half.shape)
    chips_heads = lax.all_to_all(sent, "tz", 0, 0, tiled=True)
    chip_width = out_weight.shape[1] // z_count
    chip_columns = lax.dynamic_slice_in_dim(out_weight, z_index * chip_width, chip_width, 1)
    chip_columns = chip_columns.reshape(z_count, my_half.shape[1], chip_width)
    half_out = jnp.einsum(
        "zrj,zjn->rn", chips_heads, chip_columns, preferred_element_type=jnp.float32
    ).astype(jnp.bfloat16)
    columns = chip_width // core_count
    keep = lax.dynamic_slice_in_dim(half_out, core_index * columns, columns, 1)
    give = lax.dynamic_slice_in_dim(half_out, (1 - core_index) * columns, columns, 1)
    got = lax.ppermute(give, "tc", swap)
    projected = jnp.where(
        first_core, jnp.concatenate([keep, got], axis=0), jnp.concatenate([got, keep], axis=0)
    )
    return projected


BLOCK_ROWS = 64


def attend_kernel(window, bounds_ref, q_ref, *refs):
    part_refs = list(zip(refs[0:-2:2], refs[1:-2:2]))
    fresh_ref, o_ref = refs[-2], refs[-1]
    heads, block_rows, _ = q_ref.shape
    stacked = heads * block_rows
    request_count = part_refs[0][0].shape[0]
    row_count = fresh_ref.shape[0]
    first_row = pl.program_id(0) * block_rows
    score_scale = HEAD_SIZE ** (-0.5)
    q = q_ref[...].reshape(stacked, 2 * HEAD_SIZE)
    rows = first_row + lax.broadcasted_iota(jnp.int32, (heads, block_rows, 1), 1).reshape(stacked, 1)
    r_first = jnp.int32(0)
    r_last = jnp.int32(-1)
    for k in range(request_count):
        r_first = r_first + (bounds_ref[request_count + k] <= first_row).astype(jnp.int32)
        r_last = r_last + (bounds_ref[k] < first_row + block_rows).astype(jnp.int32)
    r_last = jnp.minimum(r_last, request_count - 1)
    column = lax.broadcasted_iota(jnp.int32, (stacked, row_count), 1)
    fresh = fresh_ref[...]

    def scores_of(keys):
        return lax.dot_general(
            q, keys, (((1,), (1,)), ((), ())), preferred_element_type=jnp.float32
        ) * score_scale

    def one_request(r, out_acc):
        begin = bounds_ref[r]
        finish = bounds_ref[request_count + r]
        in_request = (rows >= begin) & (rows < finish)
        threshold = jnp.where(in_request, rows - begin + 1, window)
        newest = jnp.where(in_request, rows, -1)
        suffix_mask = (
            (column >= begin) & (column <= newest) & (rows - column < WINDOW_LENGTH)
        )
        pieces = [(fresh, scores_of(fresh), suffix_mask)]
        for keys_ref, positions_ref in part_refs:
            keys = keys_ref[r]
            pieces.append((keys, scores_of(keys), positions_ref[r] >= threshold))
        top = jnp.full((stacked, 1), MASKED_SCORE, jnp.float32)
        for _, scores, mask in pieces:
            top = jnp.maximum(
                top, jnp.max(jnp.where(mask, scores, MASKED_SCORE), axis=1, keepdims=True)
            )
        total = jnp.zeros_like(top)
        weighted = jnp.zeros((stacked, 2 * HEAD_SIZE), jnp.float32)
        for keys, scores, mask in pieces:
            raw = jnp.where(mask, jnp.exp(scores - top), 0.0)
            total = total + jnp.sum(raw, axis=1, keepdims=True)
            weighted = weighted + jnp.dot(
                raw.astype(jnp.bfloat16), keys, preferred_element_type=jnp.float32
            )
        safe_total = jnp.where(in_request, total, 1.0)
        return jnp.where(in_request, weighted / safe_total, out_acc)

    out_acc = lax.fori_loop(
        r_first, r_last + 1, one_request, jnp.zeros((stacked, 2 * HEAD_SIZE), jnp.float32)
    )
    result = out_acc[:, HEAD_SIZE:].astype(o_ref.dtype)
    for h in range(heads):
        o_ref[:, h * HEAD_SIZE : (h + 1) * HEAD_SIZE] = result[h * block_rows : (h + 1) * block_rows]


def attend(bounds, query_pad, key_parts, fresh_rows, window):
    heads, row_count, width = query_pad.shape
    block_rows = math.gcd(row_count, BLOCK_ROWS)
    part_specs = []
    part_args = []
    for keys, positions in key_parts:
        part_specs.append(pl.BlockSpec(keys.shape, lambda i, b: (0, 0, 0)))
        part_specs.append(pl.BlockSpec(positions.shape, lambda i, b: (0, 0, 0)))
        part_args.extend([keys, positions])
    return pl.pallas_call(
        functools.partial(attend_kernel, window),
        out_shape=jax.ShapeDtypeStruct((row_count, heads * HEAD_SIZE), jnp.bfloat16),
        grid_spec=pltpu.PrefetchScalarGridSpec(
            num_scalar_prefetch=1,
            grid=(row_count // block_rows,),
            in_specs=[pl.BlockSpec((heads, block_rows, width), lambda i, b: (0, i, 0))]
            + part_specs
            + [pl.BlockSpec((row_count, width), lambda i, b: (0, 0))],
            out_specs=pl.BlockSpec((block_rows, heads * HEAD_SIZE), lambda i, b: (i, 0)),
        ),
        compiler_params=pltpu.CompilerParams(
            dimension_semantics=("arbitrary",), vmem_limit_bytes=48 * 1024 * 1024
        ),
    )(bounds, query_pad, *part_args, fresh_rows)


def solution(mesh):
    cores = 2
    seq_size, tensor_size = mesh.devices.shape
    split_mesh = jax.sharding.Mesh(
        mesh.devices.reshape(seq_size, tensor_size // cores, cores), ("seq", "tz", "tc")
    )
    return jax.shard_map(
        layer,
        mesh=split_mesh,
        in_specs=(
            P("seq", None),
            P(),
            P(None, ("tz", "tc")),
            P(),
            P(),
            P("seq", None, None, None),
            P(),
            P(),
            P(),
        ),
        out_specs=P("seq", ("tz", "tc")),
        check_vma=False,
    )
```

```python
import functools
import math

import jax
import jax.numpy as jnp
from jax import lax
from jax.sharding import PartitionSpec as P
from jax.experimental import pallas as pl
from jax.experimental.pallas import tpu as pltpu

QUERY_HEADS = 32
KEY_VALUE_HEADS = 4
HEAD_SIZE = 64
WINDOW_LENGTH = 2048
DEVICE_REQUESTS = 5
PPG = 64
WP = 16


MASKED_SCORE = -1e30


def normalize(tokens, norm_gain):
    widened = tokens.astype(jnp.float32)
    factor = lax.rsqrt(jnp.mean(widened * widened, axis=-1, keepdims=True) + 1e-05)
    return (widened * factor * norm_gain).astype(jnp.bfloat16)


def layer(
    tokens,
    norm_gain,
    query_weight,
    key_value_matrix,
    out_weight,
    cache_pages,
    page_table,
    request_lengths,
    request_groups,
):
    seq_count = lax.axis_size("seq")
    seq_index = lax.axis_index("seq")
    core_index = lax.axis_index("tc")
    tensor_rank_index = lax.axis_index("tz") * lax.axis_size("tc") + core_index
    row_count = tokens.shape[0]
    resident_heads = query_weight.shape[1] // HEAD_SIZE
    key_value_head = tensor_rank_index * resident_heads // (QUERY_HEADS // KEY_VALUE_HEADS)
    pages_here = cache_pages.shape[0]
    normed = normalize(tokens, norm_gain)
    query_rows = jnp.dot(normed, query_weight, preferred_element_type=jnp.float32).astype(
        jnp.bfloat16
    )
    query_rows = query_rows.reshape(row_count, resident_heads, HEAD_SIZE)
    head_weight = lax.dynamic_index_in_dim(key_value_matrix, key_value_head, 1, keepdims=False)
    new_token_rows = jnp.dot(normed, head_weight, preferred_element_type=jnp.float32).astype(
        jnp.bfloat16
    )
    lengths = lax.dynamic_slice_in_dim(
        request_lengths, seq_index * DEVICE_REQUESTS, DEVICE_REQUESTS
    )
    my_groups = lax.dynamic_slice_in_dim(
        request_groups, seq_index * DEVICE_REQUESTS, DEVICE_REQUESTS
    )
    tail_ids = page_table[:, PPG - WP :]
    holder = tail_ids // pages_here
    local_slot = tail_ids % pages_here
    held_slot = jnp.sum(jnp.where(holder == seq_index, local_slot, 0), axis=1)
    all_groups = request_groups.reshape(seq_count, DEVICE_REQUESTS)
    page_part = cache_pages.shape[2] // lax.axis_size("tc")
    head_pages = lax.dynamic_slice(
        cache_pages,
        (0, key_value_head, core_index * page_part, 0),
        (cache_pages.shape[0], 1, page_part, cache_pages.shape[3]),
    )[:, 0]
    outgoing = head_pages[held_slot[all_groups]]
    incoming = lax.all_to_all(outgoing, "seq", 0, 0, tiled=True)
    core_count = lax.axis_size("tc")
    incoming = incoming.transpose(1, 0, 2, 3)
    partner = lax.ppermute(incoming, "tc", [(0, 1), (1, 0)])
    source_ids = lax.iota(jnp.int32, seq_count)
    page_order = jnp.sum(
        jnp.where(
            holder[:, :, None] == source_ids[None, None, :],
            lax.iota(jnp.int32, holder.shape[1])[None, :, None],
            0,
        ),
        axis=1,
    )
    page_start = page_order[my_groups][:, :, None] * (page_part * core_count)
    within = lax.iota(jnp.int32, page_part)[None, None, :]
    key_parts = []
    for part, half in ((incoming, core_index), (partner, (core_index + 1) % core_count)):
        positions = (page_start + half * page_part + within).reshape(DEVICE_REQUESTS, 1, -1)
        keys = part.reshape(DEVICE_REQUESTS, -1, 2 * HEAD_SIZE)
        key_parts.append((keys, positions))
    starts = jnp.cumsum(lengths) - lengths
    bounds = jnp.concatenate([starts, starts + lengths]).astype(jnp.int32)
    fresh_pad = new_token_rows
    query_pad = jnp.concatenate(
        [query_rows, jnp.zeros_like(query_rows)], axis=-1
    ).transpose(1, 0, 2)
    attended = attend(bounds, query_pad, key_parts, fresh_pad, WINDOW_LENGTH)
    swap = [(0, 1), (1, 0)]
    z_count = lax.axis_size("tz")
    z_index = lax.axis_index("tz")
    partner_heads = lax.ppermute(attended, "tc", swap)
    first_core = core_index == 0
    chip_heads = jnp.where(
        first_core,
        jnp.concatenate([attended, partner_heads], axis=1),
        jnp.concatenate([partner_heads, attended], axis=1),
    )
    half_rows = row_count // core_count
    my_half = lax.dynamic_slice_in_dim(chip_heads, core_index * half_rows, half_rows, 0)
    sent = jnp.broadcast_to(my_half[None], (z_count,) + my_half.shape)
    chips_heads = lax.all_to_all(sent, "tz", 0, 0, tiled=True)
    chip_width = out_weight.shape[1] // z_count
    chip_columns = lax.dynamic_slice_in_dim(out_weight, z_index * chip_width, chip_width, 1)
    chip_columns = chip_columns.reshape(z_count, my_half.shape[1], chip_width)
    half_out = jnp.einsum(
        "zrj,zjn->rn", chips_heads, chip_columns, preferred_element_type=jnp.float32
    ).astype(jnp.bfloat16)
    columns = chip_width // core_count
    keep = lax.dynamic_slice_in_dim(half_out, core_index * columns, columns, 1)
    give = lax.dynamic_slice_in_dim(half_out, (1 - core_index) * columns, columns, 1)
    got = lax.ppermute(give, "tc", swap)
    projected = jnp.where(
        first_core, jnp.concatenate([keep, got], axis=0), jnp.concatenate([got, keep], axis=0)
    )
    return projected


BLOCK_ROWS = 64


def attend_kernel(window, bounds_ref, q_ref, *refs):
    part_refs = list(zip(refs[0:-2:2], refs[1:-2:2]))
    fresh_ref, o_ref = refs[-2], refs[-1]
    heads, block_rows, _ = q_ref.shape
    stacked = heads * block_rows
    request_count = part_refs[0][0].shape[0]
    row_count = fresh_ref.shape[0]
    first_row = pl.program_id(0) * block_rows
    score_scale = HEAD_SIZE ** (-0.5)
    q = q_ref[...].reshape(stacked, 2 * HEAD_SIZE)
    rows = first_row + lax.broadcasted_iota(jnp.int32, (heads, block_rows, 1), 1).reshape(stacked, 1)
    r_first = jnp.int32(0)
    r_last = jnp.int32(-1)
    for k in range(request_count):
        r_first = r_first + (bounds_ref[request_count + k] <= first_row).astype(jnp.int32)
        r_last = r_last + (bounds_ref[k] < first_row + block_rows).astype(jnp.int32)
    r_last = jnp.minimum(r_last, request_count - 1)
    column = lax.broadcasted_iota(jnp.int32, (stacked, row_count), 1)
    fresh = fresh_ref[...]

    def scores_of(keys):
        return lax.dot_general(
            q, keys, (((1,), (1,)), ((), ())), preferred_element_type=jnp.float32
        ) * score_scale

    def one_request(r, out_acc):
        begin = bounds_ref[r]
        finish = bounds_ref[request_count + r]
        in_request = (rows >= begin) & (rows < finish)
        threshold = jnp.where(in_request, rows - begin + 1, window)
        newest = jnp.where(in_request, rows, -1)
        suffix_mask = (
            (column >= begin) & (column <= newest) & (rows - column < WINDOW_LENGTH)
        )
        pieces = [(fresh, scores_of(fresh), suffix_mask)]
        for keys_ref, positions_ref in part_refs:
            keys = keys_ref[r]
            pieces.append((keys, scores_of(keys), positions_ref[r] >= threshold))
        top = jnp.full((stacked, 1), MASKED_SCORE, jnp.float32)
        for _, scores, mask in pieces:
            top = jnp.maximum(
                top, jnp.max(jnp.where(mask, scores, MASKED_SCORE), axis=1, keepdims=True)
            )
        total = jnp.zeros_like(top)
        weighted = jnp.zeros((stacked, 2 * HEAD_SIZE), jnp.float32)
        for keys, scores, mask in pieces:
            raw = jnp.where(mask, jnp.exp(scores - top), 0.0)
            total = total + jnp.sum(raw, axis=1, keepdims=True)
            weighted = weighted + jnp.dot(
                raw.astype(jnp.bfloat16), keys, preferred_element_type=jnp.float32
            )
        safe_total = jnp.where(in_request, total, 1.0)
        return jnp.where(in_request, weighted / safe_total, out_acc)

    out_acc = lax.fori_loop(
        r_first, r_last + 1, one_request, jnp.zeros((stacked, 2 * HEAD_SIZE), jnp.float32)
    )
    result = out_acc[:, HEAD_SIZE:].astype(o_ref.dtype)
    for h in range(heads):
        o_ref[:, h * HEAD_SIZE : (h + 1) * HEAD_SIZE] = result[h * block_rows : (h + 1) * block_rows]


def attend(bounds, query_pad, key_parts, fresh_rows, window):
    heads, row_count, width = query_pad.shape
    block_rows = math.gcd(row_count, BLOCK_ROWS)
    part_specs = []
    part_args = []
    for keys, positions in key_parts:
        part_specs.append(pl.BlockSpec(keys.shape, lambda i, b: (0, 0, 0)))
        part_specs.append(pl.BlockSpec(positions.shape, lambda i, b: (0, 0, 0)))
        part_args.extend([keys, positions])
    return pl.pallas_call(
        functools.partial(attend_kernel, window),
        out_shape=jax.ShapeDtypeStruct((row_count, heads * HEAD_SIZE), jnp.bfloat16),
        grid_spec=pltpu.PrefetchScalarGridSpec(
            num_scalar_prefetch=1,
            grid=(row_count // block_rows,),
            in_specs=[pl.BlockSpec((heads, block_rows, width), lambda i, b: (0, i, 0))]
            + part_specs
            + [pl.BlockSpec((row_count, width), lambda i, b: (0, 0))],
            out_specs=pl.BlockSpec((block_rows, heads * HEAD_SIZE), lambda i, b: (i, 0)),
        ),
        compiler_params=pltpu.CompilerParams(
            dimension_semantics=("arbitrary",), vmem_limit_bytes=48 * 1024 * 1024
        ),
    )(bounds, query_pad, *part_args, fresh_rows)


def solution(mesh):
    cores = 2
    seq_size, tensor_size = mesh.devices.shape
    split_mesh = jax.sharding.Mesh(
        mesh.devices.reshape(seq_size, tensor_size // cores, cores), ("seq", "tz", "tc")
    )
    return jax.shard_map(
        layer,
        mesh=split_mesh,
        in_specs=(
            P("seq", None),
            P(),
            P(None, ("tz", "tc")),
            P(),
            P(),
            P("seq", None, None, None),
            P(),
            P(),
            P(),
        ),
        out_specs=P("seq", ("tz", "tc")),
        check_vma=False,
    )
```
